512 devices in a mesh: tm: 64 (over z, x, core), panel: 8 (over y).
Axes of the slice: x: 4, y: 8, z: 8, core: 2. Of those that a mesh axis runs over, the one named last changes fastest.
Arguments:
- observations: bfloat16 [4096, 32768], P('panel', 'tm'), may hold values from -6 to 6
- info_weight: bfloat16 [4096, 1024], P('panel'), may hold values from -0.09375 to 0.09375
- readout: bfloat16 [4096, 1024], P('panel'), may hold values from -0.1875 to 0.1875
- labels: int32 [32768], P('tm'), may hold values from 0 to 3
- rate: float32 [4, 512], P(None, 'panel'), as said below
- angle: float32 [4, 512], P(None, 'panel'), may hold values from -0.3 to 0.3
- gain: float32 [4, 512], P(None, 'panel'), may hold values from 0.5 to 2
Outputs:
- smoothed: float32 [1024, 32768], P('panel', 'tm')
- predicted: bfloat16 [4096, 32768], P('panel', 'tm')
The draws below stay inside these ranges and needn't reach their ends.
Inputs may be any that keep to these rules, and one draw needn't show every extreme that they name: `rate`: every entry is positive.
All inputs are finite; a program needn't handle non-finite values.
Results may differ from the reference program's by a relative error of at most 0.013.
Values may be sent and summed in bfloat16 or wider, within the bound.
No kernel may reach another device: no remote copies, remote signals or barrier semaphores. Data moves between devices by JAX's collectives and lax.ppermute only.
A program may use at most 128 MiB of HBM per device.

```python
import math
import jax
import jax.numpy as jnp
from jax import lax

REGION_LATENT = 128
CORTICAL_REGIONS = 8
UNITS = 4096
SWITCH_STATES = 4
INTERVAL_WIDTH = 512
LATENTS = 1024
PAIRS = 512
TEMPORAL_LENGTH = 32768


def draw_labels(key, part):
    leading_entry, trailing_segment, forced_key = jax.random.split(jax.random.fold_in(key, 11), 3)
    minimum_intensity = jax.random.randint(leading_entry, (TEMPORAL_LENGTH,), 0, SWITCH_STATES - 1)
    activation_jump = jax.random.randint(trailing_segment, (TEMPORAL_LENGTH,), 0, 32 * INTERVAL_WIDTH) == 0
    forced_bin = jax.random.randint(forced_key, (), 0, TEMPORAL_LENGTH)
    activation_jump = jnp.logical_or(activation_jump, jnp.arange(TEMPORAL_LENGTH) == forced_bin)
    return jnp.where(activation_jump, SWITCH_STATES - 1, minimum_intensity).astype(jnp.int32)


def draw_rate(key, part):
    generator_tokens = jax.random.split(jax.random.fold_in(key, 23), 4)
    neural_counts = REGION_LATENT * CORTICAL_REGIONS // 2
    fraction_value = 0.5
    deviation_scale = jnp.exp(jax.random.uniform(generator_tokens[1], (SWITCH_STATES - 1, neural_counts), jnp.float32, jnp.log(0.3), jnp.log(1.5)))
    sluggish_factor = jax.random.uniform(generator_tokens[0], (neural_counts,), jnp.float32) < fraction_value
    decay_constant = jax.random.uniform(generator_tokens[2], (SWITCH_STATES - 1, neural_counts), jnp.float32, 8.0, 24.0)
    noise_variate = jnp.where(sluggish_factor[None, :], deviation_scale / TEMPORAL_LENGTH, 1.0 / decay_constant)
    activation_jump = jax.random.uniform(generator_tokens[3], (1, neural_counts), jnp.float32, 0.22, 0.7)
    return jnp.concatenate([noise_variate, activation_jump], 0).astype(jnp.float32)


def shard_levels(stream_key, shape, cuts, least, largest):
    level, own = 1.0, jax.random.fold_in(stream_key, 6)
    for dim, shards_of in cuts:
        draws = jnp.exp(jax.random.uniform(jax.random.fold_in(own, dim), (shards_of,), jnp.float32, least / len(cuts), largest / len(cuts)))
        level = level * jnp.repeat(draws, shape[dim] // shards_of).reshape([-1 if axis == dim else 1 for axis in range(len(shape))])
    return level


def noise(stream_key, extent, deviation, bound, cuts=(), kind=jnp.bfloat16):
    result = jax.random.normal(stream_key, extent, jnp.float32) * deviation
    if len(cuts) > 0:
        result = shard_levels(stream_key, extent, cuts, -0.22, 0.18) * result
    return jnp.clip(result, min=-bound, max=bound).astype(kind)


def setup_inputs(seed: int = 0) -> dict:
    seeds = jax.random.split(jax.random.key(seed), 8)
    observations = noise(seeds[0], (UNITS, TEMPORAL_LENGTH), 1.0, 6.0, ((0, 8), (1, 64)))
    info_weight = noise(seeds[1], (UNITS, LATENTS), UNITS ** -0.5, 0.09375, ((0, 8),))
    readout = noise(seeds[2], (UNITS, LATENTS), LATENTS ** -0.5, 0.1875, ((0, 8),))
    labels = draw_labels(jax.random.fold_in(seeds[7], 71), 0)
    rate = draw_rate(jax.random.fold_in(seeds[7], 71), 0)
    angle = jnp.clip(jax.random.uniform(seeds[5], (SWITCH_STATES, PAIRS), jnp.float32, -0.3, 0.3) * shard_levels(seeds[5], (SWITCH_STATES, PAIRS), ((1, 8),), -0.4, 0.0), -0.3, 0.3)
    gain = jnp.clip(jnp.exp(math.log(2.0) - 1.3862944 * jax.random.uniform(seeds[6], (SWITCH_STATES, PAIRS), jnp.float32) ** shard_levels(seeds[6], (SWITCH_STATES, PAIRS), ((1, 8),), -0.2, 0.2)), 0.5, 2.0)
    return {"observations": observations, "info_weight": info_weight, "readout": readout, "labels": labels, "rate": rate, "angle": angle, "gain": gain}


def step_map(state, items):
    sre, sim = state
    are, aim, ure, uim = items
    nre = are * sre - aim * sim + ure
    nim = are * sim + aim * sre + uim
    return ((nre, nim), (nre, nim))

def reference(observations, info_weight, readout, labels, rate, angle, gain):
    half = REGION_LATENT // 2
    info = jnp.dot(info_weight.T, observations, preferred_element_type=jnp.float32)
    view = info.reshape(CORTICAL_REGIONS, 2, half, TEMPORAL_LENGTH)
    zre = view[:, 0].reshape(CORTICAL_REGIONS * half, TEMPORAL_LENGTH).T
    zim = view[:, 1].reshape(CORTICAL_REGIONS * half, TEMPORAL_LENGTH).T
    lam = rate[labels]
    ang = angle[labels]
    scale = gain[labels] * jnp.sqrt(-jnp.expm1(-2.0 * lam))
    mag = jnp.exp(-lam)
    are = mag * jnp.cos(ang)
    aim = mag * jnp.sin(ang)
    zero = jnp.zeros_like(zre[0])
    _, (mre, mim) = lax.scan(step_map, (zero, zero), (are, aim, scale * zre, scale * zim))
    following = jnp.concatenate([labels[1:], labels[:1] * 0])
    lam_next = rate[following]
    ang_next = angle[following]
    mag_next = jnp.exp(-lam_next)
    final = (jnp.arange(TEMPORAL_LENGTH) == TEMPORAL_LENGTH - 1)[:, None]
    gre = jnp.where(final, 0.0, mag_next * jnp.cos(ang_next))
    gim = jnp.where(final, 0.0, -(mag_next * jnp.sin(ang_next)))
    coef = jnp.where(final, 1.0, -jnp.expm1(-2.0 * lam_next))
    _, (sre, sim) = lax.scan(step_map, (zero, zero), (gre, gim, coef * mre, coef * mim), reverse=True)
    smoothed = jnp.stack([sre.T.reshape(CORTICAL_REGIONS, half, TEMPORAL_LENGTH), sim.T.reshape(CORTICAL_REGIONS, half, TEMPORAL_LENGTH)], 1).reshape(CORTICAL_REGIONS * REGION_LATENT, TEMPORAL_LENGTH)
    smoothed_half = smoothed.astype(jnp.bfloat16)
    predicted = jnp.dot(readout, smoothed_half, preferred_element_type=jnp.float32).astype(jnp.bfloat16)
    return (smoothed, predicted)
```

```python
import functools

import jax
import jax.numpy as jnp
from jax import lax
from jax.experimental import pallas as pl
from jax.experimental.pallas import tpu as pltpu
from jax.sharding import PartitionSpec as P

REGION_LATENT = 128


def from_behind(shard, axis, by):
    devices = lax.axis_size(axis)
    pairs = [(i, i + by) for i in range(devices) if 0 <= i + by < devices]
    return lax.ppermute(shard, axis, pairs)


def scan_kernel(ar_ref, ai_ref, ur_ref, ui_ref, mr_ref, mi_ref, qr_ref, qi_ref, *, reverse):
    bins, width = ar_ref.shape

    def step(i, carry):
        sr, si, qr, qi = carry
        t = bins - 1 - i if reverse else i
        a_r = ar_ref[pl.ds(t, 1), :]
        a_i = ai_ref[pl.ds(t, 1), :]
        nsr = a_r * sr - a_i * si + ur_ref[pl.ds(t, 1), :]
        nsi = a_r * si + a_i * sr + ui_ref[pl.ds(t, 1), :]
        nqr = a_r * qr - a_i * qi
        nqi = a_r * qi + a_i * qr
        mr_ref[pl.ds(t, 1), :] = nsr
        mi_ref[pl.ds(t, 1), :] = nsi
        qr_ref[pl.ds(t, 1), :] = nqr
        qi_ref[pl.ds(t, 1), :] = nqi
        return (nsr, nsi, nqr, nqi)

    zero = jnp.zeros((1, width), jnp.float32)
    one = jnp.ones((1, width), jnp.float32)
    lax.fori_loop(0, bins, step, (zero, zero, one, zero), unroll=8)


def local_scan(ar, ai, ur, ui, reverse):
    shape = jax.ShapeDtypeStruct(ar.shape, jnp.float32)
    vmem = pl.BlockSpec(memory_space=pltpu.VMEM)
    return pl.pallas_call(
        functools.partial(scan_kernel, reverse=reverse),
        out_shape=(shape,) * 4,
        in_specs=[vmem] * 4,
        out_specs=(vmem,) * 4,
    )(ar, ai, ur, ui)


def carry_in(mul, add, axis, backward):
    devices = lax.axis_size(axis)
    sign = -1 if backward else 1
    state = jnp.stack([mul[0], mul[1], add[0], add[1]])
    by = 1
    while by < devices:
        got = from_behind(state, axis, sign * by)
        mr, mi, lr, li = state[0], state[1], state[2], state[3]
        gr, gi, hr, hi = got[0], got[1], got[2], got[3]
        state = jnp.stack(
            [
                mr * gr - mi * gi,
                mr * gi + mi * gr,
                mr * hr - mi * hi + lr,
                mr * hi + mi * hr + li,
            ]
        )
        by *= 2
    got = from_behind(state[2:], axis, sign)
    return got[0], got[1]


def select(table, regime):
    result = jnp.zeros((regime.shape[0], table.shape[1]), jnp.float32)
    for which in range(table.shape[0]):
        result = jnp.where(regime[:, None] == which, table[which][None, :], result)
    return result


def body(observations, info_weight, readout, labels, rate, angle, gain):
    bins = observations.shape[1]
    lat_dev = info_weight.shape[1] // lax.axis_size("panel")
    half = REGION_LATENT // 2
    areas_dev = lat_dev // REGION_LATENT
    pair_dev = rate.shape[1]
    cols = lax.all_to_all(info_weight, "panel", split_axis=1, concat_axis=0, tiled=True)
    info = lax.dot_general(
        lax.all_gather(observations, "panel", axis=0, tiled=True),
        cols,
        (((0,), (0,)), ((), ())),
        preferred_element_type=jnp.float32,
    )
    view = info.reshape(bins, areas_dev, 2, half)
    zre = view[:, :, 0].reshape(bins, pair_dev)
    zim = view[:, :, 1].reshape(bins, pair_dev)
    lam = select(rate, labels)
    ang = select(angle, labels)
    scale = select(gain, labels) * jnp.sqrt(-jnp.expm1(-2.0 * lam))
    mag = jnp.exp(-lam)
    are = mag * jnp.cos(ang)
    aim = mag * jnp.sin(ang)
    loc_re, loc_im, prod_re, prod_im = local_scan(are, aim, scale * zre, scale * zim, False)
    in_re, in_im = carry_in(
        (prod_re[-1], prod_im[-1]), (loc_re[-1], loc_im[-1]), "tm", False
    )
    mre = loc_re + prod_re * in_re[None, :] - prod_im * in_im[None, :]
    mim = loc_im + prod_re * in_im[None, :] + prod_im * in_re[None, :]
    arriving = from_behind(labels[:1], "tm", -1)
    following = jnp.concatenate([labels[1:], arriving])
    lam_next = select(rate, following)
    ang_next = select(angle, following)
    mag_next = jnp.exp(-lam_next)
    is_last = lax.axis_index("tm") == lax.axis_size("tm") - 1
    final = jnp.logical_and(is_last, lax.iota(jnp.int32, bins) == bins - 1)[:, None]
    gre = jnp.where(final, 0.0, mag_next * jnp.cos(ang_next))
    gim = jnp.where(final, 0.0, -(mag_next * jnp.sin(ang_next)))
    coef = jnp.where(final, 1.0, -jnp.expm1(-2.0 * lam_next))
    back_re, back_im, sum_re, sum_im = local_scan(gre, gim, coef * mre, coef * mim, True)
    out_re, out_im = carry_in(
        (sum_re[0], sum_im[0]), (back_re[0], back_im[0]), "tm", True
    )
    sre = back_re + sum_re * out_re[None, :] - sum_im * out_im[None, :]
    sim = back_im + sum_re * out_im[None, :] + sum_im * out_re[None, :]
    smoothed = jnp.stack(
        [sre.reshape(bins, areas_dev, half), sim.reshape(bins, areas_dev, half)], 2
    ).reshape(bins, lat_dev).T
    smoothed_half = smoothed.astype(jnp.bfloat16)
    predicted = jnp.dot(
        readout,
        lax.all_gather(smoothed_half, "panel", axis=0, tiled=True),
        preferred_element_type=jnp.float32,
    )
    return (smoothed, predicted.astype(jnp.bfloat16))


def solution(mesh):
    return jax.shard_map(
        body,
        mesh=mesh,
        in_specs=(
            P("panel", "tm"),
            P("panel", None),
            P("panel", None),
            P("tm"),
            P(None, "panel"),
            P(None, "panel"),
            P(None, "panel"),
        ),
        out_specs=(P("panel", "tm"), P("panel", "tm")),
        check_vma=False,
    )
```

```python
import functools

import jax
import jax.numpy as jnp
from jax import lax
from jax.experimental import pallas as pl
from jax.experimental.pallas import tpu as pltpu
from jax.sharding import PartitionSpec as P

REGION_LATENT = 128


def from_behind(shard, axis, by):
    devices = lax.axis_size(axis)
    pairs = [(i, i + by) for i in range(devices) if 0 <= i + by < devices]
    return lax.ppermute(shard, axis, pairs)


def scan_kernel(ar_ref, ai_ref, ur_ref, ui_ref, mr_ref, mi_ref, qr_ref, qi_ref, *, reverse):
    bins, width = ar_ref.shape

    def step(i, carry):
        sr, si, qr, qi = carry
        t = bins - 1 - i if reverse else i
        a_r = ar_ref[pl.ds(t, 1), :]
        a_i = ai_ref[pl.ds(t, 1), :]
        nsr = a_r * sr - a_i * si + ur_ref[pl.ds(t, 1), :]
        nsi = a_r * si + a_i * sr + ui_ref[pl.ds(t, 1), :]
        nqr = a_r * qr - a_i * qi
        nqi = a_r * qi + a_i * qr
        mr_ref[pl.ds(t, 1), :] = nsr
        mi_ref[pl.ds(t, 1), :] = nsi
        qr_ref[pl.ds(t, 1), :] = nqr
        qi_ref[pl.ds(t, 1), :] = nqi
        return (nsr, nsi, nqr, nqi)

    zero = jnp.zeros((1, width), jnp.float32)
    one = jnp.ones((1, width), jnp.float32)
    lax.fori_loop(0, bins, step, (zero, zero, one, zero), unroll=8)


def local_scan(ar, ai, ur, ui, reverse):
    shape = jax.ShapeDtypeStruct(ar.shape, jnp.float32)
    vmem = pl.BlockSpec(memory_space=pltpu.VMEM)
    return pl.pallas_call(
        functools.partial(scan_kernel, reverse=reverse),
        out_shape=(shape,) * 4,
        in_specs=[vmem] * 4,
        out_specs=(vmem,) * 4,
    )(ar, ai, ur, ui)


def carry_in(mul, add, axis, backward):
    devices = lax.axis_size(axis)
    sign = -1 if backward else 1
    state = jnp.stack([mul[0], mul[1], add[0], add[1]])
    by = 1
    while by < devices:
        got = from_behind(state, axis, sign * by)
        mr, mi, lr, li = state[0], state[1], state[2], state[3]
        gr, gi, hr, hi = got[0], got[1], got[2], got[3]
        state = jnp.stack(
            [
                mr * gr - mi * gi,
                mr * gi + mi * gr,
                mr * hr - mi * hi + lr,
                mr * hi + mi * hr + li,
            ]
        )
        by *= 2
    got = from_behind(state[2:], axis, sign)
    return got[0], got[1]


def select(table, regime):
    result = jnp.zeros((regime.shape[0], table.shape[1]), jnp.float32)
    for which in range(table.shape[0]):
        result = jnp.where(regime[:, None] == which, table[which][None, :], result)
    return result


def body(observations, info_weight, readout, labels, rate, angle, gain):
    bins = observations.shape[1]
    lat_dev = info_weight.shape[1] // lax.axis_size("panel")
    half = REGION_LATENT // 2
    areas_dev = lat_dev // REGION_LATENT
    pair_dev = rate.shape[1]
    partial = lax.dot_general(
        info_weight,
        observations,
        (((0,), (0,)), ((), ())),
        preferred_element_type=jnp.float32,
    )
    info = lax.psum_scatter(partial, "panel", scatter_dimension=0, tiled=True).T
    view = info.reshape(bins, areas_dev, 2, half)
    zre = view[:, :, 0].reshape(bins, pair_dev)
    zim = view[:, :, 1].reshape(bins, pair_dev)
    lam = select(rate, labels)
    ang = select(angle, labels)
    scale = select(gain, labels) * jnp.sqrt(-jnp.expm1(-2.0 * lam))
    mag = jnp.exp(-lam)
    are = mag * jnp.cos(ang)
    aim = mag * jnp.sin(ang)
    loc_re, loc_im, prod_re, prod_im = local_scan(are, aim, scale * zre, scale * zim, False)
    in_re, in_im = carry_in(
        (prod_re[-1], prod_im[-1]), (loc_re[-1], loc_im[-1]), "tm", False
    )
    mre = loc_re + prod_re * in_re[None, :] - prod_im * in_im[None, :]
    mim = loc_im + prod_re * in_im[None, :] + prod_im * in_re[None, :]
    arriving = from_behind(labels[:1], "tm", -1)
    following = jnp.concatenate([labels[1:], arriving])
    lam_next = select(rate, following)
    ang_next = select(angle, following)
    mag_next = jnp.exp(-lam_next)
    is_last = lax.axis_index("tm") == lax.axis_size("tm") - 1
    final = jnp.logical_and(is_last, lax.iota(jnp.int32, bins) == bins - 1)[:, None]
    gre = jnp.where(final, 0.0, mag_next * jnp.cos(ang_next))
    gim = jnp.where(final, 0.0, -(mag_next * jnp.sin(ang_next)))
    coef = jnp.where(final, 1.0, -jnp.expm1(-2.0 * lam_next))
    back_re, back_im, sum_re, sum_im = local_scan(gre, gim, coef * mre, coef * mim, True)
    out_re, out_im = carry_in(
        (sum_re[0], sum_im[0]), (back_re[0], back_im[0]), "tm", True
    )
    sre = back_re + sum_re * out_re[None, :] - sum_im * out_im[None, :]
    sim = back_im + sum_re * out_im[None, :] + sum_im * out_re[None, :]
    smoothed = jnp.stack(
        [sre.reshape(bins, areas_dev, half), sim.reshape(bins, areas_dev, half)], 2
    ).reshape(bins, lat_dev).T
    smoothed_half = smoothed.astype(jnp.bfloat16)
    predicted = jnp.dot(
        readout,
        lax.all_gather(smoothed_half, "panel", axis=0, tiled=True),
        preferred_element_type=jnp.float32,
    )
    return (smoothed, predicted.astype(jnp.bfloat16))


def solution(mesh):
    return jax.shard_map(
        body,
        mesh=mesh,
        in_specs=(
            P("panel", "tm"),
            P("panel", None),
            P("panel", None),
            P("tm"),
            P(None, "panel"),
            P(None, "panel"),
            P(None, "panel"),
        ),
        out_specs=(P("panel", "tm"), P("panel", "tm")),
        check_vma=False,
    )
```

```python
import functools

import jax
import jax.numpy as jnp
from jax import lax
from jax.experimental import pallas as pl
from jax.experimental.pallas import tpu as pltpu
from jax.sharding import PartitionSpec as P

REGION_LATENT = 128


def from_behind(shard, axis, by):
    devices = lax.axis_size(axis)
    pairs = [(i, i + by) for i in range(devices) if 0 <= i + by < devices]
    return lax.ppermute(shard, axis, pairs)


def scan_kernel(ar_ref, ai_ref, ur_ref, ui_ref, mr_ref, mi_ref, qr_ref, qi_ref, *, reverse):
    bins, width = ar_ref.shape

    def step(i, carry):
        sr, si, qr, qi = carry
        t = bins - 1 - i if reverse else i
        a_r = ar_ref[pl.ds(t, 1), :]
        a_i = ai_ref[pl.ds(t, 1), :]
        nsr = a_r * sr - a_i * si + ur_ref[pl.ds(t, 1), :]
        nsi = a_r * si + a_i * sr + ui_ref[pl.ds(t, 1), :]
        nqr = a_r * qr - a_i * qi
        nqi = a_r * qi + a_i * qr
        mr_ref[pl.ds(t, 1), :] = nsr
        mi_ref[pl.ds(t, 1), :] = nsi
        qr_ref[pl.ds(t, 1), :] = nqr
        qi_ref[pl.ds(t, 1), :] = nqi
        return (nsr, nsi, nqr, nqi)

    zero = jnp.zeros((1, width), jnp.float32)
    one = jnp.ones((1, width), jnp.float32)
    lax.fori_loop(0, bins, step, (zero, zero, one, zero), unroll=8)


def local_scan(ar, ai, ur, ui, reverse):
    shape = jax.ShapeDtypeStruct(ar.shape, jnp.float32)
    vmem = pl.BlockSpec(memory_space=pltpu.VMEM)
    return pl.pallas_call(
        functools.partial(scan_kernel, reverse=reverse),
        out_shape=(shape,) * 4,
        in_specs=[vmem] * 4,
        out_specs=(vmem,) * 4,
    )(ar, ai, ur, ui)


def carry_in(mul, add, axis, backward):
    devices = lax.axis_size(axis)
    sign = -1 if backward else 1
    state = jnp.stack([mul[0], mul[1], add[0], add[1]])
    by = 1
    while by < devices:
        got = from_behind(state, axis, sign * by)
        mr, mi, lr, li = state[0], state[1], state[2], state[3]
        gr, gi, hr, hi = got[0], got[1], got[2], got[3]
        state = jnp.stack(
            [
                mr * gr - mi * gi,
                mr * gi + mi * gr,
                mr * hr - mi * hi + lr,
                mr * hi + mi * hr + li,
            ]
        )
        by *= 2
    got = from_behind(state[2:], axis, sign)
    return got[0], got[1]


def select(table, regime):
    result = jnp.zeros((regime.shape[0], table.shape[1]), jnp.float32)
    for which in range(table.shape[0]):
        result = jnp.where(regime[:, None] == which, table[which][None, :], result)
    return result


def body(observations, info_weight, readout, labels, rate, angle, gain):
    bins = observations.shape[1]
    lat_dev = info_weight.shape[1] // lax.axis_size("panel")
    half = REGION_LATENT // 2
    areas_dev = lat_dev // REGION_LATENT
    pair_dev = rate.shape[1]
    partial = lax.dot_general(
        info_weight,
        observations,
        (((0,), (0,)), ((), ())),
        preferred_element_type=jnp.float32,
    )
    panels = lax.axis_size("panel")
    pieces = lax.all_to_all(
        partial.reshape(panels, lat_dev, bins), "panel", 0, 0, tiled=True
    )
    info = jnp.sum(pieces, axis=0).T
    view = info.reshape(bins, areas_dev, 2, half)
    zre = view[:, :, 0].reshape(bins, pair_dev)
    zim = view[:, :, 1].reshape(bins, pair_dev)
    lam = select(rate, labels)
    ang = select(angle, labels)
    scale = select(gain, labels) * jnp.sqrt(-jnp.expm1(-2.0 * lam))
    mag = jnp.exp(-lam)
    are = mag * jnp.cos(ang)
    aim = mag * jnp.sin(ang)
    loc_re, loc_im, prod_re, prod_im = local_scan(are, aim, scale * zre, scale * zim, False)
    in_re, in_im = carry_in(
        (prod_re[-1], prod_im[-1]), (loc_re[-1], loc_im[-1]), "tm", False
    )
    mre = loc_re + prod_re * in_re[None, :] - prod_im * in_im[None, :]
    mim = loc_im + prod_re * in_im[None, :] + prod_im * in_re[None, :]
    arriving = from_behind(labels[:1], "tm", -1)
    following = jnp.concatenate([labels[1:], arriving])
    lam_next = select(rate, following)
    ang_next = select(angle, following)
    mag_next = jnp.exp(-lam_next)
    is_last = lax.axis_index("tm") == lax.axis_size("tm") - 1
    final = jnp.logical_and(is_last, lax.iota(jnp.int32, bins) == bins - 1)[:, None]
    gre = jnp.where(final, 0.0, mag_next * jnp.cos(ang_next))
    gim = jnp.where(final, 0.0, -(mag_next * jnp.sin(ang_next)))
    coef = jnp.where(final, 1.0, -jnp.expm1(-2.0 * lam_next))
    back_re, back_im, sum_re, sum_im = local_scan(gre, gim, coef * mre, coef * mim, True)
    out_re, out_im = carry_in(
        (sum_re[0], sum_im[0]), (back_re[0], back_im[0]), "tm", True
    )
    sre = back_re + sum_re * out_re[None, :] - sum_im * out_im[None, :]
    sim = back_im + sum_re * out_im[None, :] + sum_im * out_re[None, :]
    smoothed = jnp.stack(
        [sre.reshape(bins, areas_dev, half), sim.reshape(bins, areas_dev, half)], 2
    ).reshape(bins, lat_dev).T
    smoothed_half = smoothed.astype(jnp.bfloat16)
    copies = jnp.broadcast_to(smoothed_half[None], (panels, lat_dev, bins))
    gathered = lax.all_to_all(copies, "panel", 0, 0, tiled=True)
    predicted = jnp.dot(
        readout,
        gathered.reshape(panels * lat_dev, bins),
        preferred_element_type=jnp.float32,
    )
    return (smoothed, predicted.astype(jnp.bfloat16))


def solution(mesh):
    return jax.shard_map(
        body,
        mesh=mesh,
        in_specs=(
            P("panel", "tm"),
            P("panel", None),
            P("panel", None),
            P("tm"),
            P(None, "panel"),
            P(None, "panel"),
            P(None, "panel"),
        ),
        out_specs=(P("panel", "tm"), P("panel", "tm")),
        check_vma=False,
    )
```

```python
import functools

import jax
import jax.numpy as jnp
from jax import lax
from jax.experimental import pallas as pl
from jax.experimental.pallas import tpu as pltpu
from jax.sharding import Mesh, PartitionSpec as P

REGION_LATENT = 128


def from_behind(shard, axis, by):
    devices = lax.axis_size(axis)
    pairs = [(i, i + by) for i in range(devices) if 0 <= i + by < devices]
    return lax.ppermute(shard, axis, pairs)


def scan_kernel(ar_ref, ai_ref, ur_ref, ui_ref, mr_ref, mi_ref, qr_ref, qi_ref, *, reverse):
    bins, width = ar_ref.shape

    def step(i, carry):
        sr, si, qr, qi = carry
        t = bins - 1 - i if reverse else i
        a_r = ar_ref[pl.ds(t, 1), :]
        a_i = ai_ref[pl.ds(t, 1), :]
        nsr = a_r * sr - a_i * si + ur_ref[pl.ds(t, 1), :]
        nsi = a_r * si + a_i * sr + ui_ref[pl.ds(t, 1), :]
        nqr = a_r * qr - a_i * qi
        nqi = a_r * qi + a_i * qr
        mr_ref[pl.ds(t, 1), :] = nsr
        mi_ref[pl.ds(t, 1), :] = nsi
        qr_ref[pl.ds(t, 1), :] = nqr
        qi_ref[pl.ds(t, 1), :] = nqi
        return (nsr, nsi, nqr, nqi)

    zero = jnp.zeros((1, width), jnp.float32)
    one = jnp.ones((1, width), jnp.float32)
    lax.fori_loop(0, bins, step, (zero, zero, one, zero), unroll=8)


def local_scan(ar, ai, ur, ui, reverse):
    shape = jax.ShapeDtypeStruct(ar.shape, jnp.float32)
    vmem = pl.BlockSpec(memory_space=pltpu.VMEM)
    return pl.pallas_call(
        functools.partial(scan_kernel, reverse=reverse),
        out_shape=(shape,) * 4,
        in_specs=[vmem] * 4,
        out_specs=(vmem,) * 4,
    )(ar, ai, ur, ui)


def gather_all(part, axes):
    for axis in axes[::-1]:
        count = lax.axis_size(axis)
        copies = jnp.broadcast_to(part[None], (count,) + part.shape)
        part = lax.all_to_all(copies, axis, 0, 0, tiled=True)
    return part.reshape((-1,) + part.shape[len(axes):])


def join(earlier, later):
    ere, eim, ebr, ebi = earlier[0], earlier[1], earlier[2], earlier[3]
    lre, lim, lbr, lbi = later[0], later[1], later[2], later[3]
    return jnp.stack(
        [
            lre * ere - lim * eim,
            lre * eim + lim * ere,
            lre * ebr - lim * ebi + lbr,
            lre * ebi + lim * ebr + lbi,
        ]
    )


def carry_in(mul, add, axes, backward):
    state = jnp.stack([mul[0], mul[1], add[0], add[1]])
    pieces = gather_all(state, axes)
    count, mine = (pieces.shape[0], lax.axis_index(axes))
    if backward:
        pieces = pieces[::-1]
        mine = count - 1 - mine
    neutral = jnp.zeros_like(state).at[0].set(1.0)

    def step(position, so_far):
        longer = join(so_far, pieces[position])
        return jnp.where(position < mine, longer, so_far)

    so_far = lax.fori_loop(0, count - 1, step, neutral)
    return so_far[2], so_far[3]


def select(table, regime):
    result = jnp.zeros((regime.shape[0], table.shape[1]), jnp.float32)
    for which in range(table.shape[0]):
        result = jnp.where(regime[:, None] == which, table[which][None, :], result)
    return result


def body(observations, info_weight, readout, labels, rate, angle, gain, time_axes):
    bins = observations.shape[1]
    lat_dev = info_weight.shape[1] // lax.axis_size("panel")
    half = REGION_LATENT // 2
    areas_dev = lat_dev // REGION_LATENT
    pair_dev = rate.shape[1]
    partial = lax.dot_general(
        info_weight,
        observations,
        (((0,), (0,)), ((), ())),
        preferred_element_type=jnp.float32,
    )
    panels = lax.axis_size("panel")
    pieces = lax.all_to_all(
        partial.astype(jnp.bfloat16).reshape(panels, lat_dev, bins), "panel", 0, 0, tiled=True
    )
    info = jnp.sum(pieces.astype(jnp.float32), axis=0).T
    view = info.reshape(bins, areas_dev, 2, half)
    zre = view[:, :, 0].reshape(bins, pair_dev)
    zim = view[:, :, 1].reshape(bins, pair_dev)
    lam = select(rate, labels)
    ang = select(angle, labels)
    scale = select(gain, labels) * jnp.sqrt(-jnp.expm1(-2.0 * lam))
    mag = jnp.exp(-lam)
    are = mag * jnp.cos(ang)
    aim = mag * jnp.sin(ang)
    loc_re, loc_im, prod_re, prod_im = local_scan(are, aim, scale * zre, scale * zim, False)
    in_re, in_im = carry_in(
        (prod_re[-1], prod_im[-1]), (loc_re[-1], loc_im[-1]), time_axes, False
    )
    mre = loc_re + prod_re * in_re[None, :] - prod_im * in_im[None, :]
    mim = loc_im + prod_re * in_im[None, :] + prod_im * in_re[None, :]
    arriving = from_behind(labels[:1], time_axes, -1)
    following = jnp.concatenate([labels[1:], arriving])
    lam_next = select(rate, following)
    ang_next = select(angle, following)
    mag_next = jnp.exp(-lam_next)
    is_last = lax.axis_index(time_axes) == lax.axis_size(time_axes) - 1
    final = jnp.logical_and(is_last, lax.iota(jnp.int32, bins) == bins - 1)[:, None]
    gre = jnp.where(final, 0.0, mag_next * jnp.cos(ang_next))
    gim = jnp.where(final, 0.0, -(mag_next * jnp.sin(ang_next)))
    coef = jnp.where(final, 1.0, -jnp.expm1(-2.0 * lam_next))
    back_re, back_im, sum_re, sum_im = local_scan(gre, gim, coef * mre, coef * mim, True)
    out_re, out_im = carry_in(
        (sum_re[0], sum_im[0]), (back_re[0], back_im[0]), time_axes, True
    )
    sre = back_re + sum_re * out_re[None, :] - sum_im * out_im[None, :]
    sim = back_im + sum_re * out_im[None, :] + sum_im * out_re[None, :]
    smoothed = jnp.stack(
        [sre.reshape(bins, areas_dev, half), sim.reshape(bins, areas_dev, half)], 2
    ).reshape(bins, lat_dev).T
    smoothed_half = smoothed.astype(jnp.bfloat16)
    copies = jnp.broadcast_to(smoothed_half[None], (panels, lat_dev, bins))
    gathered = lax.all_to_all(copies, "panel", 0, 0, tiled=True)
    predicted = jnp.dot(
        readout,
        gathered.reshape(panels * lat_dev, bins),
        preferred_element_type=jnp.float32,
    )
    return (smoothed, predicted.astype(jnp.bfloat16))


def solution(mesh):
    steps = mesh.shape["tm"]
    inner = 8
    while steps % inner:
        inner //= 2
    split = Mesh(
        mesh.devices.reshape(steps // inner, inner, mesh.shape["panel"]),
        ("tg", "tl", "panel"),
    )
    tm = ("tg", "tl")
    return jax.shard_map(
        functools.partial(body, time_axes=tm),
        mesh=split,
        in_specs=(
            P("panel", tm),
            P("panel", None),
            P("panel", None),
            P(tm),
            P(None, "panel"),
            P(None, "panel"),
            P(None, "panel"),
        ),
        out_specs=(P("panel", tm), P("panel", tm)),
        check_vma=False,
    )
```

```python
import functools

import jax
import jax.numpy as jnp
from jax import lax
from jax.experimental import pallas as pl
from jax.experimental.pallas import tpu as pltpu
from jax.sharding import Mesh, PartitionSpec as P

REGION_LATENT = 128


def from_behind(shard, axis, by):
    devices = lax.axis_size(axis)
    pairs = [(i, i + by) for i in range(devices) if 0 <= i + by < devices]
    return lax.ppermute(shard, axis, pairs)


def scan_kernel(*refs, reverse, count):
    ar_ref, ai_ref = refs[0], refs[1]
    inputs = refs[2 : 2 + 2 * count]
    outputs = refs[2 + 2 * count :]
    bins, width = ar_ref.shape

    def step(i, carry):
        t = bins - 1 - i if reverse else i
        row = pl.ds(t, 1)
        a_r = ar_ref[row, :]
        a_i = ai_ref[row, :]
        new = []
        for k in range(count + 1):
            sr, si = carry[2 * k], carry[2 * k + 1]
            nsr = a_r * sr - a_i * si
            nsi = a_r * si + a_i * sr
            if k < count:
                nsr = nsr + inputs[2 * k][row, :]
                nsi = nsi + inputs[2 * k + 1][row, :]
            outputs[2 * k][row, :] = nsr
            outputs[2 * k + 1][row, :] = nsi
            new += [nsr, nsi]
        return tuple(new)

    zero = jnp.zeros((1, width), jnp.float32)
    one = jnp.ones((1, width), jnp.float32)
    lax.fori_loop(0, bins, step, (zero, zero) * count + (one, zero), unroll=8)


def local_scan(ar, ai, drives, reverse):
    flat = [part for pair in drives for part in pair]
    shape = jax.ShapeDtypeStruct(ar.shape, jnp.float32)
    vmem = pl.BlockSpec(memory_space=pltpu.VMEM)
    outs = 2 * len(drives) + 2
    return pl.pallas_call(
        functools.partial(scan_kernel, reverse=reverse, count=len(drives)),
        out_shape=(shape,) * outs,
        in_specs=[vmem] * (2 + len(flat)),
        out_specs=(vmem,) * outs,
    )(ar, ai, *flat)


def gather_all(part, axes):
    for axis in axes[::-1]:
        count = lax.axis_size(axis)
        copies = jnp.broadcast_to(part[None], (count,) + part.shape)
        part = lax.all_to_all(copies, axis, 0, 0, tiled=True)
    return part.reshape((-1,) + part.shape[len(axes):])


def join(earlier, later):
    ere, eim, ebr, ebi = earlier[0], earlier[1], earlier[2], earlier[3]
    lre, lim, lbr, lbi = later[0], later[1], later[2], later[3]
    return jnp.stack(
        [
            lre * ere - lim * eim,
            lre * eim + lim * ere,
            lre * ebr - lim * ebi + lbr,
            lre * ebi + lim * ebr + lbi,
        ]
    )


def carries(summary, axes):
    pieces = gather_all(summary, axes)
    count, mine = (pieces.shape[0], lax.axis_index(axes))
    zero = jnp.zeros_like(summary[0])

    def forward(state, piece):
        mr, mi = state
        ar, ai, lr, li = piece[0], piece[1], piece[2], piece[3]
        return (ar * mr - ai * mi + lr, ar * mi + ai * mr + li), state

    _, (fre, fim) = lax.scan(forward, (zero, zero), pieces)
    gr, gi = pieces[:, 4], pieces[:, 5]
    rr = pieces[:, 6] + pieces[:, 8] * fre - pieces[:, 9] * fim
    ri = pieces[:, 7] + pieces[:, 8] * fim + pieces[:, 9] * fre

    def backward(i, state):
        position = count - 1 - i
        sr, si = state
        nsr = gr[position] * sr - gi[position] * si + rr[position]
        nsi = gr[position] * si + gi[position] * sr + ri[position]
        keep = position > mine
        return (jnp.where(keep, nsr, sr), jnp.where(keep, nsi, si))

    sre, sim = lax.fori_loop(0, count - 1, backward, (zero, zero))
    return (fre[mine], fim[mine]), (sre, sim)


def select(table, regime):
    result = jnp.zeros((regime.shape[0], table.shape[1]), jnp.float32)
    for which in range(table.shape[0]):
        result = jnp.where(regime[:, None] == which, table[which][None, :], result)
    return result


def body(observations, info_weight, readout, labels, rate, angle, gain, time_axes):
    bins = observations.shape[1]
    lat_dev = info_weight.shape[1] // lax.axis_size("panel")
    half = REGION_LATENT // 2
    areas_dev = lat_dev // REGION_LATENT
    pair_dev = rate.shape[1]
    partial = lax.dot_general(
        info_weight,
        observations,
        (((0,), (0,)), ((), ())),
        preferred_element_type=jnp.float32,
    )
    panels = lax.axis_size("panel")
    pieces = lax.all_to_all(
        partial.astype(jnp.bfloat16).reshape(panels, lat_dev, bins), "panel", 0, 0, tiled=True
    )
    info = jnp.sum(pieces.astype(jnp.float32), axis=0).T
    view = info.reshape(bins, areas_dev, 2, half)
    zre = view[:, :, 0].reshape(bins, pair_dev)
    zim = view[:, :, 1].reshape(bins, pair_dev)
    lam = select(rate, labels)
    ang = select(angle, labels)
    scale = select(gain, labels) * jnp.sqrt(-jnp.expm1(-2.0 * lam))
    mag = jnp.exp(-lam)
    are = mag * jnp.cos(ang)
    aim = mag * jnp.sin(ang)
    loc_re, loc_im, prod_re, prod_im = local_scan(
        are, aim, [(scale * zre, scale * zim)], False
    )
    arriving = from_behind(labels[:1], time_axes, -1)
    following = jnp.concatenate([labels[1:], arriving])
    lam_next = select(rate, following)
    ang_next = select(angle, following)
    mag_next = jnp.exp(-lam_next)
    is_last = lax.axis_index(time_axes) == lax.axis_size(time_axes) - 1
    final = jnp.logical_and(is_last, lax.iota(jnp.int32, bins) == bins - 1)[:, None]
    gre = jnp.where(final, 0.0, mag_next * jnp.cos(ang_next))
    gim = jnp.where(final, 0.0, -(mag_next * jnp.sin(ang_next)))
    coef = jnp.where(final, 1.0, -jnp.expm1(-2.0 * lam_next))
    back_re, back_im, kre, kim, sum_re, sum_im = local_scan(
        gre, gim, [(coef * loc_re, coef * loc_im), (coef * prod_re, coef * prod_im)], True
    )
    summary = jnp.stack(
        [
            prod_re[-1], prod_im[-1], loc_re[-1], loc_im[-1],
            sum_re[0], sum_im[0], back_re[0], back_im[0], kre[0], kim[0],
        ]
    )
    (in_re, in_im), (out_re, out_im) = carries(summary, time_axes)
    sre = (
        back_re
        + kre * in_re[None, :] - kim * in_im[None, :]
        + sum_re * out_re[None, :] - sum_im * out_im[None, :]
    )
    sim = (
        back_im
        + kre * in_im[None, :] + kim * in_re[None, :]
        + sum_re * out_im[None, :] + sum_im * out_re[None, :]
    )
    smoothed = jnp.stack(
        [sre.reshape(bins, areas_dev, half), sim.reshape(bins, areas_dev, half)], 2
    ).reshape(bins, lat_dev).T
    smoothed_half = smoothed.astype(jnp.bfloat16)
    copies = jnp.broadcast_to(smoothed_half[None], (panels, lat_dev, bins))
    gathered = lax.all_to_all(copies, "panel", 0, 0, tiled=True)
    predicted = jnp.dot(
        readout,
        gathered.reshape(panels * lat_dev, bins),
        preferred_element_type=jnp.float32,
    )
    return (smoothed, predicted.astype(jnp.bfloat16))


def solution(mesh):
    steps = mesh.shape["tm"]
    inner = 8
    while steps % inner:
        inner //= 2
    split = Mesh(
        mesh.devices.reshape(steps // inner, inner, mesh.shape["panel"]),
        ("tg", "tl", "panel"),
    )
    tm = ("tg", "tl")
    return jax.shard_map(
        functools.partial(body, time_axes=tm),
        mesh=split,
        in_specs=(
            P("panel", tm),
            P("panel", None),
            P("panel", None),
            P(tm),
            P(None, "panel"),
            P(None, "panel"),
            P(None, "panel"),
        ),
        out_specs=(P("panel", tm), P("panel", tm)),
        check_vma=False,
    )
```

```python
import functools

import jax
import jax.numpy as jnp
from jax import lax
from jax.experimental import pallas as pl
from jax.experimental.pallas import tpu as pltpu
from jax.sharding import Mesh, PartitionSpec as P

REGION_LATENT = 128


def from_behind(shard, axis, by):
    devices = lax.axis_size(axis)
    pairs = [(i, i + by) for i in range(devices) if 0 <= i + by < devices]
    return lax.ppermute(shard, axis, pairs)


def scan_kernel(*refs, reverse, count):
    ar_ref, ai_ref = refs[0], refs[1]
    inputs = refs[2 : 2 + 2 * count]
    outputs = refs[2 + 2 * count :]
    bins, width = ar_ref.shape

    def step(i, carry):
        t = bins - 1 - i if reverse else i
        row = pl.ds(t, 1)
        a_r = ar_ref[row, :]
        a_i = ai_ref[row, :]
        new = []
        for k in range(count + 1):
            sr, si = carry[2 * k], carry[2 * k + 1]
            nsr = a_r * sr - a_i * si
            nsi = a_r * si + a_i * sr
            if k < count:
                nsr = nsr + inputs[2 * k][row, :]
                nsi = nsi + inputs[2 * k + 1][row, :]
            outputs[2 * k][row, :] = nsr
            outputs[2 * k + 1][row, :] = nsi
            new += [nsr, nsi]
        return tuple(new)

    zero = jnp.zeros((1, width), jnp.float32)
    one = jnp.ones((1, width), jnp.float32)
    lax.fori_loop(0, bins, step, (zero, zero) * count + (one, zero), unroll=8)


def local_scan(ar, ai, drives, reverse):
    flat = [part for pair in drives for part in pair]
    shape = jax.ShapeDtypeStruct(ar.shape, jnp.float32)
    vmem = pl.BlockSpec(memory_space=pltpu.VMEM)
    outs = 2 * len(drives) + 2
    return pl.pallas_call(
        functools.partial(scan_kernel, reverse=reverse, count=len(drives)),
        out_shape=(shape,) * outs,
        in_specs=[vmem] * (2 + len(flat)),
        out_specs=(vmem,) * outs,
    )(ar, ai, *flat)


def gather_all(part, axes):
    count = lax.axis_size(axes)
    copies = jnp.broadcast_to(part[None], (count,) + part.shape)
    return lax.all_to_all(copies, axes, 0, 0, tiled=True)


def join(earlier, later):
    ere, eim, ebr, ebi = earlier[0], earlier[1], earlier[2], earlier[3]
    lre, lim, lbr, lbi = later[0], later[1], later[2], later[3]
    return jnp.stack(
        [
            lre * ere - lim * eim,
            lre * eim + lim * ere,
            lre * ebr - lim * ebi + lbr,
            lre * ebi + lim * ebr + lbi,
        ]
    )


def carries(summary, axes):
    pieces = gather_all(summary, axes)
    count, mine = (pieces.shape[0], lax.axis_index(axes))
    zero = jnp.zeros_like(summary[0])

    def forward(state, piece):
        mr, mi = state
        ar, ai, lr, li = piece[0], piece[1], piece[2], piece[3]
        return (ar * mr - ai * mi + lr, ar * mi + ai * mr + li), state

    _, (fre, fim) = lax.scan(forward, (zero, zero), pieces, unroll=8)
    gr, gi = pieces[:, 4], pieces[:, 5]
    rr = pieces[:, 6] + pieces[:, 8] * fre - pieces[:, 9] * fim
    ri = pieces[:, 7] + pieces[:, 8] * fim + pieces[:, 9] * fre

    def backward(i, state):
        position = count - 1 - i
        sr, si = state
        nsr = gr[position] * sr - gi[position] * si + rr[position]
        nsi = gr[position] * si + gi[position] * sr + ri[position]
        keep = position > mine
        return (jnp.where(keep, nsr, sr), jnp.where(keep, nsi, si))

    sre, sim = lax.fori_loop(0, count - 1, backward, (zero, zero), unroll=9)
    return (fre[mine], fim[mine]), (sre, sim)


def select(table, regime):
    result = jnp.zeros((regime.shape[0], table.shape[1]), jnp.float32)
    for which in range(table.shape[0]):
        result = jnp.where(regime[:, None] == which, table[which][None, :], result)
    return result


def body(observations, info_weight, readout, labels, rate, angle, gain, time_axes):
    bins = observations.shape[1]
    lat_dev = info_weight.shape[1] // lax.axis_size("panel")
    half = REGION_LATENT // 2
    areas_dev = lat_dev // REGION_LATENT
    pair_dev = rate.shape[1]
    partial = lax.dot_general(
        info_weight,
        observations,
        (((0,), (0,)), ((), ())),
        preferred_element_type=jnp.float32,
    )
    panels = lax.axis_size("panel")
    pieces = lax.all_to_all(
        partial.astype(jnp.bfloat16).reshape(panels, lat_dev, bins), "panel", 0, 0, tiled=True
    )
    info = jnp.sum(pieces.astype(jnp.float32), axis=0).T
    view = info.reshape(bins, areas_dev, 2, half)
    zre = view[:, :, 0].reshape(bins, pair_dev)
    zim = view[:, :, 1].reshape(bins, pair_dev)
    lam = select(rate, labels)
    ang = select(angle, labels)
    scale = select(gain, labels) * jnp.sqrt(-jnp.expm1(-2.0 * lam))
    mag = jnp.exp(-lam)
    are = mag * jnp.cos(ang)
    aim = mag * jnp.sin(ang)
    loc_re, loc_im, prod_re, prod_im = local_scan(
        are, aim, [(scale * zre, scale * zim)], False
    )
    arriving = from_behind(labels[:1], time_axes, -1)
    following = jnp.concatenate([labels[1:], arriving])
    lam_next = select(rate, following)
    ang_next = select(angle, following)
    mag_next = jnp.exp(-lam_next)
    is_last = lax.axis_index(time_axes) == lax.axis_size(time_axes) - 1
    final = jnp.logical_and(is_last, lax.iota(jnp.int32, bins) == bins - 1)[:, None]
    gre = jnp.where(final, 0.0, mag_next * jnp.cos(ang_next))
    gim = jnp.where(final, 0.0, -(mag_next * jnp.sin(ang_next)))
    coef = jnp.where(final, 1.0, -jnp.expm1(-2.0 * lam_next))
    back_re, back_im, kre, kim, sum_re, sum_im = local_scan(
        gre, gim, [(coef * loc_re, coef * loc_im), (coef * prod_re, coef * prod_im)], True
    )
    summary = jnp.stack(
        [
            prod_re[-1], prod_im[-1], loc_re[-1], loc_im[-1],
            sum_re[0], sum_im[0], back_re[0], back_im[0], kre[0], kim[0],
        ]
    )
    (in_re, in_im), (out_re, out_im) = carries(summary, time_axes)
    sre = (
        back_re
        + kre * in_re[None, :] - kim * in_im[None, :]
        + sum_re * out_re[None, :] - sum_im * out_im[None, :]
    )
    sim = (
        back_im
        + kre * in_im[None, :] + kim * in_re[None, :]
        + sum_re * out_im[None, :] + sum_im * out_re[None, :]
    )
    smoothed = jnp.stack(
        [sre.reshape(bins, areas_dev, half), sim.reshape(bins, areas_dev, half)], 2
    ).reshape(bins, lat_dev).T
    smoothed_half = smoothed.astype(jnp.bfloat16)
    copies = jnp.broadcast_to(smoothed_half[None], (panels, lat_dev, bins))
    gathered = lax.all_to_all(copies, "panel", 0, 0, tiled=True)
    predicted = jnp.dot(
        readout,
        gathered.reshape(panels * lat_dev, bins),
        preferred_element_type=jnp.float32,
    )
    return (smoothed, predicted.astype(jnp.bfloat16))


def solution(mesh):
    steps = mesh.shape["tm"]
    inner = 8
    while steps % inner:
        inner //= 2
    split = Mesh(
        mesh.devices.reshape(steps // inner, inner, mesh.shape["panel"]),
        ("tg", "tl", "panel"),
    )
    tm = ("tg", "tl")
    return jax.shard_map(
        functools.partial(body, time_axes=tm),
        mesh=split,
        in_specs=(
            P("panel", tm),
            P("panel", None),
            P("panel", None),
            P(tm),
            P(None, "panel"),
            P(None, "panel"),
            P(None, "panel"),
        ),
        out_specs=(P("panel", tm), P("panel", tm)),
        check_vma=False,
    )
```

```python
import functools

import jax
import jax.numpy as jnp
from jax import lax
from jax.experimental import pallas as pl
from jax.experimental.pallas import tpu as pltpu
from jax.sharding import Mesh, PartitionSpec as P

REGION_LATENT = 128


def from_behind(shard, axis, by):
    devices = lax.axis_size(axis)
    pairs = [(i, i + by) for i in range(devices) if 0 <= i + by < devices]
    return lax.ppermute(shard, axis, pairs)


def smoother_kernel(
    ar_ref, ai_ref, sc_ref, zr_ref, zi_ref, gr_ref, gi_ref, cf_ref,
    br_ref, bi_ref, kr_ref, ki_ref, qr_ref, qi_ref, last_ref,
    lr_ref, li_ref, pr_ref, pi_ref,
):
    bins, width = ar_ref.shape

    def forward(t, carry):
        lr, li, pr, pi = carry
        row = pl.ds(t, 1)
        a_r = ar_ref[row, :]
        a_i = ai_ref[row, :]
        scale = sc_ref[row, :]
        nlr = a_r * lr - a_i * li + scale * zr_ref[row, :]
        nli = a_r * li + a_i * lr + scale * zi_ref[row, :]
        npr = a_r * pr - a_i * pi
        npi = a_r * pi + a_i * pr
        lr_ref[row, :] = nlr
        li_ref[row, :] = nli
        pr_ref[row, :] = npr
        pi_ref[row, :] = npi
        return (nlr, nli, npr, npi)

    def backward(i, carry):
        t = bins - 1 - i
        br, bi, kr, ki, qr, qi = carry
        row = pl.ds(t, 1)
        g_r = gr_ref[row, :]
        g_i = gi_ref[row, :]
        coef = cf_ref[row, :]
        nbr = g_r * br - g_i * bi + coef * lr_ref[row, :]
        nbi = g_r * bi + g_i * br + coef * li_ref[row, :]
        nkr = g_r * kr - g_i * ki + coef * pr_ref[row, :]
        nki = g_r * ki + g_i * kr + coef * pi_ref[row, :]
        nqr = g_r * qr - g_i * qi
        nqi = g_r * qi + g_i * qr
        br_ref[row, :] = nbr
        bi_ref[row, :] = nbi
        kr_ref[row, :] = nkr
        ki_ref[row, :] = nki
        qr_ref[row, :] = nqr
        qi_ref[row, :] = nqi
        return (nbr, nbi, nkr, nki, nqr, nqi)

    zero = jnp.zeros((1, width), jnp.float32)
    one = jnp.ones((1, width), jnp.float32)
    lr, li, pr, pi = lax.fori_loop(0, bins, forward, (zero, zero, one, zero), unroll=8)
    last_ref[...] = jnp.zeros(last_ref.shape, jnp.float32)
    last_ref[pl.ds(0, 1), :] = pr
    last_ref[pl.ds(1, 1), :] = pi
    last_ref[pl.ds(2, 1), :] = lr
    last_ref[pl.ds(3, 1), :] = li
    lax.fori_loop(0, bins, backward, (zero, zero, zero, zero, one, zero), unroll=8)


def smoother(*operands):
    bins, width = operands[0].shape
    shape = jax.ShapeDtypeStruct((bins, width), jnp.float32)
    vmem = pl.BlockSpec(memory_space=pltpu.VMEM)
    return pl.pallas_call(
        smoother_kernel,
        out_shape=(shape,) * 6 + (jax.ShapeDtypeStruct((8, width), jnp.float32),),
        in_specs=[vmem] * len(operands),
        out_specs=(vmem,) * 7,
        scratch_shapes=[pltpu.VMEM((bins, width), jnp.float32)] * 4,
    )(*operands)


def gather_all(part, axes):
    count = lax.axis_size(axes)
    copies = jnp.broadcast_to(part[None], (count,) + part.shape)
    return lax.all_to_all(copies, axes, 0, 0, tiled=True)


def join(earlier, later):
    ere, eim, ebr, ebi = earlier[0], earlier[1], earlier[2], earlier[3]
    lre, lim, lbr, lbi = later[0], later[1], later[2], later[3]
    return jnp.stack(
        [
            lre * ere - lim * eim,
            lre * eim + lim * ere,
            lre * ebr - lim * ebi + lbr,
            lre * ebi + lim * ebr + lbi,
        ]
    )


def carries(summary, axes):
    pieces = gather_all(summary, axes)
    count, mine = (pieces.shape[0], lax.axis_index(axes))
    zero = jnp.zeros_like(summary[0])

    def forward(state, piece):
        mr, mi = state
        ar, ai, lr, li = piece[0], piece[1], piece[2], piece[3]
        return (ar * mr - ai * mi + lr, ar * mi + ai * mr + li), state

    _, (fre, fim) = lax.scan(forward, (zero, zero), pieces, unroll=8)
    gr, gi = pieces[:, 4], pieces[:, 5]
    rr = pieces[:, 6] + pieces[:, 8] * fre - pieces[:, 9] * fim
    ri = pieces[:, 7] + pieces[:, 8] * fim + pieces[:, 9] * fre

    def backward(i, state):
        position = count - 1 - i
        sr, si = state
        nsr = gr[position] * sr - gi[position] * si + rr[position]
        nsi = gr[position] * si + gi[position] * sr + ri[position]
        keep = position > mine
        return (jnp.where(keep, nsr, sr), jnp.where(keep, nsi, si))

    sre, sim = lax.fori_loop(0, count - 1, backward, (zero, zero), unroll=9)
    return (fre[mine], fim[mine]), (sre, sim)


def select(table, regime):
    result = jnp.zeros((regime.shape[0], table.shape[1]), jnp.float32)
    for which in range(table.shape[0]):
        result = jnp.where(regime[:, None] == which, table[which][None, :], result)
    return result


def body(observations, info_weight, readout, labels, rate, angle, gain, time_axes):
    bins = observations.shape[1]
    lat_dev = info_weight.shape[1] // lax.axis_size("panel")
    half = REGION_LATENT // 2
    areas_dev = lat_dev // REGION_LATENT
    pair_dev = rate.shape[1]
    partial = lax.dot_general(
        info_weight,
        observations,
        (((0,), (0,)), ((), ())),
        preferred_element_type=jnp.float32,
    )
    panels = lax.axis_size("panel")
    pieces = lax.all_to_all(
        partial.astype(jnp.bfloat16).reshape(panels, lat_dev, bins), "panel", 0, 0, tiled=True
    )
    info = jnp.sum(pieces.astype(jnp.float32), axis=0).T
    view = info.reshape(bins, areas_dev, 2, half)
    zre = view[:, :, 0].reshape(bins, pair_dev)
    zim = view[:, :, 1].reshape(bins, pair_dev)
    lam = select(rate, labels)
    ang = select(angle, labels)
    scale = select(gain, labels) * jnp.sqrt(-jnp.expm1(-2.0 * lam))
    mag = jnp.exp(-lam)
    are = mag * jnp.cos(ang)
    aim = mag * jnp.sin(ang)
    arriving = from_behind(labels[:1], time_axes, -1)
    following = jnp.concatenate([labels[1:], arriving])
    lam_next = select(rate, following)
    ang_next = select(angle, following)
    mag_next = jnp.exp(-lam_next)
    is_last = lax.axis_index(time_axes) == lax.axis_size(time_axes) - 1
    final = jnp.logical_and(is_last, lax.iota(jnp.int32, bins) == bins - 1)[:, None]
    gre = jnp.where(final, 0.0, mag_next * jnp.cos(ang_next))
    gim = jnp.where(final, 0.0, -(mag_next * jnp.sin(ang_next)))
    coef = jnp.where(final, 1.0, -jnp.expm1(-2.0 * lam_next))
    back_re, back_im, kre, kim, sum_re, sum_im, last = smoother(
        are, aim, scale, zre, zim, gre, gim, coef
    )
    summary = jnp.concatenate(
        [last[:4], jnp.stack([sum_re[0], sum_im[0], back_re[0], back_im[0], kre[0], kim[0]])]
    )
    (in_re, in_im), (out_re, out_im) = carries(summary, time_axes)
    sre = (
        back_re
        + kre * in_re[None, :] - kim * in_im[None, :]
        + sum_re * out_re[None, :] - sum_im * out_im[None, :]
    )
    sim = (
        back_im
        + kre * in_im[None, :] + kim * in_re[None, :]
        + sum_re * out_im[None, :] + sum_im * out_re[None, :]
    )
    smoothed = jnp.stack(
        [sre.reshape(bins, areas_dev, half), sim.reshape(bins, areas_dev, half)], 2
    ).reshape(bins, lat_dev).T
    smoothed_half = smoothed.astype(jnp.bfloat16)
    copies = jnp.broadcast_to(smoothed_half[None], (panels, lat_dev, bins))
    gathered = lax.all_to_all(copies, "panel", 0, 0, tiled=True)
    predicted = jnp.dot(
        readout,
        gathered.reshape(panels * lat_dev, bins),
        preferred_element_type=jnp.float32,
    )
    return (smoothed, predicted.astype(jnp.bfloat16))


def solution(mesh):
    steps = mesh.shape["tm"]
    inner = 8
    while steps % inner:
        inner //= 2
    split = Mesh(
        mesh.devices.reshape(steps // inner, inner, mesh.shape["panel"]),
        ("tg", "tl", "panel"),
    )
    tm = ("tg", "tl")
    return jax.shard_map(
        functools.partial(body, time_axes=tm),
        mesh=split,
        in_specs=(
            P("panel", tm),
            P("panel", None),
            P("panel", None),
            P(tm),
            P(None, "panel"),
            P(None, "panel"),
            P(None, "panel"),
        ),
        out_specs=(P("panel", tm), P("panel", tm)),
        check_vma=False,
    )
```

```python
import functools

import jax
import jax.numpy as jnp
from jax import lax
from jax.experimental import pallas as pl
from jax.experimental.pallas import tpu as pltpu
from jax.sharding import Mesh, PartitionSpec as P

REGION_LATENT = 128


def from_behind(shard, axis, by):
    devices = lax.axis_size(axis)
    pairs = [(i, i + by) for i in range(devices) if 0 <= i + by < devices]
    return lax.ppermute(shard, axis, pairs)


def smoother_kernel(
    ar_ref, ai_ref, sc_ref, zr_ref, zi_ref, gr_ref, gi_ref, cf_ref,
    br_ref, bi_ref, kr_ref, ki_ref, qr_ref, qi_ref, last_ref,
    lr_ref, li_ref, pr_ref, pi_ref,
):
    bins, width = ar_ref.shape

    def forward(t, carry):
        lr, li, pr, pi = carry
        row = pl.ds(t, 1)
        a_r = ar_ref[row, :]
        a_i = ai_ref[row, :]
        scale = sc_ref[row, :]
        nlr = a_r * lr - a_i * li + scale * zr_ref[row, :]
        nli = a_r * li + a_i * lr + scale * zi_ref[row, :]
        npr = a_r * pr - a_i * pi
        npi = a_r * pi + a_i * pr
        lr_ref[row, :] = nlr
        li_ref[row, :] = nli
        pr_ref[row, :] = npr
        pi_ref[row, :] = npi
        return (nlr, nli, npr, npi)

    def backward(i, carry):
        t = bins - 1 - i
        br, bi, kr, ki, qr, qi = carry
        row = pl.ds(t, 1)
        g_r = gr_ref[row, :]
        g_i = gi_ref[row, :]
        coef = cf_ref[row, :]
        nbr = g_r * br - g_i * bi + coef * lr_ref[row, :]
        nbi = g_r * bi + g_i * br + coef * li_ref[row, :]
        nkr = g_r * kr - g_i * ki + coef * pr_ref[row, :]
        nki = g_r * ki + g_i * kr + coef * pi_ref[row, :]
        nqr = g_r * qr - g_i * qi
        nqi = g_r * qi + g_i * qr
        br_ref[row, :] = nbr
        bi_ref[row, :] = nbi
        kr_ref[row, :] = nkr
        ki_ref[row, :] = nki
        qr_ref[row, :] = nqr
        qi_ref[row, :] = nqi
        return (nbr, nbi, nkr, nki, nqr, nqi)

    zero = jnp.zeros((1, width), jnp.float32)
    one = jnp.ones((1, width), jnp.float32)
    lr, li, pr, pi = lax.fori_loop(0, bins, forward, (zero, zero, one, zero), unroll=8)
    last_ref[...] = jnp.zeros(last_ref.shape, jnp.float32)
    last_ref[pl.ds(0, 1), :] = pr
    last_ref[pl.ds(1, 1), :] = pi
    last_ref[pl.ds(2, 1), :] = lr
    last_ref[pl.ds(3, 1), :] = li
    lax.fori_loop(0, bins, backward, (zero, zero, zero, zero, one, zero), unroll=8)


def smoother(*operands):
    bins, width = operands[0].shape
    shape = jax.ShapeDtypeStruct((bins, width), jnp.float32)
    vmem = pl.BlockSpec(memory_space=pltpu.VMEM)
    return pl.pallas_call(
        smoother_kernel,
        out_shape=(shape,) * 6 + (jax.ShapeDtypeStruct((8, width), jnp.float32),),
        in_specs=[vmem] * len(operands),
        out_specs=(vmem,) * 7,
        scratch_shapes=[pltpu.VMEM((bins, width), jnp.float32)] * 4,
    )(*operands)


def gather_all(part, axes):
    count = lax.axis_size(axes)
    copies = jnp.broadcast_to(part[None], (count,) + part.shape)
    return lax.all_to_all(copies, axes, 0, 0, tiled=True)


def join(earlier, later):
    ere, eim, ebr, ebi = earlier[0], earlier[1], earlier[2], earlier[3]
    lre, lim, lbr, lbi = later[0], later[1], later[2], later[3]
    return jnp.stack(
        [
            lre * ere - lim * eim,
            lre * eim + lim * ere,
            lre * ebr - lim * ebi + lbr,
            lre * ebi + lim * ebr + lbi,
        ]
    )


def carries(summary, axes):
    pieces = gather_all(summary, axes)
    count, mine = (pieces.shape[0], lax.axis_index(axes))
    zero = jnp.zeros_like(summary[0])

    def forward(state, piece):
        mr, mi = state
        ar, ai, lr, li = piece[0], piece[1], piece[2], piece[3]
        return (ar * mr - ai * mi + lr, ar * mi + ai * mr + li), state

    _, (fre, fim) = lax.scan(forward, (zero, zero), pieces, unroll=8)
    gr, gi = pieces[:, 4], pieces[:, 5]
    rr = pieces[:, 6] + pieces[:, 8] * fre - pieces[:, 9] * fim
    ri = pieces[:, 7] + pieces[:, 8] * fim + pieces[:, 9] * fre

    def backward(i, state):
        position = count - 1 - i
        sr, si = state
        nsr = gr[position] * sr - gi[position] * si + rr[position]
        nsi = gr[position] * si + gi[position] * sr + ri[position]
        keep = position > mine
        return (jnp.where(keep, nsr, sr), jnp.where(keep, nsi, si))

    sre, sim = lax.fori_loop(0, count - 1, backward, (zero, zero), unroll=9)
    return (fre[mine], fim[mine]), (sre, sim)


def ring_gather(part, axis):
    count, mine = (lax.axis_size(axis), lax.axis_index(axis))
    up = [(i, (i + 1) % count) for i in range(count)]
    down = [(i, (i - 1) % count) for i in range(count)]
    ahead = [part] * (count // 2 + 1)
    behind = [part] * ((count - 1) // 2 + 1)
    for hop in range(1, count // 2 + 1):
        ahead[hop] = lax.ppermute(ahead[hop - 1], axis, up)
        if hop < len(behind):
            behind[hop] = lax.ppermute(behind[hop - 1], axis, down)
    relative = [part] + behind[1:] + ahead[1:][::-1]
    stacked = jnp.stack(relative)
    doubled = jnp.concatenate([stacked, stacked])
    return lax.dynamic_slice_in_dim(doubled, count - mine, count, 0)


def select(table, regime):
    result = jnp.zeros((regime.shape[0], table.shape[1]), jnp.float32)
    for which in range(table.shape[0]):
        result = jnp.where(regime[:, None] == which, table[which][None, :], result)
    return result


def body(observations, info_weight, readout, labels, rate, angle, gain, time_axes):
    bins = observations.shape[1]
    lat_dev = info_weight.shape[1] // lax.axis_size("panel")
    half = REGION_LATENT // 2
    areas_dev = lat_dev // REGION_LATENT
    pair_dev = rate.shape[1]
    partial = lax.dot_general(
        info_weight,
        observations,
        (((0,), (0,)), ((), ())),
        preferred_element_type=jnp.float32,
    )
    panels = lax.axis_size("panel")
    pieces = lax.all_to_all(
        partial.astype(jnp.bfloat16).reshape(panels, lat_dev, bins), "panel", 0, 0, tiled=True
    )
    info = jnp.sum(pieces.astype(jnp.float32), axis=0).T
    view = info.reshape(bins, areas_dev, 2, half)
    zre = view[:, :, 0].reshape(bins, pair_dev)
    zim = view[:, :, 1].reshape(bins, pair_dev)
    lam = select(rate, labels)
    ang = select(angle, labels)
    scale = select(gain, labels) * jnp.sqrt(-jnp.expm1(-2.0 * lam))
    mag = jnp.exp(-lam)
    are = mag * jnp.cos(ang)
    aim = mag * jnp.sin(ang)
    arriving = from_behind(labels[:1], time_axes, -1)
    following = jnp.concatenate([labels[1:], arriving])
    lam_next = select(rate, following)
    ang_next = select(angle, following)
    mag_next = jnp.exp(-lam_next)
    is_last = lax.axis_index(time_axes) == lax.axis_size(time_axes) - 1
    final = jnp.logical_and(is_last, lax.iota(jnp.int32, bins) == bins - 1)[:, None]
    gre = jnp.where(final, 0.0, mag_next * jnp.cos(ang_next))
    gim = jnp.where(final, 0.0, -(mag_next * jnp.sin(ang_next)))
    coef = jnp.where(final, 1.0, -jnp.expm1(-2.0 * lam_next))
    back_re, back_im, kre, kim, sum_re, sum_im, last = smoother(
        are, aim, scale, zre, zim, gre, gim, coef
    )
    summary = jnp.concatenate(
        [last[:4], jnp.stack([sum_re[0], sum_im[0], back_re[0], back_im[0], kre[0], kim[0]])]
    )
    (in_re, in_im), (out_re, out_im) = carries(summary, time_axes)
    sre = (
        back_re
        + kre * in_re[None, :] - kim * in_im[None, :]
        + sum_re * out_re[None, :] - sum_im * out_im[None, :]
    )
    sim = (
        back_im
        + kre * in_im[None, :] + kim * in_re[None, :]
        + sum_re * out_im[None, :] + sum_im * out_re[None, :]
    )
    smoothed = jnp.stack(
        [sre.reshape(bins, areas_dev, half), sim.reshape(bins, areas_dev, half)], 2
    ).reshape(bins, lat_dev).T
    smoothed_half = smoothed.astype(jnp.bfloat16)
    gathered = ring_gather(smoothed_half, "panel")
    predicted = jnp.dot(
        readout,
        gathered.reshape(panels * lat_dev, bins),
        preferred_element_type=jnp.float32,
    )
    return (smoothed, predicted.astype(jnp.bfloat16))


def solution(mesh):
    steps = mesh.shape["tm"]
    inner = 8
    while steps % inner:
        inner //= 2
    split = Mesh(
        mesh.devices.reshape(steps // inner, inner, mesh.shape["panel"]),
        ("tg", "tl", "panel"),
    )
    tm = ("tg", "tl")
    return jax.shard_map(
        functools.partial(body, time_axes=tm),
        mesh=split,
        in_specs=(
            P("panel", tm),
            P("panel", None),
            P("panel", None),
            P(tm),
            P(None, "panel"),
            P(None, "panel"),
            P(None, "panel"),
        ),
        out_specs=(P("panel", tm), P("panel", tm)),
        check_vma=False,
    )
```

```python
import functools

import jax
import jax.numpy as jnp
from jax import lax
from jax.experimental import pallas as pl
from jax.experimental.pallas import tpu as pltpu
from jax.sharding import Mesh, PartitionSpec as P

REGION_LATENT = 128


def from_behind(shard, axis, by):
    devices = lax.axis_size(axis)
    pairs = [(i, i + by) for i in range(devices) if 0 <= i + by < devices]
    return lax.ppermute(shard, axis, pairs)


def smoother_kernel(
    ar_ref, ai_ref, sc_ref, zr_ref, zi_ref, gr_ref, gi_ref, cf_ref,
    br_ref, bi_ref, kr_ref, ki_ref, qr_ref, qi_ref, last_ref,
    lr_ref, li_ref, pr_ref, pi_ref,
):
    bins, width = ar_ref.shape

    def forward(t, carry):
        lr, li, pr, pi = carry
        row = pl.ds(t, 1)
        a_r = ar_ref[row, :]
        a_i = ai_ref[row, :]
        scale = sc_ref[row, :]
        nlr = a_r * lr - a_i * li + scale * zr_ref[row, :]
        nli = a_r * li + a_i * lr + scale * zi_ref[row, :]
        npr = a_r * pr - a_i * pi
        npi = a_r * pi + a_i * pr
        lr_ref[row, :] = nlr
        li_ref[row, :] = nli
        pr_ref[row, :] = npr
        pi_ref[row, :] = npi
        return (nlr, nli, npr, npi)

    def backward(i, carry):
        t = bins - 1 - i
        br, bi, kr, ki, qr, qi = carry
        row = pl.ds(t, 1)
        g_r = gr_ref[row, :]
        g_i = gi_ref[row, :]
        coef = cf_ref[row, :]
        nbr = g_r * br - g_i * bi + coef * lr_ref[row, :]
        nbi = g_r * bi + g_i * br + coef * li_ref[row, :]
        nkr = g_r * kr - g_i * ki + coef * pr_ref[row, :]
        nki = g_r * ki + g_i * kr + coef * pi_ref[row, :]
        nqr = g_r * qr - g_i * qi
        nqi = g_r * qi + g_i * qr
        br_ref[row, :] = nbr
        bi_ref[row, :] = nbi
        kr_ref[row, :] = nkr
        ki_ref[row, :] = nki
        qr_ref[row, :] = nqr
        qi_ref[row, :] = nqi
        return (nbr, nbi, nkr, nki, nqr, nqi)

    zero = jnp.zeros((1, width), jnp.float32)
    one = jnp.ones((1, width), jnp.float32)
    lr, li, pr, pi = lax.fori_loop(0, bins, forward, (zero, zero, one, zero), unroll=8)
    last_ref[...] = jnp.zeros(last_ref.shape, jnp.float32)
    last_ref[pl.ds(0, 1), :] = pr
    last_ref[pl.ds(1, 1), :] = pi
    last_ref[pl.ds(2, 1), :] = lr
    last_ref[pl.ds(3, 1), :] = li
    ends = lax.fori_loop(0, bins, backward, (zero, zero, zero, zero, one, zero), unroll=8)
    br, bi, kr, ki, qr, qi = ends
    for index, value in enumerate((qr, qi, br, bi, kr, ki)):
        last_ref[pl.ds(4 + index, 1), :] = value


def smoother(*operands):
    bins, width = operands[0].shape
    shape = jax.ShapeDtypeStruct((bins, width), jnp.float32)
    vmem = pl.BlockSpec(memory_space=pltpu.VMEM)
    return pl.pallas_call(
        smoother_kernel,
        out_shape=(shape,) * 6 + (jax.ShapeDtypeStruct((16, width), jnp.float32),),
        in_specs=[vmem] * len(operands),
        out_specs=(vmem,) * 7,
        scratch_shapes=[pltpu.VMEM((bins, width), jnp.float32)] * 4,
    )(*operands)


def gather_all(part, axes):
    count = lax.axis_size(axes)
    copies = jnp.broadcast_to(part[None], (count,) + part.shape)
    return lax.all_to_all(copies, axes, 0, 0, tiled=True)


def join(earlier, later):
    ere, eim, ebr, ebi = earlier[0], earlier[1], earlier[2], earlier[3]
    lre, lim, lbr, lbi = later[0], later[1], later[2], later[3]
    return jnp.stack(
        [
            lre * ere - lim * eim,
            lre * eim + lim * ere,
            lre * ebr - lim * ebi + lbr,
            lre * ebi + lim * ebr + lbi,
        ]
    )


def carries(summary, axes):
    pieces = gather_all(summary, axes)
    count, mine = (pieces.shape[0], lax.axis_index(axes))
    zero = jnp.zeros_like(summary[0])

    def forward(state, piece):
        mr, mi = state
        ar, ai, lr, li = piece[0], piece[1], piece[2], piece[3]
        return (ar * mr - ai * mi + lr, ar * mi + ai * mr + li), state

    _, (fre, fim) = lax.scan(forward, (zero, zero), pieces, unroll=8)
    gr, gi = pieces[:, 4], pieces[:, 5]
    rr = pieces[:, 6] + pieces[:, 8] * fre - pieces[:, 9] * fim
    ri = pieces[:, 7] + pieces[:, 8] * fim + pieces[:, 9] * fre

    def backward(i, state):
        position = count - 1 - i
        sr, si = state
        nsr = gr[position] * sr - gi[position] * si + rr[position]
        nsi = gr[position] * si + gi[position] * sr + ri[position]
        keep = position > mine
        return (jnp.where(keep, nsr, sr), jnp.where(keep, nsi, si))

    sre, sim = lax.fori_loop(0, count - 1, backward, (zero, zero), unroll=9)
    return (fre[mine], fim[mine]), (sre, sim)


def select(table, regime):
    result = jnp.zeros((regime.shape[0], table.shape[1]), jnp.float32)
    for which in range(table.shape[0]):
        result = jnp.where(regime[:, None] == which, table[which][None, :], result)
    return result


def body(observations, info_weight, readout, labels, rate, angle, gain, time_axes):
    bins = observations.shape[1]
    lat_dev = info_weight.shape[1] // lax.axis_size("panel")
    half = REGION_LATENT // 2
    areas_dev = lat_dev // REGION_LATENT
    pair_dev = rate.shape[1]
    partial = lax.dot_general(
        info_weight,
        observations,
        (((0,), (0,)), ((), ())),
        preferred_element_type=jnp.float32,
    )
    panels = lax.axis_size("panel")
    pieces = lax.all_to_all(
        partial.astype(jnp.bfloat16).reshape(panels, lat_dev, bins), "panel", 0, 0, tiled=True
    )
    info = jnp.sum(pieces.astype(jnp.float32), axis=0).T
    view = info.reshape(bins, areas_dev, 2, half)
    zre = view[:, :, 0].reshape(bins, pair_dev)
    zim = view[:, :, 1].reshape(bins, pair_dev)
    lam = select(rate, labels)
    ang = select(angle, labels)
    scale = select(gain, labels) * jnp.sqrt(-jnp.expm1(-2.0 * lam))
    mag = jnp.exp(-lam)
    are = mag * jnp.cos(ang)
    aim = mag * jnp.sin(ang)
    arriving = from_behind(labels[:1], time_axes, -1)
    following = jnp.concatenate([labels[1:], arriving])
    lam_next = select(rate, following)
    ang_next = select(angle, following)
    mag_next = jnp.exp(-lam_next)
    is_last = lax.axis_index(time_axes) == lax.axis_size(time_axes) - 1
    final = jnp.logical_and(is_last, lax.iota(jnp.int32, bins) == bins - 1)[:, None]
    gre = jnp.where(final, 0.0, mag_next * jnp.cos(ang_next))
    gim = jnp.where(final, 0.0, -(mag_next * jnp.sin(ang_next)))
    coef = jnp.where(final, 1.0, -jnp.expm1(-2.0 * lam_next))
    back_re, back_im, kre, kim, sum_re, sum_im, last = smoother(
        are, aim, scale, zre, zim, gre, gim, coef
    )
    summary = last[:10]
    (in_re, in_im), (out_re, out_im) = carries(summary, time_axes)
    sre = (
        back_re
        + kre * in_re[None, :] - kim * in_im[None, :]
        + sum_re * out_re[None, :] - sum_im * out_im[None, :]
    )
    sim = (
        back_im
        + kre * in_im[None, :] + kim * in_re[None, :]
        + sum_re * out_im[None, :] + sum_im * out_re[None, :]
    )
    smoothed = jnp.stack(
        [sre.reshape(bins, areas_dev, half), sim.reshape(bins, areas_dev, half)], 2
    ).reshape(bins, lat_dev).T
    smoothed_half = smoothed.astype(jnp.bfloat16)
    copies = jnp.broadcast_to(smoothed_half[None], (panels, lat_dev, bins))
    gathered = lax.all_to_all(copies, "panel", 0, 0, tiled=True)
    predicted = jnp.dot(
        readout,
        gathered.reshape(panels * lat_dev, bins),
        preferred_element_type=jnp.float32,
    )
    return (smoothed, predicted.astype(jnp.bfloat16))


def solution(mesh):
    steps = mesh.shape["tm"]
    inner = 8
    while steps % inner:
        inner //= 2
    split = Mesh(
        mesh.devices.reshape(steps // inner, inner, mesh.shape["panel"]),
        ("tg", "tl", "panel"),
    )
    tm = ("tg", "tl")
    return jax.shard_map(
        functools.partial(body, time_axes=tm),
        mesh=split,
        in_specs=(
            P("panel", tm),
            P("panel", None),
            P("panel", None),
            P(tm),
            P(None, "panel"),
            P(None, "panel"),
            P(None, "panel"),
        ),
        out_specs=(P("panel", tm), P("panel", tm)),
        check_vma=False,
    )
```

```python
import functools

import jax
import jax.numpy as jnp
from jax import lax
from jax.experimental import pallas as pl
from jax.experimental.pallas import tpu as pltpu
from jax.sharding import Mesh, PartitionSpec as P

REGION_LATENT = 128


def from_behind(shard, axis, by):
    devices = lax.axis_size(axis)
    pairs = [(i, i + by) for i in range(devices) if 0 <= i + by < devices]
    return lax.ppermute(shard, axis, pairs)


def cmul(xr, xi, yr, yi):
    return xr * yr - xi * yi, xr * yi + xi * yr


def smoother_kernel(
    ar_ref, ai_ref, sc_ref, zr_ref, zi_ref, gr_ref, gi_ref, cf_ref,
    br_ref, bi_ref, kr_ref, ki_ref, qr_ref, qi_ref, last_ref,
    lr_ref, li_ref, pr_ref, pi_ref,
):
    bins, width = ar_ref.shape
    chains = 8 if bins % 8 == 0 else 1
    steps = bins // chains

    def forward(t, carry):
        lr, li, pr, pi = carry
        row = pl.ds(t, chains, stride=steps)
        a_r = ar_ref[row, :]
        a_i = ai_ref[row, :]
        scale = sc_ref[row, :]
        nlr, nli = cmul(a_r, a_i, lr, li)
        nlr = nlr + scale * zr_ref[row, :]
        nli = nli + scale * zi_ref[row, :]
        npr, npi = cmul(a_r, a_i, pr, pi)
        lr_ref[row, :] = nlr
        li_ref[row, :] = nli
        pr_ref[row, :] = npr
        pi_ref[row, :] = npi
        return (nlr, nli, npr, npi)

    def backward(i, carry):
        br, bi, kr, ki, qr, qi = carry
        row = pl.ds(steps - 1 - i, chains, stride=steps)
        g_r = gr_ref[row, :]
        g_i = gi_ref[row, :]
        coef = cf_ref[row, :]
        nbr, nbi = cmul(g_r, g_i, br, bi)
        nbr = nbr + coef * lr_ref[row, :]
        nbi = nbi + coef * li_ref[row, :]
        nkr, nki = cmul(g_r, g_i, kr, ki)
        nkr = nkr + coef * pr_ref[row, :]
        nki = nki + coef * pi_ref[row, :]
        nqr, nqi = cmul(g_r, g_i, qr, qi)
        br_ref[row, :] = nbr
        bi_ref[row, :] = nbi
        kr_ref[row, :] = nkr
        ki_ref[row, :] = nki
        qr_ref[row, :] = nqr
        qi_ref[row, :] = nqi
        return (nbr, nbi, nkr, nki, nqr, nqi)

    zero = jnp.zeros((chains, width), jnp.float32)
    one = jnp.ones((chains, width), jnp.float32)
    ler, lei, per, pei = lax.fori_loop(0, steps, forward, (zero, zero, one, zero), unroll=8)
    cr, ci = zero[:1], zero[:1]
    qr, qi = one[:1], zero[:1]
    for block in range(chains):
        rows = pl.ds(block * steps, steps)
        if block > 0:
            pbr, pbi = pr_ref[rows, :], pi_ref[rows, :]
            fr, fi = cmul(pbr, pbi, cr, ci)
            lr_ref[rows, :] = lr_ref[rows, :] + fr
            li_ref[rows, :] = li_ref[rows, :] + fi
            pr_ref[rows, :], pi_ref[rows, :] = cmul(pbr, pbi, qr, qi)
        er, ei = per[block : block + 1], pei[block : block + 1]
        cr, ci = cmul(er, ei, cr, ci)
        cr = cr + ler[block : block + 1]
        ci = ci + lei[block : block + 1]
        qr, qi = cmul(er, ei, qr, qi)
    last_ref[...] = jnp.zeros(last_ref.shape, jnp.float32)
    for index, value in enumerate((qr, qi, cr, ci)):
        last_ref[pl.ds(index, 1), :] = value
    sbr, sbi, skr, ski, sqr, sqi = lax.fori_loop(
        0, steps, backward, (zero, zero, zero, zero, one, zero), unroll=8
    )
    dr, di = zero[:1], zero[:1]
    hr, hi = zero[:1], zero[:1]
    er, ei = one[:1], zero[:1]
    for block in reversed(range(chains)):
        rows = pl.ds(block * steps, steps)
        if block < chains - 1:
            gbr, gbi = qr_ref[rows, :], qi_ref[rows, :]
            fr, fi = cmul(gbr, gbi, dr, di)
            br_ref[rows, :] = br_ref[rows, :] + fr
            bi_ref[rows, :] = bi_ref[rows, :] + fi
            fr, fi = cmul(gbr, gbi, hr, hi)
            kr_ref[rows, :] = kr_ref[rows, :] + fr
            ki_ref[rows, :] = ki_ref[rows, :] + fi
            qr_ref[rows, :], qi_ref[rows, :] = cmul(gbr, gbi, er, ei)
        gr, gi = sqr[block : block + 1], sqi[block : block + 1]
        dr, di = cmul(gr, gi, dr, di)
        dr = dr + sbr[block : block + 1]
        di = di + sbi[block : block + 1]
        hr, hi = cmul(gr, gi, hr, hi)
        hr = hr + skr[block : block + 1]
        hi = hi + ski[block : block + 1]
        er, ei = cmul(gr, gi, er, ei)
    for index, value in enumerate((er, ei, dr, di, hr, hi)):
        last_ref[pl.ds(4 + index, 1), :] = value


def smoother(*operands):
    bins, width = operands[0].shape
    shape = jax.ShapeDtypeStruct((bins, width), jnp.float32)
    vmem = pl.BlockSpec(memory_space=pltpu.VMEM)
    return pl.pallas_call(
        smoother_kernel,
        out_shape=(shape,) * 6 + (jax.ShapeDtypeStruct((16, width), jnp.float32),),
        in_specs=[vmem] * len(operands),
        out_specs=(vmem,) * 7,
        scratch_shapes=[pltpu.VMEM((bins, width), jnp.float32)] * 4,
    )(*operands)


def gather_all(part, axes):
    count = lax.axis_size(axes)
    copies = jnp.broadcast_to(part[None], (count,) + part.shape)
    return lax.all_to_all(copies, axes, 0, 0, tiled=True)


def join(earlier, later):
    ere, eim, ebr, ebi = earlier[0], earlier[1], earlier[2], earlier[3]
    lre, lim, lbr, lbi = later[0], later[1], later[2], later[3]
    return jnp.stack(
        [
            lre * ere - lim * eim,
            lre * eim + lim * ere,
            lre * ebr - lim * ebi + lbr,
            lre * ebi + lim * ebr + lbi,
        ]
    )


def carries(summary, axes):
    pieces = gather_all(summary, axes)
    count, mine = (pieces.shape[0], lax.axis_index(axes))
    zero = jnp.zeros_like(summary[0])

    def forward(state, piece):
        mr, mi = state
        ar, ai, lr, li = piece[0], piece[1], piece[2], piece[3]
        return (ar * mr - ai * mi + lr, ar * mi + ai * mr + li), state

    _, (fre, fim) = lax.scan(forward, (zero, zero), pieces, unroll=8)
    gr, gi = pieces[:, 4], pieces[:, 5]
    rr = pieces[:, 6] + pieces[:, 8] * fre - pieces[:, 9] * fim
    ri = pieces[:, 7] + pieces[:, 8] * fim + pieces[:, 9] * fre

    def backward(i, state):
        position = count - 1 - i
        sr, si = state
        nsr = gr[position] * sr - gi[position] * si + rr[position]
        nsi = gr[position] * si + gi[position] * sr + ri[position]
        keep = position > mine
        return (jnp.where(keep, nsr, sr), jnp.where(keep, nsi, si))

    sre, sim = lax.fori_loop(0, count - 1, backward, (zero, zero), unroll=9)
    return (fre[mine], fim[mine]), (sre, sim)


def select(table, regime):
    result = jnp.zeros((regime.shape[0], table.shape[1]), jnp.float32)
    for which in range(table.shape[0]):
        result = jnp.where(regime[:, None] == which, table[which][None, :], result)
    return result


def body(observations, info_weight, readout, labels, rate, angle, gain, time_axes):
    bins = observations.shape[1]
    lat_dev = info_weight.shape[1] // lax.axis_size("panel")
    half = REGION_LATENT // 2
    areas_dev = lat_dev // REGION_LATENT
    pair_dev = rate.shape[1]
    partial = lax.dot_general(
        info_weight,
        observations,
        (((0,), (0,)), ((), ())),
        preferred_element_type=jnp.float32,
    )
    panels = lax.axis_size("panel")
    pieces = lax.all_to_all(
        partial.astype(jnp.bfloat16).reshape(panels, lat_dev, bins), "panel", 0, 0, tiled=True
    )
    info = jnp.sum(pieces.astype(jnp.float32), axis=0).T
    view = info.reshape(bins, areas_dev, 2, half)
    zre = view[:, :, 0].reshape(bins, pair_dev)
    zim = view[:, :, 1].reshape(bins, pair_dev)
    lam = select(rate, labels)
    ang = select(angle, labels)
    scale = select(gain, labels) * jnp.sqrt(-jnp.expm1(-2.0 * lam))
    mag = jnp.exp(-lam)
    are = mag * jnp.cos(ang)
    aim = mag * jnp.sin(ang)
    arriving = from_behind(labels[:1], time_axes, -1)
    following = jnp.concatenate([labels[1:], arriving])
    lam_next = select(rate, following)
    ang_next = select(angle, following)
    mag_next = jnp.exp(-lam_next)
    is_last = lax.axis_index(time_axes) == lax.axis_size(time_axes) - 1
    final = jnp.logical_and(is_last, lax.iota(jnp.int32, bins) == bins - 1)[:, None]
    gre = jnp.where(final, 0.0, mag_next * jnp.cos(ang_next))
    gim = jnp.where(final, 0.0, -(mag_next * jnp.sin(ang_next)))
    coef = jnp.where(final, 1.0, -jnp.expm1(-2.0 * lam_next))
    back_re, back_im, kre, kim, sum_re, sum_im, last = smoother(
        are, aim, scale, zre, zim, gre, gim, coef
    )
    summary = last[:10]
    (in_re, in_im), (out_re, out_im) = carries(summary, time_axes)
    sre = (
        back_re
        + kre * in_re[None, :] - kim * in_im[None, :]
        + sum_re * out_re[None, :] - sum_im * out_im[None, :]
    )
    sim = (
        back_im
        + kre * in_im[None, :] + kim * in_re[None, :]
        + sum_re * out_im[None, :] + sum_im * out_re[None, :]
    )
    smoothed = jnp.stack(
        [sre.reshape(bins, areas_dev, half), sim.reshape(bins, areas_dev, half)], 2
    ).reshape(bins, lat_dev).T
    smoothed_half = smoothed.astype(jnp.bfloat16)
    copies = jnp.broadcast_to(smoothed_half[None], (panels, lat_dev, bins))
    gathered = lax.all_to_all(copies, "panel", 0, 0, tiled=True)
    predicted = jnp.dot(
        readout,
        gathered.reshape(panels * lat_dev, bins),
        preferred_element_type=jnp.float32,
    )
    return (smoothed, predicted.astype(jnp.bfloat16))


def solution(mesh):
    steps = mesh.shape["tm"]
    inner = 8
    while steps % inner:
        inner //= 2
    split = Mesh(
        mesh.devices.reshape(steps // inner, inner, mesh.shape["panel"]),
        ("tg", "tl", "panel"),
    )
    tm = ("tg", "tl")
    return jax.shard_map(
        functools.partial(body, time_axes=tm),
        mesh=split,
        in_specs=(
            P("panel", tm),
            P("panel", None),
            P("panel", None),
            P(tm),
            P(None, "panel"),
            P(None, "panel"),
            P(None, "panel"),
        ),
        out_specs=(P("panel", tm), P("panel", tm)),
        check_vma=False,
    )
```

```python
import functools

import jax
import jax.numpy as jnp
from jax import lax
from jax.experimental import pallas as pl
from jax.experimental.pallas import tpu as pltpu
from jax.sharding import Mesh, PartitionSpec as P

REGION_LATENT = 128


def from_behind(shard, axis, by):
    devices = lax.axis_size(axis)
    pairs = [(i, i + by) for i in range(devices) if 0 <= i + by < devices]
    return lax.ppermute(shard, axis, pairs)


def smoother_kernel(
    ar_ref, ai_ref, sc_ref, zr_ref, zi_ref, gr_ref, gi_ref, cf_ref,
    br_ref, bi_ref, kr_ref, ki_ref, qr_ref, qi_ref, last_ref,
    lr_ref, li_ref, pr_ref, pi_ref,
):
    bins, width = ar_ref.shape

    def forward(t, carry):
        lr, li, pr, pi = carry
        row = pl.ds(t, 1)
        a_r = ar_ref[row, :]
        a_i = ai_ref[row, :]
        scale = sc_ref[row, :]
        nlr = a_r * lr - a_i * li + scale * zr_ref[row, :]
        nli = a_r * li + a_i * lr + scale * zi_ref[row, :]
        npr = a_r * pr - a_i * pi
        npi = a_r * pi + a_i * pr
        lr_ref[row, :] = nlr
        li_ref[row, :] = nli
        pr_ref[row, :] = npr
        pi_ref[row, :] = npi
        return (nlr, nli, npr, npi)

    def backward(i, carry):
        t = bins - 1 - i
        br, bi, kr, ki, qr, qi = carry
        row = pl.ds(t, 1)
        g_r = gr_ref[row, :]
        g_i = gi_ref[row, :]
        coef = cf_ref[row, :]
        nbr = g_r * br - g_i * bi + coef * lr_ref[row, :]
        nbi = g_r * bi + g_i * br + coef * li_ref[row, :]
        nkr = g_r * kr - g_i * ki + coef * pr_ref[row, :]
        nki = g_r * ki + g_i * kr + coef * pi_ref[row, :]
        nqr = g_r * qr - g_i * qi
        nqi = g_r * qi + g_i * qr
        br_ref[row, :] = nbr
        bi_ref[row, :] = nbi
        kr_ref[row, :] = nkr
        ki_ref[row, :] = nki
        qr_ref[row, :] = nqr
        qi_ref[row, :] = nqi
        return (nbr, nbi, nkr, nki, nqr, nqi)

    zero = jnp.zeros((1, width), jnp.float32)
    one = jnp.ones((1, width), jnp.float32)
    lr, li, pr, pi = lax.fori_loop(0, bins, forward, (zero, zero, one, zero), unroll=8)
    last_ref[...] = jnp.zeros(last_ref.shape, jnp.float32)
    last_ref[pl.ds(0, 1), :] = pr
    last_ref[pl.ds(1, 1), :] = pi
    last_ref[pl.ds(2, 1), :] = lr
    last_ref[pl.ds(3, 1), :] = li
    ends = lax.fori_loop(0, bins, backward, (zero, zero, zero, zero, one, zero), unroll=8)
    br, bi, kr, ki, qr, qi = ends
    for index, value in enumerate((qr, qi, br, bi, kr, ki)):
        last_ref[pl.ds(4 + index, 1), :] = value


def smoother(*operands):
    bins, width = operands[0].shape
    shape = jax.ShapeDtypeStruct((bins, width), jnp.float32)
    vmem = pl.BlockSpec(memory_space=pltpu.VMEM)
    return pl.pallas_call(
        smoother_kernel,
        out_shape=(shape,) * 6 + (jax.ShapeDtypeStruct((16, width), jnp.float32),),
        in_specs=[vmem] * len(operands),
        out_specs=(vmem,) * 7,
        scratch_shapes=[pltpu.VMEM((bins, width), jnp.float32)] * 4,
    )(*operands)


def gather_all(part, axes):
    count = lax.axis_size(axes)
    copies = jnp.broadcast_to(part[None], (count,) + part.shape)
    return lax.all_to_all(copies, axes, 0, 0, tiled=True)


def join(earlier, later):
    ere, eim, ebr, ebi = earlier[0], earlier[1], earlier[2], earlier[3]
    lre, lim, lbr, lbi = later[0], later[1], later[2], later[3]
    return jnp.stack(
        [
            lre * ere - lim * eim,
            lre * eim + lim * ere,
            lre * ebr - lim * ebi + lbr,
            lre * ebi + lim * ebr + lbi,
        ]
    )


def carry_kernel(mine_ref, pieces_ref, out_ref, fr_ref, fi_ref):
    rows = pieces_ref.shape[0] // fr_ref.shape[0]
    count, width = fr_ref.shape
    mine = mine_ref[0]

    def piece(position, k):
        return pieces_ref[pl.ds(position * rows + k, 1), :]

    def forward(position, state):
        mr, mi = state
        fr_ref[pl.ds(position, 1), :] = mr
        fi_ref[pl.ds(position, 1), :] = mi
        ar, ai = piece(position, 0), piece(position, 1)
        return (ar * mr - ai * mi + piece(position, 2), ar * mi + ai * mr + piece(position, 3))

    zero = jnp.zeros((1, width), jnp.float32)
    lax.fori_loop(0, count, forward, (zero, zero), unroll=8)

    def backward(i, state):
        position = count - 1 - i
        sr, si = state
        mr = fr_ref[pl.ds(position, 1), :]
        mi = fi_ref[pl.ds(position, 1), :]
        kr, ki = piece(position, 8), piece(position, 9)
        rr = piece(position, 6) + kr * mr - ki * mi
        ri = piece(position, 7) + kr * mi + ki * mr
        gr, gi = piece(position, 4), piece(position, 5)
        nsr = gr * sr - gi * si + rr
        nsi = gr * si + gi * sr + ri
        keep = position > mine
        return (jnp.where(keep, nsr, sr), jnp.where(keep, nsi, si))

    sre, sim = lax.fori_loop(0, count - 1, backward, (zero, zero), unroll=8)
    out_ref[...] = jnp.zeros(out_ref.shape, jnp.float32)
    out_ref[pl.ds(0, 1), :] = fr_ref[pl.ds(mine, 1), :]
    out_ref[pl.ds(1, 1), :] = fi_ref[pl.ds(mine, 1), :]
    out_ref[pl.ds(2, 1), :] = sre
    out_ref[pl.ds(3, 1), :] = sim


def carries(summary, axes):
    pieces = gather_all(summary, axes)
    count, rows, width = pieces.shape
    mine = lax.axis_index(axes).astype(jnp.int32).reshape(1)
    vmem = pl.BlockSpec(memory_space=pltpu.VMEM)
    result = pl.pallas_call(
        carry_kernel,
        out_shape=jax.ShapeDtypeStruct((8, width), jnp.float32),
        in_specs=[pl.BlockSpec(memory_space=pltpu.SMEM), vmem],
        out_specs=vmem,
        scratch_shapes=[pltpu.VMEM((count, width), jnp.float32)] * 2,
    )(mine, pieces.reshape(count * rows, width))
    return (result[0], result[1]), (result[2], result[3])


def select(table, regime):
    result = jnp.zeros((regime.shape[0], table.shape[1]), jnp.float32)
    for which in range(table.shape[0]):
        result = jnp.where(regime[:, None] == which, table[which][None, :], result)
    return result


def body(observations, info_weight, readout, labels, rate, angle, gain, time_axes):
    bins = observations.shape[1]
    lat_dev = info_weight.shape[1] // lax.axis_size("panel")
    half = REGION_LATENT // 2
    areas_dev = lat_dev // REGION_LATENT
    pair_dev = rate.shape[1]
    partial = lax.dot_general(
        info_weight,
        observations,
        (((0,), (0,)), ((), ())),
        preferred_element_type=jnp.float32,
    )
    panels = lax.axis_size("panel")
    pieces = lax.all_to_all(
        partial.astype(jnp.bfloat16).reshape(panels, lat_dev, bins), "panel", 0, 0, tiled=True
    )
    info = jnp.sum(pieces.astype(jnp.float32), axis=0).T
    view = info.reshape(bins, areas_dev, 2, half)
    zre = view[:, :, 0].reshape(bins, pair_dev)
    zim = view[:, :, 1].reshape(bins, pair_dev)
    lam = select(rate, labels)
    ang = select(angle, labels)
    scale = select(gain, labels) * jnp.sqrt(-jnp.expm1(-2.0 * lam))
    mag = jnp.exp(-lam)
    are = mag * jnp.cos(ang)
    aim = mag * jnp.sin(ang)
    arriving = from_behind(labels[:1], time_axes, -1)
    following = jnp.concatenate([labels[1:], arriving])
    lam_next = select(rate, following)
    ang_next = select(angle, following)
    mag_next = jnp.exp(-lam_next)
    is_last = lax.axis_index(time_axes) == lax.axis_size(time_axes) - 1
    final = jnp.logical_and(is_last, lax.iota(jnp.int32, bins) == bins - 1)[:, None]
    gre = jnp.where(final, 0.0, mag_next * jnp.cos(ang_next))
    gim = jnp.where(final, 0.0, -(mag_next * jnp.sin(ang_next)))
    coef = jnp.where(final, 1.0, -jnp.expm1(-2.0 * lam_next))
    back_re, back_im, kre, kim, sum_re, sum_im, last = smoother(
        are, aim, scale, zre, zim, gre, gim, coef
    )
    summary = last
    (in_re, in_im), (out_re, out_im) = carries(summary, time_axes)
    sre = (
        back_re
        + kre * in_re[None, :] - kim * in_im[None, :]
        + sum_re * out_re[None, :] - sum_im * out_im[None, :]
    )
    sim = (
        back_im
        + kre * in_im[None, :] + kim * in_re[None, :]
        + sum_re * out_im[None, :] + sum_im * out_re[None, :]
    )
    smoothed = jnp.stack(
        [sre.reshape(bins, areas_dev, half), sim.reshape(bins, areas_dev, half)], 2
    ).reshape(bins, lat_dev).T
    smoothed_half = smoothed.astype(jnp.bfloat16)
    copies = jnp.broadcast_to(smoothed_half[None], (panels, lat_dev, bins))
    gathered = lax.all_to_all(copies, "panel", 0, 0, tiled=True)
    predicted = jnp.dot(
        readout,
        gathered.reshape(panels * lat_dev, bins),
        preferred_element_type=jnp.float32,
    )
    return (smoothed, predicted.astype(jnp.bfloat16))


def solution(mesh):
    steps = mesh.shape["tm"]
    inner = 8
    while steps % inner:
        inner //= 2
    split = Mesh(
        mesh.devices.reshape(steps // inner, inner, mesh.shape["panel"]),
        ("tg", "tl", "panel"),
    )
    tm = ("tg", "tl")
    return jax.shard_map(
        functools.partial(body, time_axes=tm),
        mesh=split,
        in_specs=(
            P("panel", tm),
            P("panel", None),
            P("panel", None),
            P(tm),
            P(None, "panel"),
            P(None, "panel"),
            P(None, "panel"),
        ),
        out_specs=(P("panel", tm), P("panel", tm)),
        check_vma=False,
    )
```

```python
import functools

import jax
import jax.numpy as jnp
from jax import lax
from jax.experimental import pallas as pl
from jax.experimental.pallas import tpu as pltpu
from jax.sharding import Mesh, PartitionSpec as P

REGION_LATENT = 128


def from_behind(shard, axis, by):
    devices = lax.axis_size(axis)
    pairs = [(i, i + by) for i in range(devices) if 0 <= i + by < devices]
    return lax.ppermute(shard, axis, pairs)


def smoother_kernel(
    ar_ref, ai_ref, sc_ref, zr_ref, zi_ref, gr_ref, gi_ref, cf_ref,
    br_ref, bi_ref, kr_ref, ki_ref, qr_ref, qi_ref, last_ref,
    lr_ref, li_ref, pr_ref, pi_ref,
):
    bins, width = ar_ref.shape

    def forward(t, carry):
        lr, li, pr, pi = carry
        row = pl.ds(t, 1)
        a_r = ar_ref[row, :]
        a_i = ai_ref[row, :]
        scale = sc_ref[row, :]
        nlr = a_r * lr - a_i * li + scale * zr_ref[row, :]
        nli = a_r * li + a_i * lr + scale * zi_ref[row, :]
        npr = a_r * pr - a_i * pi
        npi = a_r * pi + a_i * pr
        lr_ref[row, :] = nlr
        li_ref[row, :] = nli
        pr_ref[row, :] = npr
        pi_ref[row, :] = npi
        return (nlr, nli, npr, npi)

    def backward(i, carry):
        t = bins - 1 - i
        br, bi, kr, ki, qr, qi = carry
        row = pl.ds(t, 1)
        g_r = gr_ref[row, :]
        g_i = gi_ref[row, :]
        coef = cf_ref[row, :]
        nbr = g_r * br - g_i * bi + coef * lr_ref[row, :]
        nbi = g_r * bi + g_i * br + coef * li_ref[row, :]
        nkr = g_r * kr - g_i * ki + coef * pr_ref[row, :]
        nki = g_r * ki + g_i * kr + coef * pi_ref[row, :]
        nqr = g_r * qr - g_i * qi
        nqi = g_r * qi + g_i * qr
        br_ref[row, :] = nbr
        bi_ref[row, :] = nbi
        kr_ref[row, :] = nkr
        ki_ref[row, :] = nki
        qr_ref[row, :] = nqr
        qi_ref[row, :] = nqi
        return (nbr, nbi, nkr, nki, nqr, nqi)

    zero = jnp.zeros((1, width), jnp.float32)
    one = jnp.ones((1, width), jnp.float32)
    lr, li, pr, pi = lax.fori_loop(0, bins, forward, (zero, zero, one, zero), unroll=8)
    last_ref[...] = jnp.zeros(last_ref.shape, jnp.float32)
    last_ref[pl.ds(0, 1), :] = pr
    last_ref[pl.ds(1, 1), :] = pi
    last_ref[pl.ds(2, 1), :] = lr
    last_ref[pl.ds(3, 1), :] = li
    ends = lax.fori_loop(0, bins, backward, (zero, zero, zero, zero, one, zero), unroll=8)
    br, bi, kr, ki, qr, qi = ends
    for index, value in enumerate((qr, qi, br, bi, kr, ki)):
        last_ref[pl.ds(4 + index, 1), :] = value


def smoother(*operands):
    bins, width = operands[0].shape
    shape = jax.ShapeDtypeStruct((bins, width), jnp.float32)
    vmem = pl.BlockSpec(memory_space=pltpu.VMEM)
    return pl.pallas_call(
        smoother_kernel,
        out_shape=(shape,) * 6 + (jax.ShapeDtypeStruct((16, width), jnp.float32),),
        in_specs=[vmem] * len(operands),
        out_specs=(vmem,) * 7,
        scratch_shapes=[pltpu.VMEM((bins, width), jnp.float32)] * 4,
    )(*operands)


def gather_all(part, axes):
    count = lax.axis_size(axes)
    copies = jnp.broadcast_to(part[None], (count,) + part.shape)
    return lax.all_to_all(copies, axes, 0, 0, tiled=True)


def join(earlier, later):
    ere, eim, ebr, ebi = earlier[0], earlier[1], earlier[2], earlier[3]
    lre, lim, lbr, lbi = later[0], later[1], later[2], later[3]
    return jnp.stack(
        [
            lre * ere - lim * eim,
            lre * eim + lim * ere,
            lre * ebr - lim * ebi + lbr,
            lre * ebi + lim * ebr + lbi,
        ]
    )


def carries(summary, axes):
    pieces = gather_all(summary, axes)
    count, mine = (pieces.shape[0], lax.axis_index(axes))
    zero = jnp.zeros_like(summary[0])

    def forward(state, piece):
        mr, mi = state
        ar, ai, lr, li = piece[0], piece[1], piece[2], piece[3]
        return (ar * mr - ai * mi + lr, ar * mi + ai * mr + li), state

    _, (fre, fim) = lax.scan(forward, (zero, zero), pieces, unroll=8)
    gr, gi = pieces[:, 4], pieces[:, 5]
    rr = pieces[:, 6] + pieces[:, 8] * fre - pieces[:, 9] * fim
    ri = pieces[:, 7] + pieces[:, 8] * fim + pieces[:, 9] * fre

    def backward(i, state):
        position = count - 1 - i
        sr, si = state
        nsr = gr[position] * sr - gi[position] * si + rr[position]
        nsi = gr[position] * si + gi[position] * sr + ri[position]
        keep = position > mine
        return (jnp.where(keep, nsr, sr), jnp.where(keep, nsi, si))

    sre, sim = lax.fori_loop(0, count - 1, backward, (zero, zero), unroll=9)
    return (fre[mine], fim[mine]), (sre, sim)


def two_round_gather(part, axis):
    count = lax.axis_size(axis)
    if count != 8:
        copies = jnp.broadcast_to(part[None], (count,) + part.shape)
        return lax.all_to_all(copies, axis, 0, 0, tiled=True)
    mine = lax.axis_index(axis)

    def shift(value, by):
        return lax.ppermute(value, axis, [(i, (i + by) % count) for i in range(count)])

    up1, down1, up2, down2 = shift(part, 1), shift(part, -1), shift(part, 2), shift(part, -2)
    up3, down3, down4 = shift(up2, 1), shift(down2, -1), shift(down2, -2)
    relative = jnp.stack([part, down1, down2, down3, down4, up3, up2, up1])
    doubled = jnp.concatenate([relative, relative])
    return lax.dynamic_slice_in_dim(doubled, count - mine, count, 0)


def select(table, regime):
    result = jnp.zeros((regime.shape[0], table.shape[1]), jnp.float32)
    for which in range(table.shape[0]):
        result = jnp.where(regime[:, None] == which, table[which][None, :], result)
    return result


def body(observations, info_weight, readout, labels, rate, angle, gain, time_axes):
    bins = observations.shape[1]
    lat_dev = info_weight.shape[1] // lax.axis_size("panel")
    half = REGION_LATENT // 2
    areas_dev = lat_dev // REGION_LATENT
    pair_dev = rate.shape[1]
    partial = lax.dot_general(
        info_weight,
        observations,
        (((0,), (0,)), ((), ())),
        preferred_element_type=jnp.float32,
    )
    panels = lax.axis_size("panel")
    pieces = lax.all_to_all(
        partial.astype(jnp.bfloat16).reshape(panels, lat_dev, bins), "panel", 0, 0, tiled=True
    )
    info = jnp.sum(pieces.astype(jnp.float32), axis=0).T
    view = info.reshape(bins, areas_dev, 2, half)
    zre = view[:, :, 0].reshape(bins, pair_dev)
    zim = view[:, :, 1].reshape(bins, pair_dev)
    lam = select(rate, labels)
    ang = select(angle, labels)
    scale = select(gain, labels) * jnp.sqrt(-jnp.expm1(-2.0 * lam))
    mag = jnp.exp(-lam)
    are = mag * jnp.cos(ang)
    aim = mag * jnp.sin(ang)
    arriving = from_behind(labels[:1], time_axes, -1)
    following = jnp.concatenate([labels[1:], arriving])
    lam_next = select(rate, following)
    ang_next = select(angle, following)
    mag_next = jnp.exp(-lam_next)
    is_last = lax.axis_index(time_axes) == lax.axis_size(time_axes) - 1
    final = jnp.logical_and(is_last, lax.iota(jnp.int32, bins) == bins - 1)[:, None]
    gre = jnp.where(final, 0.0, mag_next * jnp.cos(ang_next))
    gim = jnp.where(final, 0.0, -(mag_next * jnp.sin(ang_next)))
    coef = jnp.where(final, 1.0, -jnp.expm1(-2.0 * lam_next))
    back_re, back_im, kre, kim, sum_re, sum_im, last = smoother(
        are, aim, scale, zre, zim, gre, gim, coef
    )
    summary = last[:10]
    (in_re, in_im), (out_re, out_im) = carries(summary, time_axes)
    sre = (
        back_re
        + kre * in_re[None, :] - kim * in_im[None, :]
        + sum_re * out_re[None, :] - sum_im * out_im[None, :]
    )
    sim = (
        back_im
        + kre * in_im[None, :] + kim * in_re[None, :]
        + sum_re * out_im[None, :] + sum_im * out_re[None, :]
    )
    smoothed = jnp.stack(
        [sre.reshape(bins, areas_dev, half), sim.reshape(bins, areas_dev, half)], 2
    ).reshape(bins, lat_dev).T
    smoothed_half = smoothed.astype(jnp.bfloat16)
    gathered = two_round_gather(smoothed_half, "panel")
    predicted = jnp.dot(
        readout,
        gathered.reshape(panels * lat_dev, bins),
        preferred_element_type=jnp.float32,
    )
    return (smoothed, predicted.astype(jnp.bfloat16))


def solution(mesh):
    steps = mesh.shape["tm"]
    inner = 8
    while steps % inner:
        inner //= 2
    split = Mesh(
        mesh.devices.reshape(steps // inner, inner, mesh.shape["panel"]),
        ("tg", "tl", "panel"),
    )
    tm = ("tg", "tl")
    return jax.shard_map(
        functools.partial(body, time_axes=tm),
        mesh=split,
        in_specs=(
            P("panel", tm),
            P("panel", None),
            P("panel", None),
            P(tm),
            P(None, "panel"),
            P(None, "panel"),
            P(None, "panel"),
        ),
        out_specs=(P("panel", tm), P("panel", tm)),
        check_vma=False,
    )
```

```python
import functools

import jax
import jax.numpy as jnp
from jax import lax
from jax.experimental import pallas as pl
from jax.experimental.pallas import tpu as pltpu
from jax.sharding import Mesh, PartitionSpec as P

REGION_LATENT = 128


def from_behind(shard, axis, by):
    devices = lax.axis_size(axis)
    pairs = [(i, i + by) for i in range(devices) if 0 <= i + by < devices]
    return lax.ppermute(shard, axis, pairs)


def smoother_kernel(
    ar_ref, ai_ref, sc_ref, zr_ref, zi_ref, gr_ref, gi_ref, cf_ref,
    br_ref, bi_ref, kr_ref, ki_ref, qr_ref, qi_ref, last_ref,
    lr_ref, li_ref, pr_ref, pi_ref,
):
    bins, width = ar_ref.shape

    def forward(t, carry):
        lr, li, pr, pi = carry
        row = pl.ds(t, 1)
        a_r = ar_ref[row, :]
        a_i = ai_ref[row, :]
        scale = sc_ref[row, :]
        nlr = a_r * lr - a_i * li + scale * zr_ref[row, :]
        nli = a_r * li + a_i * lr + scale * zi_ref[row, :]
        npr = a_r * pr - a_i * pi
        npi = a_r * pi + a_i * pr
        lr_ref[row, :] = nlr
        li_ref[row, :] = nli
        pr_ref[row, :] = npr
        pi_ref[row, :] = npi
        return (nlr, nli, npr, npi)

    def backward(i, carry):
        t = bins - 1 - i
        br, bi, kr, ki, qr, qi = carry
        row = pl.ds(t, 1)
        g_r = gr_ref[row, :]
        g_i = gi_ref[row, :]
        coef = cf_ref[row, :]
        nbr = g_r * br - g_i * bi + coef * lr_ref[row, :]
        nbi = g_r * bi + g_i * br + coef * li_ref[row, :]
        nkr = g_r * kr - g_i * ki + coef * pr_ref[row, :]
        nki = g_r * ki + g_i * kr + coef * pi_ref[row, :]
        nqr = g_r * qr - g_i * qi
        nqi = g_r * qi + g_i * qr
        br_ref[row, :] = nbr
        bi_ref[row, :] = nbi
        kr_ref[row, :] = nkr
        ki_ref[row, :] = nki
        qr_ref[row, :] = nqr
        qi_ref[row, :] = nqi
        return (nbr, nbi, nkr, nki, nqr, nqi)

    zero = jnp.zeros((1, width), jnp.float32)
    one = jnp.ones((1, width), jnp.float32)
    lr, li, pr, pi = lax.fori_loop(0, bins, forward, (zero, zero, one, zero), unroll=8)
    last_ref[...] = jnp.zeros(last_ref.shape, jnp.float32)
    last_ref[pl.ds(0, 1), :] = pr
    last_ref[pl.ds(1, 1), :] = pi
    last_ref[pl.ds(2, 1), :] = lr
    last_ref[pl.ds(3, 1), :] = li
    ends = lax.fori_loop(0, bins, backward, (zero, zero, zero, zero, one, zero), unroll=8)
    br, bi, kr, ki, qr, qi = ends
    for index, value in enumerate((qr, qi, br, bi, kr, ki)):
        last_ref[pl.ds(4 + index, 1), :] = value


def smoother(*operands):
    bins, width = operands[0].shape
    shape = jax.ShapeDtypeStruct((bins, width), jnp.float32)
    vmem = pl.BlockSpec(memory_space=pltpu.VMEM)
    return pl.pallas_call(
        smoother_kernel,
        out_shape=(shape,) * 6 + (jax.ShapeDtypeStruct((16, width), jnp.float32),),
        in_specs=[vmem] * len(operands),
        out_specs=(vmem,) * 7,
        scratch_shapes=[pltpu.VMEM((bins, width), jnp.float32)] * 4,
    )(*operands)


def gather_all(part, axes):
    count = lax.axis_size(axes)
    copies = jnp.broadcast_to(part[None], (count,) + part.shape)
    return lax.all_to_all(copies, axes, 0, 0, tiled=True)


def join(earlier, later):
    ere, eim, ebr, ebi = earlier[0], earlier[1], earlier[2], earlier[3]
    lre, lim, lbr, lbi = later[0], later[1], later[2], later[3]
    return jnp.stack(
        [
            lre * ere - lim * eim,
            lre * eim + lim * ere,
            lre * ebr - lim * ebi + lbr,
            lre * ebi + lim * ebr + lbi,
        ]
    )


def carries(summary, axes):
    pieces = gather_all(summary, axes)
    count, mine = (pieces.shape[0], lax.axis_index(axes))
    zero = jnp.zeros_like(summary[0])

    def forward(state, piece):
        mr, mi = state
        ar, ai, lr, li = piece[0], piece[1], piece[2], piece[3]
        return (ar * mr - ai * mi + lr, ar * mi + ai * mr + li), state

    _, (fre, fim) = lax.scan(forward, (zero, zero), pieces, unroll=8)
    gr, gi = pieces[:, 4], pieces[:, 5]
    rr = pieces[:, 6] + pieces[:, 8] * fre - pieces[:, 9] * fim
    ri = pieces[:, 7] + pieces[:, 8] * fim + pieces[:, 9] * fre

    def backward(i, state):
        position = count - 1 - i
        sr, si = state
        nsr = gr[position] * sr - gi[position] * si + rr[position]
        nsi = gr[position] * si + gi[position] * sr + ri[position]
        keep = position > mine
        return (jnp.where(keep, nsr, sr), jnp.where(keep, nsi, si))

    sre, sim = lax.fori_loop(0, count - 1, backward, (zero, zero), unroll=9)
    return (fre[mine], fim[mine]), (sre, sim)


def two_round_gather(part, axis):
    count = lax.axis_size(axis)
    if count != 8:
        copies = jnp.broadcast_to(part[None], (count,) + part.shape)
        return lax.all_to_all(copies, axis, 0, 0, tiled=True), 0
    mine = lax.axis_index(axis)

    def shift(value, by):
        return lax.ppermute(value, axis, [(i, (i + by) % count) for i in range(count)])

    up1, down1, up2, down2 = shift(part, 1), shift(part, -1), shift(part, 2), shift(part, -2)
    up3, down3, down4 = shift(up2, 1), shift(down2, -1), shift(down2, -2)
    return jnp.stack([part, down1, down2, down3, down4, up3, up2, up1]), mine


def select(table, regime):
    result = jnp.zeros((regime.shape[0], table.shape[1]), jnp.float32)
    for which in range(table.shape[0]):
        result = jnp.where(regime[:, None] == which, table[which][None, :], result)
    return result


def body(observations, info_weight, readout, labels, rate, angle, gain, time_axes):
    bins = observations.shape[1]
    lat_dev = info_weight.shape[1] // lax.axis_size("panel")
    half = REGION_LATENT // 2
    areas_dev = lat_dev // REGION_LATENT
    pair_dev = rate.shape[1]
    partial = lax.dot_general(
        info_weight,
        observations,
        (((0,), (0,)), ((), ())),
        preferred_element_type=jnp.float32,
    )
    panels = lax.axis_size("panel")
    pieces = lax.all_to_all(
        partial.astype(jnp.bfloat16).reshape(panels, lat_dev, bins), "panel", 0, 0, tiled=True
    )
    info = jnp.sum(pieces.astype(jnp.float32), axis=0).T
    view = info.reshape(bins, areas_dev, 2, half)
    zre = view[:, :, 0].reshape(bins, pair_dev)
    zim = view[:, :, 1].reshape(bins, pair_dev)
    lam = select(rate, labels)
    ang = select(angle, labels)
    scale = select(gain, labels) * jnp.sqrt(-jnp.expm1(-2.0 * lam))
    mag = jnp.exp(-lam)
    are = mag * jnp.cos(ang)
    aim = mag * jnp.sin(ang)
    arriving = from_behind(labels[:1], time_axes, -1)
    following = jnp.concatenate([labels[1:], arriving])
    lam_next = select(rate, following)
    ang_next = select(angle, following)
    mag_next = jnp.exp(-lam_next)
    is_last = lax.axis_index(time_axes) == lax.axis_size(time_axes) - 1
    final = jnp.logical_and(is_last, lax.iota(jnp.int32, bins) == bins - 1)[:, None]
    gre = jnp.where(final, 0.0, mag_next * jnp.cos(ang_next))
    gim = jnp.where(final, 0.0, -(mag_next * jnp.sin(ang_next)))
    coef = jnp.where(final, 1.0, -jnp.expm1(-2.0 * lam_next))
    back_re, back_im, kre, kim, sum_re, sum_im, last = smoother(
        are, aim, scale, zre, zim, gre, gim, coef
    )
    summary = last[:10]
    (in_re, in_im), (out_re, out_im) = carries(summary, time_axes)
    sre = (
        back_re
        + kre * in_re[None, :] - kim * in_im[None, :]
        + sum_re * out_re[None, :] - sum_im * out_im[None, :]
    )
    sim = (
        back_im
        + kre * in_im[None, :] + kim * in_re[None, :]
        + sum_re * out_im[None, :] + sum_im * out_re[None, :]
    )
    smoothed = jnp.stack(
        [sre.reshape(bins, areas_dev, half), sim.reshape(bins, areas_dev, half)], 2
    ).reshape(bins, lat_dev).T
    smoothed_half = smoothed.astype(jnp.bfloat16)
    gathered, first = two_round_gather(smoothed_half, "panel")
    turned = lax.dynamic_slice_in_dim(
        jnp.concatenate([readout, readout], 1), first * lat_dev, panels * lat_dev, 1
    )
    predicted = jnp.dot(
        turned,
        gathered.reshape(panels * lat_dev, bins),
        preferred_element_type=jnp.float32,
    )
    return (smoothed, predicted.astype(jnp.bfloat16))


def solution(mesh):
    steps = mesh.shape["tm"]
    inner = 8
    while steps % inner:
        inner //= 2
    split = Mesh(
        mesh.devices.reshape(steps // inner, inner, mesh.shape["panel"]),
        ("tg", "tl", "panel"),
    )
    tm = ("tg", "tl")
    return jax.shard_map(
        functools.partial(body, time_axes=tm),
        mesh=split,
        in_specs=(
            P("panel", tm),
            P("panel", None),
            P("panel", None),
            P(tm),
            P(None, "panel"),
            P(None, "panel"),
            P(None, "panel"),
        ),
        out_specs=(P("panel", tm), P("panel", tm)),
        check_vma=False,
    )
```

```python
import functools

import jax
import jax.numpy as jnp
from jax import lax
from jax.experimental import pallas as pl
from jax.experimental.pallas import tpu as pltpu
from jax.sharding import Mesh, PartitionSpec as P

REGION_LATENT = 128


def from_behind(shard, axis, by):
    devices = lax.axis_size(axis)
    pairs = [(i, i + by) for i in range(devices) if 0 <= i + by < devices]
    return lax.ppermute(shard, axis, pairs)


def smoother_kernel(
    ar_ref, ai_ref, sc_ref, zr_ref, zi_ref, gr_ref, gi_ref, cf_ref,
    br_ref, bi_ref, kr_ref, ki_ref, qr_ref, qi_ref, last_ref,
    lr_ref, li_ref, pr_ref, pi_ref,
):
    bins, width = ar_ref.shape

    def forward(t, carry):
        lr, li, pr, pi = carry
        row = pl.ds(t, 1)
        a_r = ar_ref[row, :]
        a_i = ai_ref[row, :]
        scale = sc_ref[row, :]
        nlr = a_r * lr - a_i * li + scale * zr_ref[row, :]
        nli = a_r * li + a_i * lr + scale * zi_ref[row, :]
        npr = a_r * pr - a_i * pi
        npi = a_r * pi + a_i * pr
        lr_ref[row, :] = nlr
        li_ref[row, :] = nli
        pr_ref[row, :] = npr
        pi_ref[row, :] = npi
        return (nlr, nli, npr, npi)

    def backward(i, carry):
        t = bins - 1 - i
        br, bi, kr, ki, qr, qi = carry
        row = pl.ds(t, 1)
        g_r = gr_ref[row, :]
        g_i = gi_ref[row, :]
        coef = cf_ref[row, :]
        nbr = g_r * br - g_i * bi + coef * lr_ref[row, :]
        nbi = g_r * bi + g_i * br + coef * li_ref[row, :]
        nkr = g_r * kr - g_i * ki + coef * pr_ref[row, :]
        nki = g_r * ki + g_i * kr + coef * pi_ref[row, :]
        nqr = g_r * qr - g_i * qi
        nqi = g_r * qi + g_i * qr
        br_ref[row, :] = nbr
        bi_ref[row, :] = nbi
        kr_ref[row, :] = nkr
        ki_ref[row, :] = nki
        qr_ref[row, :] = nqr
        qi_ref[row, :] = nqi
        return (nbr, nbi, nkr, nki, nqr, nqi)

    zero = jnp.zeros((1, width), jnp.float32)
    one = jnp.ones((1, width), jnp.float32)
    lr, li, pr, pi = lax.fori_loop(0, bins, forward, (zero, zero, one, zero), unroll=8)
    last_ref[...] = jnp.zeros(last_ref.shape, jnp.float32)
    last_ref[pl.ds(0, 1), :] = pr
    last_ref[pl.ds(1, 1), :] = pi
    last_ref[pl.ds(2, 1), :] = lr
    last_ref[pl.ds(3, 1), :] = li
    ends = lax.fori_loop(0, bins, backward, (zero, zero, zero, zero, one, zero), unroll=8)
    br, bi, kr, ki, qr, qi = ends
    for index, value in enumerate((qr, qi, br, bi, kr, ki)):
        last_ref[pl.ds(4 + index, 1), :] = value


def smoother(*operands):
    bins, width = operands[0].shape
    shape = jax.ShapeDtypeStruct((bins, width), jnp.float32)
    vmem = pl.BlockSpec(memory_space=pltpu.VMEM)
    return pl.pallas_call(
        smoother_kernel,
        out_shape=(shape,) * 6 + (jax.ShapeDtypeStruct((16, width), jnp.float32),),
        in_specs=[vmem] * len(operands),
        out_specs=(vmem,) * 7,
        scratch_shapes=[pltpu.VMEM((bins, width), jnp.float32)] * 4,
    )(*operands)


def gather_all(part, axes):
    count = lax.axis_size(axes)
    copies = jnp.broadcast_to(part[None], (count,) + part.shape)
    return lax.all_to_all(copies, axes, 0, 0, tiled=True)


def join(earlier, later):
    ere, eim, ebr, ebi = earlier[0], earlier[1], earlier[2], earlier[3]
    lre, lim, lbr, lbi = later[0], later[1], later[2], later[3]
    return jnp.stack(
        [
            lre * ere - lim * eim,
            lre * eim + lim * ere,
            lre * ebr - lim * ebi + lbr,
            lre * ebi + lim * ebr + lbi,
        ]
    )


def carries(summary, axes):
    pieces = gather_all(summary, axes)
    count, mine = (pieces.shape[0], lax.axis_index(axes))
    zero = jnp.zeros_like(summary[0])

    def forward(state, piece):
        mr, mi = state
        ar, ai, lr, li = piece[0], piece[1], piece[2], piece[3]
        return (ar * mr - ai * mi + lr, ar * mi + ai * mr + li), state

    _, (fre, fim) = lax.scan(forward, (zero, zero), pieces, unroll=8)
    gr, gi = pieces[:, 4], pieces[:, 5]
    rr = pieces[:, 6] + pieces[:, 8] * fre - pieces[:, 9] * fim
    ri = pieces[:, 7] + pieces[:, 8] * fim + pieces[:, 9] * fre

    def backward(i, state):
        position = count - 1 - i
        sr, si = state
        nsr = gr[position] * sr - gi[position] * si + rr[position]
        nsi = gr[position] * si + gi[position] * sr + ri[position]
        keep = position > mine
        return (jnp.where(keep, nsr, sr), jnp.where(keep, nsi, si))

    sre, sim = lax.fori_loop(0, count - 1, backward, (zero, zero), unroll=9)
    return (fre[mine], fim[mine]), (sre, sim)


def two_round_scatter(partial, axis):
    count = lax.axis_size(axis)
    rows = partial.shape[0] // count
    if count != 8:
        pieces = lax.all_to_all(
            partial.astype(jnp.bfloat16).reshape((count, rows) + partial.shape[1:]),
            axis, 0, 0, tiled=True,
        )
        return jnp.sum(pieces.astype(jnp.float32), axis=0)
    mine = lax.axis_index(axis)

    def chunk(ahead):
        return lax.dynamic_slice_in_dim(partial, ((mine + ahead) % count) * rows, rows, 0)

    def shift(value, by):
        pairs = [(i, (i + by) % count) for i in range(count)]
        return lax.ppermute(value.astype(jnp.bfloat16), axis, pairs).astype(jnp.float32)

    near_up, near_down = shift(chunk(1), 1), shift(chunk(-1), -1)
    via_up, via_down, via_far = shift(chunk(3), 1), shift(chunk(-3), -1), shift(chunk(-4), -2)
    far_up = shift(chunk(2) + via_up, 2)
    far_down = shift(chunk(-2) + via_down + via_far, -2)
    return chunk(0) + near_up + near_down + far_up + far_down


def two_round_gather(part, axis):
    count = lax.axis_size(axis)
    if count != 8:
        copies = jnp.broadcast_to(part[None], (count,) + part.shape)
        return lax.all_to_all(copies, axis, 0, 0, tiled=True), 0
    mine = lax.axis_index(axis)

    def shift(value, by):
        return lax.ppermute(value, axis, [(i, (i + by) % count) for i in range(count)])

    up1, down1, up2, down2 = shift(part, 1), shift(part, -1), shift(part, 2), shift(part, -2)
    up3, down3, down4 = shift(up2, 1), shift(down2, -1), shift(down2, -2)
    return jnp.stack([part, down1, down2, down3, down4, up3, up2, up1]), mine


def select(table, regime):
    result = jnp.zeros((regime.shape[0], table.shape[1]), jnp.float32)
    for which in range(table.shape[0]):
        result = jnp.where(regime[:, None] == which, table[which][None, :], result)
    return result


def body(observations, info_weight, readout, labels, rate, angle, gain, time_axes):
    bins = observations.shape[1]
    lat_dev = info_weight.shape[1] // lax.axis_size("panel")
    half = REGION_LATENT // 2
    areas_dev = lat_dev // REGION_LATENT
    pair_dev = rate.shape[1]
    partial = lax.dot_general(
        info_weight,
        observations,
        (((0,), (0,)), ((), ())),
        preferred_element_type=jnp.float32,
    )
    panels = lax.axis_size("panel")
    info = two_round_scatter(partial, "panel").T
    view = info.reshape(bins, areas_dev, 2, half)
    zre = view[:, :, 0].reshape(bins, pair_dev)
    zim = view[:, :, 1].reshape(bins, pair_dev)
    lam = select(rate, labels)
    ang = select(angle, labels)
    scale = select(gain, labels) * jnp.sqrt(-jnp.expm1(-2.0 * lam))
    mag = jnp.exp(-lam)
    are = mag * jnp.cos(ang)
    aim = mag * jnp.sin(ang)
    arriving = from_behind(labels[:1], time_axes, -1)
    following = jnp.concatenate([labels[1:], arriving])
    lam_next = select(rate, following)
    ang_next = select(angle, following)
    mag_next = jnp.exp(-lam_next)
    is_last = lax.axis_index(time_axes) == lax.axis_size(time_axes) - 1
    final = jnp.logical_and(is_last, lax.iota(jnp.int32, bins) == bins - 1)[:, None]
    gre = jnp.where(final, 0.0, mag_next * jnp.cos(ang_next))
    gim = jnp.where(final, 0.0, -(mag_next * jnp.sin(ang_next)))
    coef = jnp.where(final, 1.0, -jnp.expm1(-2.0 * lam_next))
    back_re, back_im, kre, kim, sum_re, sum_im, last = smoother(
        are, aim, scale, zre, zim, gre, gim, coef
    )
    summary = last[:10]
    (in_re, in_im), (out_re, out_im) = carries(summary, time_axes)
    sre = (
        back_re
        + kre * in_re[None, :] - kim * in_im[None, :]
        + sum_re * out_re[None, :] - sum_im * out_im[None, :]
    )
    sim = (
        back_im
        + kre * in_im[None, :] + kim * in_re[None, :]
        + sum_re * out_im[None, :] + sum_im * out_re[None, :]
    )
    smoothed = jnp.stack(
        [sre.reshape(bins, areas_dev, half), sim.reshape(bins, areas_dev, half)], 2
    ).reshape(bins, lat_dev).T
    smoothed_half = smoothed.astype(jnp.bfloat16)
    gathered, first = two_round_gather(smoothed_half, "panel")
    turned = lax.dynamic_slice_in_dim(
        jnp.concatenate([readout, readout], 1), first * lat_dev, panels * lat_dev, 1
    )
    predicted = jnp.dot(
        turned,
        gathered.reshape(panels * lat_dev, bins),
        preferred_element_type=jnp.float32,
    )
    return (smoothed, predicted.astype(jnp.bfloat16))


def solution(mesh):
    steps = mesh.shape["tm"]
    inner = 8
    while steps % inner:
        inner //= 2
    split = Mesh(
        mesh.devices.reshape(steps // inner, inner, mesh.shape["panel"]),
        ("tg", "tl", "panel"),
    )
    tm = ("tg", "tl")
    return jax.shard_map(
        functools.partial(body, time_axes=tm),
        mesh=split,
        in_specs=(
            P("panel", tm),
            P("panel", None),
            P("panel", None),
            P(tm),
            P(None, "panel"),
            P(None, "panel"),
            P(None, "panel"),
        ),
        out_specs=(P("panel", tm), P("panel", tm)),
        check_vma=False,
    )
```

```python
import functools

import jax
import jax.numpy as jnp
from jax import lax
from jax.experimental import pallas as pl
from jax.experimental.pallas import tpu as pltpu
from jax.sharding import Mesh, PartitionSpec as P

REGION_LATENT = 128


def from_behind(shard, axis, by):
    devices = lax.axis_size(axis)
    pairs = [(i, i + by) for i in range(devices) if 0 <= i + by < devices]
    return lax.ppermute(shard, axis, pairs)


def smoother_kernel(
    ar_ref, ai_ref, sc_ref, zr_ref, zi_ref, gr_ref, gi_ref, cf_ref,
    br_ref, bi_ref, kr_ref, ki_ref, qr_ref, qi_ref, last_ref,
    lr_ref, li_ref, pr_ref, pi_ref,
):
    bins, width = ar_ref.shape

    def forward(t, carry):
        lr, li, pr, pi = carry
        row = pl.ds(t, 1)
        a_r = ar_ref[row, :]
        a_i = ai_ref[row, :]
        scale = sc_ref[row, :]
        nlr = a_r * lr - a_i * li + scale * zr_ref[row, :]
        nli = a_r * li + a_i * lr + scale * zi_ref[row, :]
        npr = a_r * pr - a_i * pi
        npi = a_r * pi + a_i * pr
        lr_ref[row, :] = nlr
        li_ref[row, :] = nli
        pr_ref[row, :] = npr
        pi_ref[row, :] = npi
        return (nlr, nli, npr, npi)

    def backward(i, carry):
        t = bins - 1 - i
        br, bi, kr, ki, qr, qi = carry
        row = pl.ds(t, 1)
        g_r = gr_ref[row, :]
        g_i = gi_ref[row, :]
        coef = cf_ref[row, :]
        nbr = g_r * br - g_i * bi + coef * lr_ref[row, :]
        nbi = g_r * bi + g_i * br + coef * li_ref[row, :]
        nkr = g_r * kr - g_i * ki + coef * pr_ref[row, :]
        nki = g_r * ki + g_i * kr + coef * pi_ref[row, :]
        nqr = g_r * qr - g_i * qi
        nqi = g_r * qi + g_i * qr
        br_ref[row, :] = nbr
        bi_ref[row, :] = nbi
        kr_ref[row, :] = nkr
        ki_ref[row, :] = nki
        qr_ref[row, :] = nqr
        qi_ref[row, :] = nqi
        return (nbr, nbi, nkr, nki, nqr, nqi)

    zero = jnp.zeros((1, width), jnp.float32)
    one = jnp.ones((1, width), jnp.float32)
    lr, li, pr, pi = lax.fori_loop(0, bins, forward, (zero, zero, one, zero), unroll=8)
    last_ref[...] = jnp.zeros(last_ref.shape, jnp.float32)
    last_ref[pl.ds(0, 1), :] = pr
    last_ref[pl.ds(1, 1), :] = pi
    last_ref[pl.ds(2, 1), :] = lr
    last_ref[pl.ds(3, 1), :] = li
    ends = lax.fori_loop(0, bins, backward, (zero, zero, zero, zero, one, zero), unroll=8)
    br, bi, kr, ki, qr, qi = ends
    for index, value in enumerate((qr, qi, br, bi, kr, ki)):
        last_ref[pl.ds(4 + index, 1), :] = value


def smoother(*operands):
    bins, width = operands[0].shape
    shape = jax.ShapeDtypeStruct((bins, width), jnp.float32)
    vmem = pl.BlockSpec(memory_space=pltpu.VMEM)
    return pl.pallas_call(
        smoother_kernel,
        out_shape=(shape,) * 6 + (jax.ShapeDtypeStruct((16, width), jnp.float32),),
        in_specs=[vmem] * len(operands),
        out_specs=(vmem,) * 7,
        scratch_shapes=[pltpu.VMEM((bins, width), jnp.float32)] * 4,
    )(*operands)


def gather_all(part, axes):
    outer, inner = axes
    if lax.axis_size(inner) == 2:
        other = lax.ppermute(part, inner, [(0, 1), (1, 0)])
        first = lax.axis_index(inner) == 0
        part = jnp.where(first, jnp.stack([part, other]), jnp.stack([other, part]))
    else:
        part = lax.all_to_all(
            jnp.broadcast_to(part[None], (lax.axis_size(inner),) + part.shape), inner, 0, 0, tiled=True
        )
    count = lax.axis_size(outer)
    copies = jnp.broadcast_to(part[None], (count,) + part.shape)
    gathered = lax.all_to_all(copies, outer, 0, 0, tiled=True)
    return gathered.reshape((-1,) + gathered.shape[2:])


def join(earlier, later):
    ere, eim, ebr, ebi = earlier[0], earlier[1], earlier[2], earlier[3]
    lre, lim, lbr, lbi = later[0], later[1], later[2], later[3]
    return jnp.stack(
        [
            lre * ere - lim * eim,
            lre * eim + lim * ere,
            lre * ebr - lim * ebi + lbr,
            lre * ebi + lim * ebr + lbi,
        ]
    )


def carries(summary, axes):
    pieces = gather_all(summary, axes)
    count, mine = (pieces.shape[0], lax.axis_index(axes))
    zero = jnp.zeros_like(summary[0])

    def forward(state, piece):
        mr, mi = state
        ar, ai, lr, li = piece[0], piece[1], piece[2], piece[3]
        return (ar * mr - ai * mi + lr, ar * mi + ai * mr + li), state

    _, (fre, fim) = lax.scan(forward, (zero, zero), pieces, unroll=8)
    gr, gi = pieces[:, 4], pieces[:, 5]
    rr = pieces[:, 6] + pieces[:, 8] * fre - pieces[:, 9] * fim
    ri = pieces[:, 7] + pieces[:, 8] * fim + pieces[:, 9] * fre

    def backward(i, state):
        position = count - 1 - i
        sr, si = state
        nsr = gr[position] * sr - gi[position] * si + rr[position]
        nsi = gr[position] * si + gi[position] * sr + ri[position]
        keep = position > mine
        return (jnp.where(keep, nsr, sr), jnp.where(keep, nsi, si))

    sre, sim = lax.fori_loop(0, count - 1, backward, (zero, zero), unroll=9)
    return (fre[mine], fim[mine]), (sre, sim)


def two_round_gather(part, axis):
    count = lax.axis_size(axis)
    if count != 8:
        copies = jnp.broadcast_to(part[None], (count,) + part.shape)
        return lax.all_to_all(copies, axis, 0, 0, tiled=True), 0
    mine = lax.axis_index(axis)

    def shift(value, by):
        return lax.ppermute(value, axis, [(i, (i + by) % count) for i in range(count)])

    up1, down1, up2, down2 = shift(part, 1), shift(part, -1), shift(part, 2), shift(part, -2)
    up3, down3, down4 = shift(up2, 1), shift(down2, -1), shift(down2, -2)
    return jnp.stack([part, down1, down2, down3, down4, up3, up2, up1]), mine


def select(table, regime):
    result = jnp.zeros((regime.shape[0], table.shape[1]), jnp.float32)
    for which in range(table.shape[0]):
        result = jnp.where(regime[:, None] == which, table[which][None, :], result)
    return result


def body(observations, info_weight, readout, labels, rate, angle, gain, time_axes):
    bins = observations.shape[1]
    lat_dev = info_weight.shape[1] // lax.axis_size("panel")
    half = REGION_LATENT // 2
    areas_dev = lat_dev // REGION_LATENT
    pair_dev = rate.shape[1]
    partial = lax.dot_general(
        info_weight,
        observations,
        (((0,), (0,)), ((), ())),
        preferred_element_type=jnp.float32,
    )
    panels = lax.axis_size("panel")
    pieces = lax.all_to_all(
        partial.astype(jnp.bfloat16).reshape(panels, lat_dev, bins), "panel", 0, 0, tiled=True
    )
    info = jnp.sum(pieces.astype(jnp.float32), axis=0).T
    view = info.reshape(bins, areas_dev, 2, half)
    zre = view[:, :, 0].reshape(bins, pair_dev)
    zim = view[:, :, 1].reshape(bins, pair_dev)
    lam = select(rate, labels)
    ang = select(angle, labels)
    scale = select(gain, labels) * jnp.sqrt(-jnp.expm1(-2.0 * lam))
    mag = jnp.exp(-lam)
    are = mag * jnp.cos(ang)
    aim = mag * jnp.sin(ang)
    arriving = from_behind(labels[:1], time_axes, -1)
    following = jnp.concatenate([labels[1:], arriving])
    lam_next = select(rate, following)
    ang_next = select(angle, following)
    mag_next = jnp.exp(-lam_next)
    is_last = lax.axis_index(time_axes) == lax.axis_size(time_axes) - 1
    final = jnp.logical_and(is_last, lax.iota(jnp.int32, bins) == bins - 1)[:, None]
    gre = jnp.where(final, 0.0, mag_next * jnp.cos(ang_next))
    gim = jnp.where(final, 0.0, -(mag_next * jnp.sin(ang_next)))
    coef = jnp.where(final, 1.0, -jnp.expm1(-2.0 * lam_next))
    back_re, back_im, kre, kim, sum_re, sum_im, last = smoother(
        are, aim, scale, zre, zim, gre, gim, coef
    )
    summary = last[:10]
    (in_re, in_im), (out_re, out_im) = carries(summary, time_axes)
    sre = (
        back_re
        + kre * in_re[None, :] - kim * in_im[None, :]
        + sum_re * out_re[None, :] - sum_im * out_im[None, :]
    )
    sim = (
        back_im
        + kre * in_im[None, :] + kim * in_re[None, :]
        + sum_re * out_im[None, :] + sum_im * out_re[None, :]
    )
    smoothed = jnp.stack(
        [sre.reshape(bins, areas_dev, half), sim.reshape(bins, areas_dev, half)], 2
    ).reshape(bins, lat_dev).T
    smoothed_half = smoothed.astype(jnp.bfloat16)
    gathered, first = two_round_gather(smoothed_half, "panel")
    turned = lax.dynamic_slice_in_dim(
        jnp.concatenate([readout, readout], 1), first * lat_dev, panels * lat_dev, 1
    )
    predicted = jnp.dot(
        turned,
        gathered.reshape(panels * lat_dev, bins),
        preferred_element_type=jnp.float32,
    )
    return (smoothed, predicted.astype(jnp.bfloat16))


def solution(mesh):
    steps = mesh.shape["tm"]
    inner = 2 if steps % 2 == 0 else 1
    split = Mesh(
        mesh.devices.reshape(steps // inner, inner, mesh.shape["panel"]),
        ("tg", "tl", "panel"),
    )
    tm = ("tg", "tl")
    return jax.shard_map(
        functools.partial(body, time_axes=tm),
        mesh=split,
        in_specs=(
            P("panel", tm),
            P("panel", None),
            P("panel", None),
            P(tm),
            P(None, "panel"),
            P(None, "panel"),
            P(None, "panel"),
        ),
        out_specs=(P("panel", tm), P("panel", tm)),
        check_vma=False,
    )
```

```python
import functools

import jax
import jax.numpy as jnp
from jax import lax
from jax.experimental import pallas as pl
from jax.experimental.pallas import tpu as pltpu
from jax.sharding import Mesh, PartitionSpec as P

REGION_LATENT = 128


def from_behind(shard, axis, by):
    devices = lax.axis_size(axis)
    pairs = [(i, i + by) for i in range(devices) if 0 <= i + by < devices]
    return lax.ppermute(shard, axis, pairs)


def smoother_kernel(
    ar_ref, ai_ref, sc_ref, zr_ref, zi_ref, gr_ref, gi_ref, cf_ref,
    br_ref, bi_ref, kr_ref, ki_ref, qr_ref, qi_ref, last_ref,
    lr_ref, li_ref, pr_ref, pi_ref,
):
    bins, width = ar_ref.shape

    def forward(t, carry):
        lr, li, pr, pi = carry
        row = pl.ds(t, 1)
        a_r = ar_ref[row, :]
        a_i = ai_ref[row, :]
        scale = sc_ref[row, :]
        nlr = a_r * lr - a_i * li + scale * zr_ref[row, :]
        nli = a_r * li + a_i * lr + scale * zi_ref[row, :]
        npr = a_r * pr - a_i * pi
        npi = a_r * pi + a_i * pr
        lr_ref[row, :] = nlr
        li_ref[row, :] = nli
        pr_ref[row, :] = npr
        pi_ref[row, :] = npi
        return (nlr, nli, npr, npi)

    def backward(i, carry):
        t = bins - 1 - i
        br, bi, kr, ki, qr, qi = carry
        row = pl.ds(t, 1)
        g_r = gr_ref[row, :]
        g_i = gi_ref[row, :]
        coef = cf_ref[row, :]
        nbr = g_r * br - g_i * bi + coef * lr_ref[row, :]
        nbi = g_r * bi + g_i * br + coef * li_ref[row, :]
        nkr = g_r * kr - g_i * ki + coef * pr_ref[row, :]
        nki = g_r * ki + g_i * kr + coef * pi_ref[row, :]
        nqr = g_r * qr - g_i * qi
        nqi = g_r * qi + g_i * qr
        br_ref[row, :] = nbr
        bi_ref[row, :] = nbi
        kr_ref[row, :] = nkr
        ki_ref[row, :] = nki
        qr_ref[row, :] = nqr
        qi_ref[row, :] = nqi
        return (nbr, nbi, nkr, nki, nqr, nqi)

    zero = jnp.zeros((1, width), jnp.float32)
    one = jnp.ones((1, width), jnp.float32)
    lr, li, pr, pi = lax.fori_loop(0, bins, forward, (zero, zero, one, zero), unroll=8)
    last_ref[...] = jnp.zeros(last_ref.shape, jnp.float32)
    last_ref[pl.ds(0, 1), :] = pr
    last_ref[pl.ds(1, 1), :] = pi
    last_ref[pl.ds(2, 1), :] = lr
    last_ref[pl.ds(3, 1), :] = li
    ends = lax.fori_loop(0, bins, backward, (zero, zero, zero, zero, one, zero), unroll=8)
    br, bi, kr, ki, qr, qi = ends
    for index, value in enumerate((qr, qi, br, bi, kr, ki)):
        last_ref[pl.ds(4 + index, 1), :] = value


def smoother(*operands):
    bins, width = operands[0].shape
    shape = jax.ShapeDtypeStruct((bins, width), jnp.float32)
    vmem = pl.BlockSpec(memory_space=pltpu.VMEM)
    return pl.pallas_call(
        smoother_kernel,
        out_shape=(shape,) * 6 + (jax.ShapeDtypeStruct((16, width), jnp.float32),),
        in_specs=[vmem] * len(operands),
        out_specs=(vmem,) * 7,
        scratch_shapes=[pltpu.VMEM((bins, width), jnp.float32)] * 4,
    )(*operands)


def gather_all(part, axes):
    count = lax.axis_size(axes)
    copies = jnp.broadcast_to(part[None], (count,) + part.shape)
    return lax.all_to_all(copies, axes, 0, 0, tiled=True)


def join(earlier, later):
    ere, eim, ebr, ebi = earlier[0], earlier[1], earlier[2], earlier[3]
    lre, lim, lbr, lbi = later[0], later[1], later[2], later[3]
    return jnp.stack(
        [
            lre * ere - lim * eim,
            lre * eim + lim * ere,
            lre * ebr - lim * ebi + lbr,
            lre * ebi + lim * ebr + lbi,
        ]
    )


def carries(summary, axes):
    pieces = gather_all(summary, axes)
    count, mine = (pieces.shape[0], lax.axis_index(axes))
    zero = jnp.zeros_like(summary[0])

    def forward(state, piece):
        mr, mi = state
        ar, ai, lr, li = piece[0], piece[1], piece[2], piece[3]
        return (ar * mr - ai * mi + lr, ar * mi + ai * mr + li), state

    _, (fre, fim) = lax.scan(forward, (zero, zero), pieces, unroll=8)
    gr, gi = pieces[:, 4], pieces[:, 5]
    rr = pieces[:, 6] + pieces[:, 8] * fre - pieces[:, 9] * fim
    ri = pieces[:, 7] + pieces[:, 8] * fim + pieces[:, 9] * fre

    def backward(i, state):
        position = count - 1 - i
        sr, si = state
        nsr = gr[position] * sr - gi[position] * si + rr[position]
        nsi = gr[position] * si + gi[position] * sr + ri[position]
        keep = position > mine
        return (jnp.where(keep, nsr, sr), jnp.where(keep, nsi, si))

    sre, sim = lax.fori_loop(0, count - 1, backward, (zero, zero), unroll=9)
    return (fre[mine], fim[mine]), (sre, sim)


def two_round_gather(part, axis):
    count = lax.axis_size(axis)
    if count != 8:
        copies = jnp.broadcast_to(part[None], (count,) + part.shape)
        return lax.all_to_all(copies, axis, 0, 0, tiled=True), 0
    mine = lax.axis_index(axis)

    def shift(value, by):
        return lax.ppermute(value, axis, [(i, (i + by) % count) for i in range(count)])

    up1, down1, up2, down2 = shift(part, 1), shift(part, -1), shift(part, 2), shift(part, -2)
    up3, down3, down4 = shift(up2, 1), shift(down2, -1), shift(down2, -2)
    return jnp.stack([part, down1, down2, down3, down4, up3, up2, up1]), mine


def select(table, regime):
    result = jnp.zeros((regime.shape[0], table.shape[1]), jnp.float32)
    for which in range(table.shape[0]):
        result = jnp.where(regime[:, None] == which, table[which][None, :], result)
    return result


def body(observations, info_weight, readout, labels, rate, angle, gain, time_axes):
    bins = observations.shape[1]
    lat_dev = info_weight.shape[1] // lax.axis_size("panel")
    half = REGION_LATENT // 2
    areas_dev = lat_dev // REGION_LATENT
    pair_dev = rate.shape[1]
    partial = lax.dot_general(
        info_weight,
        observations,
        (((0,), (0,)), ((), ())),
        preferred_element_type=jnp.float32,
    )
    panels = lax.axis_size("panel")
    halves = partial.astype(jnp.bfloat16).reshape(panels, lat_dev, 2, bins // 2)
    pieces = [
        lax.all_to_all(halves[:, :, side], "panel", 0, 0, tiled=True) for side in range(2)
    ]
    info = jnp.concatenate(
        [jnp.sum(piece.astype(jnp.float32), axis=0) for piece in pieces], 1
    ).T
    view = info.reshape(bins, areas_dev, 2, half)
    zre = view[:, :, 0].reshape(bins, pair_dev)
    zim = view[:, :, 1].reshape(bins, pair_dev)
    lam = select(rate, labels)
    ang = select(angle, labels)
    scale = select(gain, labels) * jnp.sqrt(-jnp.expm1(-2.0 * lam))
    mag = jnp.exp(-lam)
    are = mag * jnp.cos(ang)
    aim = mag * jnp.sin(ang)
    arriving = from_behind(labels[:1], time_axes, -1)
    following = jnp.concatenate([labels[1:], arriving])
    lam_next = select(rate, following)
    ang_next = select(angle, following)
    mag_next = jnp.exp(-lam_next)
    is_last = lax.axis_index(time_axes) == lax.axis_size(time_axes) - 1
    final = jnp.logical_and(is_last, lax.iota(jnp.int32, bins) == bins - 1)[:, None]
    gre = jnp.where(final, 0.0, mag_next * jnp.cos(ang_next))
    gim = jnp.where(final, 0.0, -(mag_next * jnp.sin(ang_next)))
    coef = jnp.where(final, 1.0, -jnp.expm1(-2.0 * lam_next))
    back_re, back_im, kre, kim, sum_re, sum_im, last = smoother(
        are, aim, scale, zre, zim, gre, gim, coef
    )
    summary = last[:10]
    (in_re, in_im), (out_re, out_im) = carries(summary, time_axes)
    sre = (
        back_re
        + kre * in_re[None, :] - kim * in_im[None, :]
        + sum_re * out_re[None, :] - sum_im * out_im[None, :]
    )
    sim = (
        back_im
        + kre * in_im[None, :] + kim * in_re[None, :]
        + sum_re * out_im[None, :] + sum_im * out_re[None, :]
    )
    smoothed = jnp.stack(
        [sre.reshape(bins, areas_dev, half), sim.reshape(bins, areas_dev, half)], 2
    ).reshape(bins, lat_dev).T
    smoothed_half = smoothed.astype(jnp.bfloat16)
    gathered, first = two_round_gather(smoothed_half, "panel")
    turned = lax.dynamic_slice_in_dim(
        jnp.concatenate([readout, readout], 1), first * lat_dev, panels * lat_dev, 1
    )
    predicted = jnp.dot(
        turned,
        gathered.reshape(panels * lat_dev, bins),
        preferred_element_type=jnp.float32,
    )
    return (smoothed, predicted.astype(jnp.bfloat16))


def solution(mesh):
    steps = mesh.shape["tm"]
    inner = 8
    while steps % inner:
        inner //= 2
    split = Mesh(
        mesh.devices.reshape(steps // inner, inner, mesh.shape["panel"]),
        ("tg", "tl", "panel"),
    )
    tm = ("tg", "tl")
    return jax.shard_map(
        functools.partial(body, time_axes=tm),
        mesh=split,
        in_specs=(
            P("panel", tm),
            P("panel", None),
            P("panel", None),
            P(tm),
            P(None, "panel"),
            P(None, "panel"),
            P(None, "panel"),
        ),
        out_specs=(P("panel", tm), P("panel", tm)),
        check_vma=False,
    )
```

```python
import functools

import jax
import jax.numpy as jnp
from jax import lax
from jax.experimental import pallas as pl
from jax.experimental.pallas import tpu as pltpu
from jax.sharding import Mesh, PartitionSpec as P

REGION_LATENT = 128


def from_behind(shard, axis, by):
    devices = lax.axis_size(axis)
    pairs = [(i, i + by) for i in range(devices) if 0 <= i + by < devices]
    return lax.ppermute(shard, axis, pairs)


def smoother_kernel(
    ar_ref, ai_ref, sc_ref, z_ref, gr_ref, gi_ref, cf_ref,
    br_ref, bi_ref, kr_ref, ki_ref, qr_ref, qi_ref, last_ref,
    lr_ref, li_ref, pr_ref, pi_ref,
):
    bins, width = ar_ref.shape

    def forward(t, carry):
        lr, li, pr, pi = carry
        row = pl.ds(t, 1)
        a_r = ar_ref[row, :]
        a_i = ai_ref[row, :]
        scale = sc_ref[row, :]
        z = z_ref[row, :]
        nlr = a_r * lr - a_i * li + scale * z[:, :width]
        nli = a_r * li + a_i * lr + scale * z[:, width:]
        npr = a_r * pr - a_i * pi
        npi = a_r * pi + a_i * pr
        lr_ref[row, :] = nlr
        li_ref[row, :] = nli
        pr_ref[row, :] = npr
        pi_ref[row, :] = npi
        return (nlr, nli, npr, npi)

    def backward(i, carry):
        t = bins - 1 - i
        br, bi, kr, ki, qr, qi = carry
        row = pl.ds(t, 1)
        g_r = gr_ref[row, :]
        g_i = gi_ref[row, :]
        coef = cf_ref[row, :]
        nbr = g_r * br - g_i * bi + coef * lr_ref[row, :]
        nbi = g_r * bi + g_i * br + coef * li_ref[row, :]
        nkr = g_r * kr - g_i * ki + coef * pr_ref[row, :]
        nki = g_r * ki + g_i * kr + coef * pi_ref[row, :]
        nqr = g_r * qr - g_i * qi
        nqi = g_r * qi + g_i * qr
        br_ref[row, :] = nbr
        bi_ref[row, :] = nbi
        kr_ref[row, :] = nkr
        ki_ref[row, :] = nki
        qr_ref[row, :] = nqr
        qi_ref[row, :] = nqi
        return (nbr, nbi, nkr, nki, nqr, nqi)

    zero = jnp.zeros((1, width), jnp.float32)
    one = jnp.ones((1, width), jnp.float32)
    lr, li, pr, pi = lax.fori_loop(0, bins, forward, (zero, zero, one, zero), unroll=8)
    last_ref[...] = jnp.zeros(last_ref.shape, jnp.float32)
    last_ref[pl.ds(0, 1), :] = pr
    last_ref[pl.ds(1, 1), :] = pi
    last_ref[pl.ds(2, 1), :] = lr
    last_ref[pl.ds(3, 1), :] = li
    ends = lax.fori_loop(0, bins, backward, (zero, zero, zero, zero, one, zero), unroll=8)
    br, bi, kr, ki, qr, qi = ends
    for index, value in enumerate((qr, qi, br, bi, kr, ki)):
        last_ref[pl.ds(4 + index, 1), :] = value


def smoother(*operands):
    bins, width = operands[0].shape
    shape = jax.ShapeDtypeStruct((bins, width), jnp.float32)
    vmem = pl.BlockSpec(memory_space=pltpu.VMEM)
    return pl.pallas_call(
        smoother_kernel,
        out_shape=(shape,) * 6 + (jax.ShapeDtypeStruct((16, width), jnp.float32),),
        in_specs=[vmem] * len(operands),
        out_specs=(vmem,) * 7,
        scratch_shapes=[pltpu.VMEM((bins, width), jnp.float32)] * 4,
    )(*operands)


def gather_all(part, axes):
    count = lax.axis_size(axes)
    copies = jnp.broadcast_to(part[None], (count,) + part.shape)
    return lax.all_to_all(copies, axes, 0, 0, tiled=True)


def join(earlier, later):
    ere, eim, ebr, ebi = earlier[0], earlier[1], earlier[2], earlier[3]
    lre, lim, lbr, lbi = later[0], later[1], later[2], later[3]
    return jnp.stack(
        [
            lre * ere - lim * eim,
            lre * eim + lim * ere,
            lre * ebr - lim * ebi + lbr,
            lre * ebi + lim * ebr + lbi,
        ]
    )


def carries(summary, axes):
    pieces = gather_all(summary, axes)
    count, mine = (pieces.shape[0], lax.axis_index(axes))
    zero = jnp.zeros_like(summary[0])

    def forward(state, piece):
        mr, mi = state
        ar, ai, lr, li = piece[0], piece[1], piece[2], piece[3]
        return (ar * mr - ai * mi + lr, ar * mi + ai * mr + li), state

    _, (fre, fim) = lax.scan(forward, (zero, zero), pieces, unroll=8)
    gr, gi = pieces[:, 4], pieces[:, 5]
    rr = pieces[:, 6] + pieces[:, 8] * fre - pieces[:, 9] * fim
    ri = pieces[:, 7] + pieces[:, 8] * fim + pieces[:, 9] * fre

    def backward(i, state):
        position = count - 1 - i
        sr, si = state
        nsr = gr[position] * sr - gi[position] * si + rr[position]
        nsi = gr[position] * si + gi[position] * sr + ri[position]
        keep = position > mine
        return (jnp.where(keep, nsr, sr), jnp.where(keep, nsi, si))

    sre, sim = lax.fori_loop(0, count - 1, backward, (zero, zero), unroll=9)
    return (fre[mine], fim[mine]), (sre, sim)


def two_round_gather(part, axis):
    count = lax.axis_size(axis)
    if count != 8:
        copies = jnp.broadcast_to(part[None], (count,) + part.shape)
        return lax.all_to_all(copies, axis, 0, 0, tiled=True), 0
    mine = lax.axis_index(axis)

    def shift(value, by):
        return lax.ppermute(value, axis, [(i, (i + by) % count) for i in range(count)])

    up1, down1, up2, down2 = shift(part, 1), shift(part, -1), shift(part, 2), shift(part, -2)
    up3, down3, down4 = shift(up2, 1), shift(down2, -1), shift(down2, -2)
    return jnp.stack([part, down1, down2, down3, down4, up3, up2, up1]), mine


def select(table, regime):
    result = jnp.zeros((regime.shape[0], table.shape[1]), jnp.float32)
    for which in range(table.shape[0]):
        result = jnp.where(regime[:, None] == which, table[which][None, :], result)
    return result


def body(observations, info_weight, readout, labels, rate, angle, gain, time_axes):
    bins = observations.shape[1]
    lat_dev = info_weight.shape[1] // lax.axis_size("panel")
    half = REGION_LATENT // 2
    areas_dev = lat_dev // REGION_LATENT
    pair_dev = rate.shape[1]
    assert areas_dev == 1
    partial = lax.dot_general(
        info_weight,
        observations,
        (((0,), (0,)), ((), ())),
        preferred_element_type=jnp.float32,
    )
    panels = lax.axis_size("panel")
    pieces = lax.all_to_all(
        partial.astype(jnp.bfloat16).reshape(panels, lat_dev, bins), "panel", 0, 0, tiled=True
    )
    info = jnp.sum(pieces.astype(jnp.float32), axis=0).T
    lam = select(rate, labels)
    ang = select(angle, labels)
    scale = select(gain, labels) * jnp.sqrt(-jnp.expm1(-2.0 * lam))
    mag = jnp.exp(-lam)
    are = mag * jnp.cos(ang)
    aim = mag * jnp.sin(ang)
    arriving = from_behind(labels[:1], time_axes, -1)
    following = jnp.concatenate([labels[1:], arriving])
    lam_next = select(rate, following)
    ang_next = select(angle, following)
    mag_next = jnp.exp(-lam_next)
    is_last = lax.axis_index(time_axes) == lax.axis_size(time_axes) - 1
    final = jnp.logical_and(is_last, lax.iota(jnp.int32, bins) == bins - 1)[:, None]
    gre = jnp.where(final, 0.0, mag_next * jnp.cos(ang_next))
    gim = jnp.where(final, 0.0, -(mag_next * jnp.sin(ang_next)))
    coef = jnp.where(final, 1.0, -jnp.expm1(-2.0 * lam_next))
    back_re, back_im, kre, kim, sum_re, sum_im, last = smoother(
        are, aim, scale, info, gre, gim, coef
    )
    summary = last[:10]
    (in_re, in_im), (out_re, out_im) = carries(summary, time_axes)
    sre = (
        back_re
        + kre * in_re[None, :] - kim * in_im[None, :]
        + sum_re * out_re[None, :] - sum_im * out_im[None, :]
    )
    sim = (
        back_im
        + kre * in_im[None, :] + kim * in_re[None, :]
        + sum_re * out_im[None, :] + sum_im * out_re[None, :]
    )
    smoothed = jnp.stack(
        [sre.reshape(bins, areas_dev, half), sim.reshape(bins, areas_dev, half)], 2
    ).reshape(bins, lat_dev).T
    smoothed_half = smoothed.astype(jnp.bfloat16)
    gathered, first = two_round_gather(smoothed_half, "panel")
    turned = lax.dynamic_slice_in_dim(
        jnp.concatenate([readout, readout], 1), first * lat_dev, panels * lat_dev, 1
    )
    predicted = jnp.dot(
        turned,
        gathered.reshape(panels * lat_dev, bins),
        preferred_element_type=jnp.float32,
    )
    return (smoothed, predicted.astype(jnp.bfloat16))


def solution(mesh):
    steps = mesh.shape["tm"]
    inner = 8
    while steps % inner:
        inner //= 2
    split = Mesh(
        mesh.devices.reshape(steps // inner, inner, mesh.shape["panel"]),
        ("tg", "tl", "panel"),
    )
    tm = ("tg", "tl")
    return jax.shard_map(
        functools.partial(body, time_axes=tm),
        mesh=split,
        in_specs=(
            P("panel", tm),
            P("panel", None),
            P("panel", None),
            P(tm),
            P(None, "panel"),
            P(None, "panel"),
            P(None, "panel"),
        ),
        out_specs=(P("panel", tm), P("panel", tm)),
        check_vma=False,
    )
```

```python
import functools

import jax
import jax.numpy as jnp
from jax import lax
from jax.experimental import pallas as pl
from jax.experimental.pallas import tpu as pltpu
from jax.sharding import Mesh, PartitionSpec as P

REGION_LATENT = 128


def from_behind(shard, axis, by):
    devices = lax.axis_size(axis)
    pairs = [(i, i + by) for i in range(devices) if 0 <= i + by < devices]
    return lax.ppermute(shard, axis, pairs)


def smoother_kernel(
    ar_ref, ai_ref, sc_ref, zr_ref, zi_ref, gr_ref, gi_ref, cf_ref,
    br_ref, bi_ref, kr_ref, ki_ref, qr_ref, qi_ref, last_ref,
    lr_ref, li_ref, pr_ref, pi_ref,
):
    bins, width = ar_ref.shape

    def forward(t, carry):
        lr, li, pr, pi = carry
        row = pl.ds(t, 1)
        a_r = ar_ref[row, :]
        a_i = ai_ref[row, :]
        scale = sc_ref[row, :]
        nlr = a_r * lr - a_i * li + scale * zr_ref[row, :]
        nli = a_r * li + a_i * lr + scale * zi_ref[row, :]
        npr = a_r * pr - a_i * pi
        npi = a_r * pi + a_i * pr
        lr_ref[row, :] = nlr
        li_ref[row, :] = nli
        pr_ref[row, :] = npr
        pi_ref[row, :] = npi
        return (nlr, nli, npr, npi)

    def backward(i, carry):
        t = bins - 1 - i
        br, bi, kr, ki, qr, qi = carry
        row = pl.ds(t, 1)
        g_r = gr_ref[row, :]
        g_i = gi_ref[row, :]
        coef = cf_ref[row, :]
        nbr = g_r * br - g_i * bi + coef * lr_ref[row, :]
        nbi = g_r * bi + g_i * br + coef * li_ref[row, :]
        nkr = g_r * kr - g_i * ki + coef * pr_ref[row, :]
        nki = g_r * ki + g_i * kr + coef * pi_ref[row, :]
        nqr = g_r * qr - g_i * qi
        nqi = g_r * qi + g_i * qr
        br_ref[row, :] = nbr
        bi_ref[row, :] = nbi
        kr_ref[row, :] = nkr
        ki_ref[row, :] = nki
        qr_ref[row, :] = nqr
        qi_ref[row, :] = nqi
        return (nbr, nbi, nkr, nki, nqr, nqi)

    zero = jnp.zeros((1, width), jnp.float32)
    one = jnp.ones((1, width), jnp.float32)
    lr, li, pr, pi = lax.fori_loop(0, bins, forward, (zero, zero, one, zero), unroll=16)
    last_ref[...] = jnp.zeros(last_ref.shape, jnp.float32)
    last_ref[pl.ds(0, 1), :] = pr
    last_ref[pl.ds(1, 1), :] = pi
    last_ref[pl.ds(2, 1), :] = lr
    last_ref[pl.ds(3, 1), :] = li
    ends = lax.fori_loop(0, bins, backward, (zero, zero, zero, zero, one, zero), unroll=16)
    br, bi, kr, ki, qr, qi = ends
    for index, value in enumerate((qr, qi, br, bi, kr, ki)):
        last_ref[pl.ds(4 + index, 1), :] = value


def smoother(*operands):
    bins, width = operands[0].shape
    shape = jax.ShapeDtypeStruct((bins, width), jnp.float32)
    vmem = pl.BlockSpec(memory_space=pltpu.VMEM)
    return pl.pallas_call(
        smoother_kernel,
        out_shape=(shape,) * 6 + (jax.ShapeDtypeStruct((16, width), jnp.float32),),
        in_specs=[vmem] * len(operands),
        out_specs=(vmem,) * 7,
        scratch_shapes=[pltpu.VMEM((bins, width), jnp.float32)] * 4,
    )(*operands)


def gather_all(part, axes):
    count = lax.axis_size(axes)
    copies = jnp.broadcast_to(part[None], (count,) + part.shape)
    return lax.all_to_all(copies, axes, 0, 0, tiled=True)


def join(earlier, later):
    ere, eim, ebr, ebi = earlier[0], earlier[1], earlier[2], earlier[3]
    lre, lim, lbr, lbi = later[0], later[1], later[2], later[3]
    return jnp.stack(
        [
            lre * ere - lim * eim,
            lre * eim + lim * ere,
            lre * ebr - lim * ebi + lbr,
            lre * ebi + lim * ebr + lbi,
        ]
    )


def carries(summary, axes):
    pieces = gather_all(summary, axes)
    count, mine = (pieces.shape[0], lax.axis_index(axes))
    zero = jnp.zeros_like(summary[0])

    def forward(state, piece):
        mr, mi = state
        ar, ai, lr, li = piece[0], piece[1], piece[2], piece[3]
        return (ar * mr - ai * mi + lr, ar * mi + ai * mr + li), state

    _, (fre, fim) = lax.scan(forward, (zero, zero), pieces, unroll=8)
    gr, gi = pieces[:, 4], pieces[:, 5]
    rr = pieces[:, 6] + pieces[:, 8] * fre - pieces[:, 9] * fim
    ri = pieces[:, 7] + pieces[:, 8] * fim + pieces[:, 9] * fre

    def backward(i, state):
        position = count - 1 - i
        sr, si = state
        nsr = gr[position] * sr - gi[position] * si + rr[position]
        nsi = gr[position] * si + gi[position] * sr + ri[position]
        keep = position > mine
        return (jnp.where(keep, nsr, sr), jnp.where(keep, nsi, si))

    sre, sim = lax.fori_loop(0, count - 1, backward, (zero, zero), unroll=9)
    return (fre[mine], fim[mine]), (sre, sim)


def two_round_gather(part, axis):
    count = lax.axis_size(axis)
    if count != 8:
        copies = jnp.broadcast_to(part[None], (count,) + part.shape)
        return lax.all_to_all(copies, axis, 0, 0, tiled=True), 0
    mine = lax.axis_index(axis)

    def shift(value, by):
        return lax.ppermute(value, axis, [(i, (i + by) % count) for i in range(count)])

    up1, down1, up2, down2 = shift(part, 1), shift(part, -1), shift(part, 2), shift(part, -2)
    up3, down3, down4 = shift(up2, 1), shift(down2, -1), shift(down2, -2)
    return jnp.stack([part, down1, down2, down3, down4, up3, up2, up1]), mine


def select(table, regime):
    result = jnp.zeros((regime.shape[0], table.shape[1]), jnp.float32)
    for which in range(table.shape[0]):
        result = jnp.where(regime[:, None] == which, table[which][None, :], result)
    return result


def body(observations, info_weight, readout, labels, rate, angle, gain, time_axes):
    bins = observations.shape[1]
    lat_dev = info_weight.shape[1] // lax.axis_size("panel")
    half = REGION_LATENT // 2
    areas_dev = lat_dev // REGION_LATENT
    pair_dev = rate.shape[1]
    partial = lax.dot_general(
        info_weight,
        observations,
        (((0,), (0,)), ((), ())),
        preferred_element_type=jnp.float32,
    )
    panels = lax.axis_size("panel")
    pieces = lax.all_to_all(
        partial.astype(jnp.bfloat16).reshape(panels, lat_dev, bins), "panel", 0, 0, tiled=True
    )
    info = jnp.sum(pieces.astype(jnp.float32), axis=0).T
    view = info.reshape(bins, areas_dev, 2, half)
    zre = view[:, :, 0].reshape(bins, pair_dev)
    zim = view[:, :, 1].reshape(bins, pair_dev)
    lam = select(rate, labels)
    ang = select(angle, labels)
    scale = select(gain, labels) * jnp.sqrt(-jnp.expm1(-2.0 * lam))
    mag = jnp.exp(-lam)
    are = mag * jnp.cos(ang)
    aim = mag * jnp.sin(ang)
    arriving = from_behind(labels[:1], time_axes, -1)
    following = jnp.concatenate([labels[1:], arriving])
    lam_next = select(rate, following)
    ang_next = select(angle, following)
    mag_next = jnp.exp(-lam_next)
    is_last = lax.axis_index(time_axes) == lax.axis_size(time_axes) - 1
    final = jnp.logical_and(is_last, lax.iota(jnp.int32, bins) == bins - 1)[:, None]
    gre = jnp.where(final, 0.0, mag_next * jnp.cos(ang_next))
    gim = jnp.where(final, 0.0, -(mag_next * jnp.sin(ang_next)))
    coef = jnp.where(final, 1.0, -jnp.expm1(-2.0 * lam_next))
    back_re, back_im, kre, kim, sum_re, sum_im, last = smoother(
        are, aim, scale, zre, zim, gre, gim, coef
    )
    summary = last[:10]
    (in_re, in_im), (out_re, out_im) = carries(summary, time_axes)
    sre = (
        back_re
        + kre * in_re[None, :] - kim * in_im[None, :]
        + sum_re * out_re[None, :] - sum_im * out_im[None, :]
    )
    sim = (
        back_im
        + kre * in_im[None, :] + kim * in_re[None, :]
        + sum_re * out_im[None, :] + sum_im * out_re[None, :]
    )
    smoothed = jnp.stack(
        [sre.reshape(bins, areas_dev, half), sim.reshape(bins, areas_dev, half)], 2
    ).reshape(bins, lat_dev).T
    smoothed_half = smoothed.astype(jnp.bfloat16)
    gathered, first = two_round_gather(smoothed_half, "panel")
    turned = lax.dynamic_slice_in_dim(
        jnp.concatenate([readout, readout], 1), first * lat_dev, panels * lat_dev, 1
    )
    predicted = jnp.dot(
        turned,
        gathered.reshape(panels * lat_dev, bins),
        preferred_element_type=jnp.float32,
    )
    return (smoothed, predicted.astype(jnp.bfloat16))


def solution(mesh):
    steps = mesh.shape["tm"]
    inner = 8
    while steps % inner:
        inner //= 2
    split = Mesh(
        mesh.devices.reshape(steps // inner, inner, mesh.shape["panel"]),
        ("tg", "tl", "panel"),
    )
    tm = ("tg", "tl")
    return jax.shard_map(
        functools.partial(body, time_axes=tm),
        mesh=split,
        in_specs=(
            P("panel", tm),
            P("panel", None),
            P("panel", None),
            P(tm),
            P(None, "panel"),
            P(None, "panel"),
            P(None, "panel"),
        ),
        out_specs=(P("panel", tm), P("panel", tm)),
        check_vma=False,
    )
```

```python
import functools

import jax
import jax.numpy as jnp
from jax import lax
from jax.experimental import pallas as pl
from jax.experimental.pallas import tpu as pltpu
from jax.sharding import Mesh, PartitionSpec as P

REGION_LATENT = 128


def from_behind(shard, axis, by):
    devices = lax.axis_size(axis)
    pairs = [(i, i + by) for i in range(devices) if 0 <= i + by < devices]
    return lax.ppermute(shard, axis, pairs)


def smoother_kernel(
    ar_ref, ai_ref, sc_ref, zr_ref, zi_ref, gr_ref, gi_ref, cf_ref,
    br_ref, bi_ref, kr_ref, ki_ref, qr_ref, qi_ref, last_ref,
    lr_ref, li_ref, pr_ref, pi_ref,
):
    bins, width = ar_ref.shape

    def forward(t, carry):
        lr, li, pr, pi = carry
        row = pl.ds(t, 1)
        a_r = ar_ref[row, :]
        a_i = ai_ref[row, :]
        scale = sc_ref[row, :]
        nlr = a_r * lr - a_i * li + scale * zr_ref[row, :]
        nli = a_r * li + a_i * lr + scale * zi_ref[row, :]
        npr = a_r * pr - a_i * pi
        npi = a_r * pi + a_i * pr
        lr_ref[row, :] = nlr
        li_ref[row, :] = nli
        pr_ref[row, :] = npr
        pi_ref[row, :] = npi
        return (nlr, nli, npr, npi)

    def backward(i, carry):
        t = bins - 1 - i
        br, bi, kr, ki, qr, qi = carry
        row = pl.ds(t, 1)
        g_r = gr_ref[row, :]
        g_i = gi_ref[row, :]
        coef = cf_ref[row, :]
        nbr = g_r * br - g_i * bi + coef * lr_ref[row, :]
        nbi = g_r * bi + g_i * br + coef * li_ref[row, :]
        nkr = g_r * kr - g_i * ki + coef * pr_ref[row, :]
        nki = g_r * ki + g_i * kr + coef * pi_ref[row, :]
        nqr = g_r * qr - g_i * qi
        nqi = g_r * qi + g_i * qr
        br_ref[row, :] = nbr
        bi_ref[row, :] = nbi
        kr_ref[row, :] = nkr
        ki_ref[row, :] = nki
        qr_ref[row, :] = nqr
        qi_ref[row, :] = nqi
        return (nbr, nbi, nkr, nki, nqr, nqi)

    zero = jnp.zeros((1, width), jnp.float32)
    one = jnp.ones((1, width), jnp.float32)
    lr, li, pr, pi = lax.fori_loop(0, bins, forward, (zero, zero, one, zero), unroll=32)
    last_ref[...] = jnp.zeros(last_ref.shape, jnp.float32)
    last_ref[pl.ds(0, 1), :] = pr
    last_ref[pl.ds(1, 1), :] = pi
    last_ref[pl.ds(2, 1), :] = lr
    last_ref[pl.ds(3, 1), :] = li
    ends = lax.fori_loop(0, bins, backward, (zero, zero, zero, zero, one, zero), unroll=32)
    br, bi, kr, ki, qr, qi = ends
    for index, value in enumerate((qr, qi, br, bi, kr, ki)):
        last_ref[pl.ds(4 + index, 1), :] = value


def smoother(*operands):
    bins, width = operands[0].shape
    shape = jax.ShapeDtypeStruct((bins, width), jnp.float32)
    vmem = pl.BlockSpec(memory_space=pltpu.VMEM)
    return pl.pallas_call(
        smoother_kernel,
        out_shape=(shape,) * 6 + (jax.ShapeDtypeStruct((16, width), jnp.float32),),
        in_specs=[vmem] * len(operands),
        out_specs=(vmem,) * 7,
        scratch_shapes=[pltpu.VMEM((bins, width), jnp.float32)] * 4,
    )(*operands)


def gather_all(part, axes):
    count = lax.axis_size(axes)
    copies = jnp.broadcast_to(part[None], (count,) + part.shape)
    return lax.all_to_all(copies, axes, 0, 0, tiled=True)


def join(earlier, later):
    ere, eim, ebr, ebi = earlier[0], earlier[1], earlier[2], earlier[3]
    lre, lim, lbr, lbi = later[0], later[1], later[2], later[3]
    return jnp.stack(
        [
            lre * ere - lim * eim,
            lre * eim + lim * ere,
            lre * ebr - lim * ebi + lbr,
            lre * ebi + lim * ebr + lbi,
        ]
    )


def carries(summary, axes):
    pieces = gather_all(summary, axes)
    count, mine = (pieces.shape[0], lax.axis_index(axes))
    zero = jnp.zeros_like(summary[0])

    def forward(state, piece):
        mr, mi = state
        ar, ai, lr, li = piece[0], piece[1], piece[2], piece[3]
        return (ar * mr - ai * mi + lr, ar * mi + ai * mr + li), state

    _, (fre, fim) = lax.scan(forward, (zero, zero), pieces, unroll=8)
    gr, gi = pieces[:, 4], pieces[:, 5]
    rr = pieces[:, 6] + pieces[:, 8] * fre - pieces[:, 9] * fim
    ri = pieces[:, 7] + pieces[:, 8] * fim + pieces[:, 9] * fre

    def backward(i, state):
        position = count - 1 - i
        sr, si = state
        nsr = gr[position] * sr - gi[position] * si + rr[position]
        nsi = gr[position] * si + gi[position] * sr + ri[position]
        keep = position > mine
        return (jnp.where(keep, nsr, sr), jnp.where(keep, nsi, si))

    sre, sim = lax.fori_loop(0, count - 1, backward, (zero, zero), unroll=9)
    return (fre[mine], fim[mine]), (sre, sim)


def two_round_gather(part, axis):
    count = lax.axis_size(axis)
    if count != 8:
        copies = jnp.broadcast_to(part[None], (count,) + part.shape)
        return lax.all_to_all(copies, axis, 0, 0, tiled=True), 0
    mine = lax.axis_index(axis)

    def shift(value, by):
        return lax.ppermute(value, axis, [(i, (i + by) % count) for i in range(count)])

    up1, down1, up2, down2 = shift(part, 1), shift(part, -1), shift(part, 2), shift(part, -2)
    up3, down3, down4 = shift(up2, 1), shift(down2, -1), shift(down2, -2)
    return jnp.stack([part, down1, down2, down3, down4, up3, up2, up1]), mine


def select(table, regime):
    result = jnp.zeros((regime.shape[0], table.shape[1]), jnp.float32)
    for which in range(table.shape[0]):
        result = jnp.where(regime[:, None] == which, table[which][None, :], result)
    return result


def body(observations, info_weight, readout, labels, rate, angle, gain, time_axes):
    bins = observations.shape[1]
    lat_dev = info_weight.shape[1] // lax.axis_size("panel")
    half = REGION_LATENT // 2
    areas_dev = lat_dev // REGION_LATENT
    pair_dev = rate.shape[1]
    partial = lax.dot_general(
        info_weight,
        observations,
        (((0,), (0,)), ((), ())),
        preferred_element_type=jnp.float32,
    )
    panels = lax.axis_size("panel")
    pieces = lax.all_to_all(
        partial.astype(jnp.bfloat16).reshape(panels, lat_dev, bins), "panel", 0, 0, tiled=True
    )
    info = jnp.sum(pieces.astype(jnp.float32), axis=0).T
    view = info.reshape(bins, areas_dev, 2, half)
    zre = view[:, :, 0].reshape(bins, pair_dev)
    zim = view[:, :, 1].reshape(bins, pair_dev)
    lam = select(rate, labels)
    ang = select(angle, labels)
    scale = select(gain, labels) * jnp.sqrt(-jnp.expm1(-2.0 * lam))
    mag = jnp.exp(-lam)
    are = mag * jnp.cos(ang)
    aim = mag * jnp.sin(ang)
    arriving = from_behind(labels[:1], time_axes, -1)
    following = jnp.concatenate([labels[1:], arriving])
    lam_next = select(rate, following)
    ang_next = select(angle, following)
    mag_next = jnp.exp(-lam_next)
    is_last = lax.axis_index(time_axes) == lax.axis_size(time_axes) - 1
    final = jnp.logical_and(is_last, lax.iota(jnp.int32, bins) == bins - 1)[:, None]
    gre = jnp.where(final, 0.0, mag_next * jnp.cos(ang_next))
    gim = jnp.where(final, 0.0, -(mag_next * jnp.sin(ang_next)))
    coef = jnp.where(final, 1.0, -jnp.expm1(-2.0 * lam_next))
    back_re, back_im, kre, kim, sum_re, sum_im, last = smoother(
        are, aim, scale, zre, zim, gre, gim, coef
    )
    summary = last[:10]
    (in_re, in_im), (out_re, out_im) = carries(summary, time_axes)
    sre = (
        back_re
        + kre * in_re[None, :] - kim * in_im[None, :]
        + sum_re * out_re[None, :] - sum_im * out_im[None, :]
    )
    sim = (
        back_im
        + kre * in_im[None, :] + kim * in_re[None, :]
        + sum_re * out_im[None, :] + sum_im * out_re[None, :]
    )
    smoothed = jnp.stack(
        [sre.reshape(bins, areas_dev, half), sim.reshape(bins, areas_dev, half)], 2
    ).reshape(bins, lat_dev).T
    smoothed_half = smoothed.astype(jnp.bfloat16)
    gathered, first = two_round_gather(smoothed_half, "panel")
    turned = lax.dynamic_slice_in_dim(
        jnp.concatenate([readout, readout], 1), first * lat_dev, panels * lat_dev, 1
    )
    predicted = jnp.dot(
        turned,
        gathered.reshape(panels * lat_dev, bins),
        preferred_element_type=jnp.float32,
    )
    return (smoothed, predicted.astype(jnp.bfloat16))


def solution(mesh):
    steps = mesh.shape["tm"]
    inner = 8
    while steps % inner:
        inner //= 2
    split = Mesh(
        mesh.devices.reshape(steps // inner, inner, mesh.shape["panel"]),
        ("tg", "tl", "panel"),
    )
    tm = ("tg", "tl")
    return jax.shard_map(
        functools.partial(body, time_axes=tm),
        mesh=split,
        in_specs=(
            P("panel", tm),
            P("panel", None),
            P("panel", None),
            P(tm),
            P(None, "panel"),
            P(None, "panel"),
            P(None, "panel"),
        ),
        out_specs=(P("panel", tm), P("panel", tm)),
        check_vma=False,
    )
```

```python
import functools

import jax
import jax.numpy as jnp
from jax import lax
from jax.experimental import pallas as pl
from jax.experimental.pallas import tpu as pltpu
from jax.sharding import Mesh, PartitionSpec as P

REGION_LATENT = 128


def from_behind(shard, axis, by):
    devices = lax.axis_size(axis)
    pairs = [(i, i + by) for i in range(devices) if 0 <= i + by < devices]
    return lax.ppermute(shard, axis, pairs)


def smoother_kernel(
    ar_ref, ai_ref, sc_ref, zr_ref, zi_ref, gr_ref, gi_ref, cf_ref,
    br_ref, bi_ref, kr_ref, ki_ref, qr_ref, qi_ref, last_ref,
    lr_ref, li_ref, pr_ref, pi_ref,
):
    bins, width = ar_ref.shape

    def forward(t, carry):
        lr, li, pr, pi = carry
        row = pl.ds(t, 1)
        a_r = ar_ref[row, :]
        a_i = ai_ref[row, :]
        scale = sc_ref[row, :]
        nlr = a_r * lr - a_i * li + scale * zr_ref[row, :]
        nli = a_r * li + a_i * lr + scale * zi_ref[row, :]
        npr = a_r * pr - a_i * pi
        npi = a_r * pi + a_i * pr
        lr_ref[row, :] = nlr
        li_ref[row, :] = nli
        pr_ref[row, :] = npr
        pi_ref[row, :] = npi
        return (nlr, nli, npr, npi)

    def backward(i, carry):
        t = bins - 1 - i
        br, bi, kr, ki, qr, qi = carry
        row = pl.ds(t, 1)
        g_r = gr_ref[row, :]
        g_i = gi_ref[row, :]
        coef = cf_ref[row, :]
        nbr = g_r * br - g_i * bi + coef * lr_ref[row, :]
        nbi = g_r * bi + g_i * br + coef * li_ref[row, :]
        nkr = g_r * kr - g_i * ki + coef * pr_ref[row, :]
        nki = g_r * ki + g_i * kr + coef * pi_ref[row, :]
        nqr = g_r * qr - g_i * qi
        nqi = g_r * qi + g_i * qr
        br_ref[row, :] = nbr
        bi_ref[row, :] = nbi
        kr_ref[row, :] = nkr
        ki_ref[row, :] = nki
        qr_ref[row, :] = nqr
        qi_ref[row, :] = nqi
        return (nbr, nbi, nkr, nki, nqr, nqi)

    zero = jnp.zeros((1, width), jnp.float32)
    one = jnp.ones((1, width), jnp.float32)
    lr, li, pr, pi = lax.fori_loop(0, bins, forward, (zero, zero, one, zero), unroll=16)
    last_ref[...] = jnp.zeros(last_ref.shape, jnp.float32)
    last_ref[pl.ds(0, 1), :] = pr
    last_ref[pl.ds(1, 1), :] = pi
    last_ref[pl.ds(2, 1), :] = lr
    last_ref[pl.ds(3, 1), :] = li
    ends = lax.fori_loop(0, bins, backward, (zero, zero, zero, zero, one, zero), unroll=16)
    br, bi, kr, ki, qr, qi = ends
    for index, value in enumerate((qr, qi, br, bi, kr, ki)):
        last_ref[pl.ds(4 + index, 1), :] = value


def smoother(*operands):
    bins, width = operands[0].shape
    shape = jax.ShapeDtypeStruct((bins, width), jnp.float32)
    vmem = pl.BlockSpec(memory_space=pltpu.VMEM)
    return pl.pallas_call(
        smoother_kernel,
        out_shape=(shape,) * 6 + (jax.ShapeDtypeStruct((16, width), jnp.float32),),
        in_specs=[vmem] * len(operands),
        out_specs=(vmem,) * 7,
        scratch_shapes=[pltpu.VMEM((bins, width), jnp.float32)] * 4,
    )(*operands)


def gather_all(part, axes):
    count = lax.axis_size(axes)
    copies = jnp.broadcast_to(part[None], (count,) + part.shape)
    return lax.all_to_all(copies, axes, 0, 0, tiled=True)


def join(earlier, later):
    ere, eim, ebr, ebi = earlier[0], earlier[1], earlier[2], earlier[3]
    lre, lim, lbr, lbi = later[0], later[1], later[2], later[3]
    return jnp.stack(
        [
            lre * ere - lim * eim,
            lre * eim + lim * ere,
            lre * ebr - lim * ebi + lbr,
            lre * ebi + lim * ebr + lbi,
        ]
    )


def carries(summary, axes):
    pieces = gather_all(summary, axes)
    count, mine = (pieces.shape[0], lax.axis_index(axes))
    zero = jnp.zeros_like(summary[0])

    def forward(state, piece):
        mr, mi = state
        ar, ai, lr, li = piece[0], piece[1], piece[2], piece[3]
        return (ar * mr - ai * mi + lr, ar * mi + ai * mr + li), state

    _, (fre, fim) = lax.scan(forward, (zero, zero), pieces, unroll=True)
    gr, gi = pieces[:, 4], pieces[:, 5]
    rr = pieces[:, 6] + pieces[:, 8] * fre - pieces[:, 9] * fim
    ri = pieces[:, 7] + pieces[:, 8] * fim + pieces[:, 9] * fre

    def backward(i, state):
        position = count - 1 - i
        sr, si = state
        nsr = gr[position] * sr - gi[position] * si + rr[position]
        nsi = gr[position] * si + gi[position] * sr + ri[position]
        keep = position > mine
        return (jnp.where(keep, nsr, sr), jnp.where(keep, nsi, si))

    sre, sim = lax.fori_loop(0, count - 1, backward, (zero, zero), unroll=True)
    return (fre[mine], fim[mine]), (sre, sim)


def two_round_gather(part, axis):
    count = lax.axis_size(axis)
    if count != 8:
        copies = jnp.broadcast_to(part[None], (count,) + part.shape)
        return lax.all_to_all(copies, axis, 0, 0, tiled=True), 0
    mine = lax.axis_index(axis)

    def shift(value, by):
        return lax.ppermute(value, axis, [(i, (i + by) % count) for i in range(count)])

    up1, down1, up2, down2 = shift(part, 1), shift(part, -1), shift(part, 2), shift(part, -2)
    up3, down3, down4 = shift(up2, 1), shift(down2, -1), shift(down2, -2)
    return jnp.stack([part, down1, down2, down3, down4, up3, up2, up1]), mine


def select(table, regime):
    result = jnp.zeros((regime.shape[0], table.shape[1]), jnp.float32)
    for which in range(table.shape[0]):
        result = jnp.where(regime[:, None] == which, table[which][None, :], result)
    return result


def body(observations, info_weight, readout, labels, rate, angle, gain, time_axes):
    bins = observations.shape[1]
    lat_dev = info_weight.shape[1] // lax.axis_size("panel")
    half = REGION_LATENT // 2
    areas_dev = lat_dev // REGION_LATENT
    pair_dev = rate.shape[1]
    partial = lax.dot_general(
        info_weight,
        observations,
        (((0,), (0,)), ((), ())),
        preferred_element_type=jnp.float32,
    )
    panels = lax.axis_size("panel")
    pieces = lax.all_to_all(
        partial.astype(jnp.bfloat16).reshape(panels, lat_dev, bins), "panel", 0, 0, tiled=True
    )
    info = jnp.sum(pieces.astype(jnp.float32), axis=0).T
    view = info.reshape(bins, areas_dev, 2, half)
    zre = view[:, :, 0].reshape(bins, pair_dev)
    zim = view[:, :, 1].reshape(bins, pair_dev)
    lam = select(rate, labels)
    ang = select(angle, labels)
    scale = select(gain, labels) * jnp.sqrt(-jnp.expm1(-2.0 * lam))
    mag = jnp.exp(-lam)
    are = mag * jnp.cos(ang)
    aim = mag * jnp.sin(ang)
    arriving = from_behind(labels[:1], time_axes, -1)
    following = jnp.concatenate([labels[1:], arriving])
    lam_next = select(rate, following)
    ang_next = select(angle, following)
    mag_next = jnp.exp(-lam_next)
    is_last = lax.axis_index(time_axes) == lax.axis_size(time_axes) - 1
    final = jnp.logical_and(is_last, lax.iota(jnp.int32, bins) == bins - 1)[:, None]
    gre = jnp.where(final, 0.0, mag_next * jnp.cos(ang_next))
    gim = jnp.where(final, 0.0, -(mag_next * jnp.sin(ang_next)))
    coef = jnp.where(final, 1.0, -jnp.expm1(-2.0 * lam_next))
    back_re, back_im, kre, kim, sum_re, sum_im, last = smoother(
        are, aim, scale, zre, zim, gre, gim, coef
    )
    summary = last[:10]
    (in_re, in_im), (out_re, out_im) = carries(summary, time_axes)
    sre = (
        back_re
        + kre * in_re[None, :] - kim * in_im[None, :]
        + sum_re * out_re[None, :] - sum_im * out_im[None, :]
    )
    sim = (
        back_im
        + kre * in_im[None, :] + kim * in_re[None, :]
        + sum_re * out_im[None, :] + sum_im * out_re[None, :]
    )
    smoothed = jnp.stack(
        [sre.reshape(bins, areas_dev, half), sim.reshape(bins, areas_dev, half)], 2
    ).reshape(bins, lat_dev).T
    smoothed_half = smoothed.astype(jnp.bfloat16)
    gathered, first = two_round_gather(smoothed_half, "panel")
    turned = lax.dynamic_slice_in_dim(
        jnp.concatenate([readout, readout], 1), first * lat_dev, panels * lat_dev, 1
    )
    predicted = jnp.dot(
        turned,
        gathered.reshape(panels * lat_dev, bins),
        preferred_element_type=jnp.float32,
    )
    return (smoothed, predicted.astype(jnp.bfloat16))


def solution(mesh):
    steps = mesh.shape["tm"]
    inner = 8
    while steps % inner:
        inner //= 2
    split = Mesh(
        mesh.devices.reshape(steps // inner, inner, mesh.shape["panel"]),
        ("tg", "tl", "panel"),
    )
    tm = ("tg", "tl")
    return jax.shard_map(
        functools.partial(body, time_axes=tm),
        mesh=split,
        in_specs=(
            P("panel", tm),
            P("panel", None),
            P("panel", None),
            P(tm),
            P(None, "panel"),
            P(None, "panel"),
            P(None, "panel"),
        ),
        out_specs=(P("panel", tm), P("panel", tm)),
        check_vma=False,
    )
```

```python
import functools

import jax
import jax.numpy as jnp
from jax import lax
from jax.experimental import pallas as pl
from jax.experimental.pallas import tpu as pltpu
from jax.sharding import Mesh, PartitionSpec as P

REGION_LATENT = 128


def from_behind(shard, axis, by):
    devices = lax.axis_size(axis)
    pairs = [(i, i + by) for i in range(devices) if 0 <= i + by < devices]
    return lax.ppermute(shard, axis, pairs)


def smoother_kernel(
    ar_ref, ai_ref, sc_ref, zr_ref, zi_ref, gr_ref, gi_ref, cf_ref,
    br_ref, bi_ref, kr_ref, ki_ref, qr_ref, qi_ref, last_ref,
    lr_ref, li_ref, pr_ref, pi_ref,
):
    bins, width = ar_ref.shape

    def forward(t, carry):
        lr, li, pr, pi = carry
        row = pl.ds(t, 1)
        a_r = ar_ref[row, :]
        a_i = ai_ref[row, :]
        scale = sc_ref[row, :]
        nlr = a_r * lr - a_i * li + scale * zr_ref[row, :]
        nli = a_r * li + a_i * lr + scale * zi_ref[row, :]
        npr = a_r * pr - a_i * pi
        npi = a_r * pi + a_i * pr
        lr_ref[row, :] = nlr
        li_ref[row, :] = nli
        pr_ref[row, :] = npr
        pi_ref[row, :] = npi
        return (nlr, nli, npr, npi)

    def backward(i, carry):
        t = bins - 1 - i
        br, bi, kr, ki, qr, qi = carry
        row = pl.ds(t, 1)
        g_r = gr_ref[row, :]
        g_i = gi_ref[row, :]
        coef = cf_ref[row, :]
        nbr = g_r * br - g_i * bi + coef * lr_ref[row, :]
        nbi = g_r * bi + g_i * br + coef * li_ref[row, :]
        nkr = g_r * kr - g_i * ki + coef * pr_ref[row, :]
        nki = g_r * ki + g_i * kr + coef * pi_ref[row, :]
        nqr = g_r * qr - g_i * qi
        nqi = g_r * qi + g_i * qr
        br_ref[row, :] = nbr
        bi_ref[row, :] = nbi
        kr_ref[row, :] = nkr
        ki_ref[row, :] = nki
        qr_ref[row, :] = nqr
        qi_ref[row, :] = nqi
        return (nbr, nbi, nkr, nki, nqr, nqi)

    zero = jnp.zeros((1, width), jnp.float32)
    one = jnp.ones((1, width), jnp.float32)
    lr, li, pr, pi = lax.fori_loop(0, bins, forward, (zero, zero, one, zero), unroll=16)
    last_ref[...] = jnp.zeros(last_ref.shape, jnp.float32)
    last_ref[pl.ds(0, 1), :] = pr
    last_ref[pl.ds(1, 1), :] = pi
    last_ref[pl.ds(2, 1), :] = lr
    last_ref[pl.ds(3, 1), :] = li
    ends = lax.fori_loop(0, bins, backward, (zero, zero, zero, zero, one, zero), unroll=16)
    br, bi, kr, ki, qr, qi = ends
    for index, value in enumerate((qr, qi, br, bi, kr, ki)):
        last_ref[pl.ds(4 + index, 1), :] = value


def smoother(*operands):
    bins, width = operands[0].shape
    shape = jax.ShapeDtypeStruct((bins, width), jnp.float32)
    vmem = pl.BlockSpec(memory_space=pltpu.VMEM)
    return pl.pallas_call(
        smoother_kernel,
        out_shape=(shape,) * 6 + (jax.ShapeDtypeStruct((16, width), jnp.float32),),
        in_specs=[vmem] * len(operands),
        out_specs=(vmem,) * 7,
        scratch_shapes=[pltpu.VMEM((bins, width), jnp.float32)] * 4,
    )(*operands)


def gather_all(part, axes):
    count = lax.axis_size(axes)
    copies = jnp.broadcast_to(part[None], (count,) + part.shape)
    return lax.all_to_all(copies, axes, 0, 0, tiled=True)


def join(earlier, later):
    ere, eim, ebr, ebi = earlier[0], earlier[1], earlier[2], earlier[3]
    lre, lim, lbr, lbi = later[0], later[1], later[2], later[3]
    return jnp.stack(
        [
            lre * ere - lim * eim,
            lre * eim + lim * ere,
            lre * ebr - lim * ebi + lbr,
            lre * ebi + lim * ebr + lbi,
        ]
    )


def carries(summary, axes):
    pieces = gather_all(summary, axes)
    count, mine = (pieces.shape[0], lax.axis_index(axes))
    zero = jnp.zeros_like(summary[0])

    def forward(state, piece):
        mr, mi = state
        ar, ai, lr, li = piece[0], piece[1], piece[2], piece[3]
        return (ar * mr - ai * mi + lr, ar * mi + ai * mr + li), state

    _, (fre, fim) = lax.scan(forward, (zero, zero), pieces, unroll=16)
    gr, gi = pieces[:, 4], pieces[:, 5]
    rr = pieces[:, 6] + pieces[:, 8] * fre - pieces[:, 9] * fim
    ri = pieces[:, 7] + pieces[:, 8] * fim + pieces[:, 9] * fre

    def backward(i, state):
        position = count - 1 - i
        sr, si = state
        nsr = gr[position] * sr - gi[position] * si + rr[position]
        nsi = gr[position] * si + gi[position] * sr + ri[position]
        keep = position > mine
        return (jnp.where(keep, nsr, sr), jnp.where(keep, nsi, si))

    sre, sim = lax.fori_loop(0, count - 1, backward, (zero, zero), unroll=21)
    return (fre[mine], fim[mine]), (sre, sim)


def two_round_gather(part, axis):
    count = lax.axis_size(axis)
    if count != 8:
        copies = jnp.broadcast_to(part[None], (count,) + part.shape)
        return lax.all_to_all(copies, axis, 0, 0, tiled=True), 0
    mine = lax.axis_index(axis)

    def shift(value, by):
        return lax.ppermute(value, axis, [(i, (i + by) % count) for i in range(count)])

    up1, down1, up2, down2 = shift(part, 1), shift(part, -1), shift(part, 2), shift(part, -2)
    up3, down3, down4 = shift(up2, 1), shift(down2, -1), shift(down2, -2)
    return jnp.stack([part, down1, down2, down3, down4, up3, up2, up1]), mine


def select(table, regime):
    result = jnp.zeros((regime.shape[0], table.shape[1]), jnp.float32)
    for which in range(table.shape[0]):
        result = jnp.where(regime[:, None] == which, table[which][None, :], result)
    return result


def body(observations, info_weight, readout, labels, rate, angle, gain, time_axes):
    bins = observations.shape[1]
    lat_dev = info_weight.shape[1] // lax.axis_size("panel")
    half = REGION_LATENT // 2
    areas_dev = lat_dev // REGION_LATENT
    pair_dev = rate.shape[1]
    partial = lax.dot_general(
        info_weight,
        observations,
        (((0,), (0,)), ((), ())),
        preferred_element_type=jnp.float32,
    )
    panels = lax.axis_size("panel")
    pieces = lax.all_to_all(
        partial.astype(jnp.bfloat16).reshape(panels, lat_dev, bins), "panel", 0, 0, tiled=True
    )
    info = jnp.sum(pieces.astype(jnp.float32), axis=0).T
    view = info.reshape(bins, areas_dev, 2, half)
    zre = view[:, :, 0].reshape(bins, pair_dev)
    zim = view[:, :, 1].reshape(bins, pair_dev)
    lam = select(rate, labels)
    ang = select(angle, labels)
    scale = select(gain, labels) * jnp.sqrt(-jnp.expm1(-2.0 * lam))
    mag = jnp.exp(-lam)
    are = mag * jnp.cos(ang)
    aim = mag * jnp.sin(ang)
    arriving = from_behind(labels[:1], time_axes, -1)
    following = jnp.concatenate([labels[1:], arriving])
    lam_next = select(rate, following)
    ang_next = select(angle, following)
    mag_next = jnp.exp(-lam_next)
    is_last = lax.axis_index(time_axes) == lax.axis_size(time_axes) - 1
    final = jnp.logical_and(is_last, lax.iota(jnp.int32, bins) == bins - 1)[:, None]
    gre = jnp.where(final, 0.0, mag_next * jnp.cos(ang_next))
    gim = jnp.where(final, 0.0, -(mag_next * jnp.sin(ang_next)))
    coef = jnp.where(final, 1.0, -jnp.expm1(-2.0 * lam_next))
    back_re, back_im, kre, kim, sum_re, sum_im, last = smoother(
        are, aim, scale, zre, zim, gre, gim, coef
    )
    summary = last[:10]
    (in_re, in_im), (out_re, out_im) = carries(summary, time_axes)
    sre = (
        back_re
        + kre * in_re[None, :] - kim * in_im[None, :]
        + sum_re * out_re[None, :] - sum_im * out_im[None, :]
    )
    sim = (
        back_im
        + kre * in_im[None, :] + kim * in_re[None, :]
        + sum_re * out_im[None, :] + sum_im * out_re[None, :]
    )
    smoothed = jnp.stack(
        [sre.reshape(bins, areas_dev, half), sim.reshape(bins, areas_dev, half)], 2
    ).reshape(bins, lat_dev).T
    smoothed_half = smoothed.astype(jnp.bfloat16)
    gathered, first = two_round_gather(smoothed_half, "panel")
    turned = lax.dynamic_slice_in_dim(
        jnp.concatenate([readout, readout], 1), first * lat_dev, panels * lat_dev, 1
    )
    predicted = jnp.dot(
        turned,
        gathered.reshape(panels * lat_dev, bins),
        preferred_element_type=jnp.float32,
    )
    return (smoothed, predicted.astype(jnp.bfloat16))


def solution(mesh):
    steps = mesh.shape["tm"]
    inner = 8
    while steps % inner:
        inner //= 2
    split = Mesh(
        mesh.devices.reshape(steps // inner, inner, mesh.shape["panel"]),
        ("tg", "tl", "panel"),
    )
    tm = ("tg", "tl")
    return jax.shard_map(
        functools.partial(body, time_axes=tm),
        mesh=split,
        in_specs=(
            P("panel", tm),
            P("panel", None),
            P("panel", None),
            P(tm),
            P(None, "panel"),
            P(None, "panel"),
            P(None, "panel"),
        ),
        out_specs=(P("panel", tm), P("panel", tm)),
        check_vma=False,
    )
```
